32 devices in a mesh: dp: 4 (over z), seq: 8 (over y, x, core).
Axes of the slice: x: 2, y: 2, z: 4, core: 2. Of those that a mesh axis runs over, the one named last changes fastest.
Arguments:
- tokens: bfloat16 [4, 1024, 2048], P('dp', 'seq'), may hold values from -6 to 6
- query_weight: bfloat16 [2048, 256], replicated, may hold values from -0.125 to 0.125
- key_weight: bfloat16 [2048, 256], replicated, may hold values from -0.125 to 0.125
- value_weight: bfloat16 [2048, 2048], replicated, may hold values from -0.125 to 0.125
- cotangent: bfloat16 [4, 1024, 2048], P('dp', 'seq'), may hold values from -6 to 6
- doc_ids: int32 [4, 1024], P('dp', 'seq'), may hold values from 0 to 3, never falling along the last dimension, each value on 1 to 512 neighbouring positions
Outputs:
- mixed: bfloat16 [4, 1024, 2048], P('dp', 'seq')
- grad_tokens: bfloat16 [4, 1024, 2048], P('dp', 'seq')
- grad_weights: float32 [2048, 2560], P(('dp', 'seq'))
The draws below stay inside these ranges and needn't reach their ends.
Inputs may be any that keep to these rules, and one draw needn't show every extreme that they name: `doc_ids`: document numbers never fall along a pack and begin at 0; each document has at most 512 positions and one has exactly that many.
All inputs are finite; a program needn't handle non-finite values.
Results may differ from the reference program's by a relative error of at most 0.0049.
Values sent between devices are 32-bit elements; how exact they have to be, the bound alone decides.
No kernel may reach another device: no remote copies, remote signals or barrier semaphores. Data moves between devices by JAX's collectives and lax.ppermute only.
A program may use at most 256 MiB of HBM per device.

```python
import math
import jax
import jax.numpy as jnp
import numpy as np
from jax import lax

D = 2048
HEADS = 16
FEAT = 16
HEAD_DIM = 128
TAYLOR = 153
TOK_DEV = 128
DOCS = 4
SEQLEN = 1024
PACKS = 4


def block_levels(key, shape, pieces, smallest, largest):
    factor_of, own = 1.0, jax.random.fold_in(key, 6)
    for position, blocks in pieces:
        draws = jnp.exp(jax.random.uniform(jax.random.fold_in(own, position), (blocks,), jnp.float32, smallest / len(pieces), largest / len(pieces)))
        factor_of = factor_of * jnp.repeat(draws, shape[position] // blocks).reshape([-1 if axis == position else 1 for axis in range(len(shape))])
    return factor_of


def split_up(number_of, total, reach, slope):
    weights = [(1 << 20) // math.isqrt(standing ** slope) + 1 for standing in range(2, number_of + 1)]
    surplus, given = total - reach - (number_of - 1), [1] * (number_of - 1)
    while surplus > 0:
        movable = [i for i in range(number_of - 1) if given[i] < reach]
        mass, left = sum([weights[i] for i in movable]), surplus
        for i in movable:
            extra = min(reach - given[i], max(1, left * weights[i] // mass), surplus)
            given[i] = given[i] + extra
            surplus = surplus - extra
    return np.array([reach] + given)


def ragged(rng, count, total, most, slope):
    if count == 2:
        one = jax.random.randint(rng, (), max(1, total - most), min(most, total - 1) + 1)
        return jnp.stack([one, total - one])
    tallies = jnp.asarray(split_up(count, total, most, slope), jnp.int32)
    twos = (count - 1) // 2
    giver, receiver = tallies[1:1 + 2 * twos:2], tallies[2:2 + 2 * twos:2]
    margin = jnp.minimum(giver - 1, most - receiver)
    moved = jax.random.randint(jax.random.fold_in(rng, 1), (twos,), 0, 1 << 20) % (margin + 1)
    tallies = tallies.at[1:1 + 2 * twos:2].set(giver - moved).at[2:2 + 2 * twos:2].set(receiver + moved)
    return tallies[jax.random.permutation(jax.random.fold_in(rng, 2), count)]


def normal_values(key, dims, spread, reach, pieces=(), kind=jnp.bfloat16):
    factor_of = block_levels(key, dims, pieces, -0.22, 0.18) if pieces else 1.0
    drawn = jax.random.normal(key, dims, jnp.float32) * spread * factor_of
    return jnp.minimum(jnp.maximum(drawn, -reach), reach).astype(kind)


def setup_inputs(seed: int = 0) -> dict:
    keys = jax.random.split(jax.random.key(seed), 7)
    return {
        "tokens": normal_values(keys[0], (PACKS, SEQLEN, D), 1.0, 6.0, ((0, 4), (1, 8))),
        "query_weight": normal_values(keys[1], (D, HEADS * FEAT), D ** -0.5, 0.125),
        "key_weight": normal_values(keys[2], (D, HEADS * FEAT), D ** -0.5, 0.125),
        "value_weight": normal_values(keys[3], (D, D), D ** -0.5, 0.125),
        "cotangent": normal_values(keys[4], (PACKS, SEQLEN, D), 1.0, 6.0, ((0, 4), (1, 8))),
        "doc_ids": jax.vmap(lambda own: jnp.searchsorted(jnp.cumsum(ragged(own, DOCS, SEQLEN, SEQLEN // 2, 1)), jnp.arange(SEQLEN), side="right"))(jax.random.split(keys[5], PACKS)).reshape((PACKS, SEQLEN)).astype(jnp.int32),
    }


highest = lax.Precision.HIGHEST

def taylor_table(feat_width):
    row_index, col_index = np.triu_indices(feat_width)
    taylor_map = np.zeros((feat_width * feat_width, len(row_index)), np.float32)
    taylor_map[row_index * feat_width + col_index, np.arange(len(row_index))] = np.where(row_index == col_index, 1.0 / np.sqrt(2.0), 1.0)
    return jnp.asarray(taylor_map)

def expand_features(vectors, taylor_map):
    lead_shape = vectors.shape[:-1]
    feat_width = vectors.shape[-1]
    outer_prod = (vectors[..., :, None] * vectors[..., None, :]).reshape(lead_shape + (feat_width * feat_width,))
    square = jnp.einsum('thp,pc->thc', outer_prod, taylor_map.astype(vectors.dtype), precision=highest)
    return jnp.concatenate([jnp.ones(lead_shape + (1,), vectors.dtype), vectors, square], axis=-1)

def block_forward(query_raw, key_raw, value_all, doc_local, prev_id, state_in, norm_in, taylor_map):
    length = query_raw.shape[0]
    queries = (0.5 * query_raw).reshape(length, HEADS, FEAT)
    key_feats = (0.5 * key_raw).reshape(length, HEADS, FEAT)
    values = value_all.reshape(length, HEADS, HEAD_DIM)
    scores = jnp.einsum('thf,shf->hts', queries, key_feats, precision=highest)
    kernel = 1.0 + scores + 0.5 * scores * scores
    positions = jnp.arange(length)
    allowed = (positions[:, None] >= positions[None, :]) & (doc_local[:, None] == doc_local[None, :])
    kernel = jnp.where(allowed[None], kernel, 0.0)
    numerator = jnp.einsum('hts,shd->thd', kernel, values, precision=highest)
    denominator = lax.optimization_barrier(jnp.sum(kernel, axis=2)).T
    carried = (doc_local == prev_id).astype(kernel.dtype)[:, None]
    phi_query = expand_features(queries, taylor_map)
    numerator = numerator + carried[:, :, None] * jnp.einsum('thf,hfd->thd', phi_query, state_in, precision=highest)
    denominator = denominator + carried * jnp.einsum('thf,hf->th', phi_query, norm_in, precision=highest)
    return (numerator / denominator[:, :, None]).reshape(length, HEADS * HEAD_DIM)

def block_summary(key_raw, value_all, doc_local, taylor_map):
    length = key_raw.shape[0]
    key_feats = (0.5 * key_raw).reshape(length, HEADS, FEAT)
    values = value_all.reshape(length, HEADS, HEAD_DIM)
    phi_key = expand_features(key_feats, taylor_map)
    tail_mask = (doc_local == doc_local[-1]).astype(phi_key.dtype)[:, None, None]
    weighted = phi_key * tail_mask
    state_sum = jnp.einsum('thf,thd->hfd', weighted, values, precision=highest)
    norm_sum = lax.optimization_barrier(jnp.sum(weighted, axis=0))
    return (state_sum, norm_sum)

def pack_forward(projected, pack_ids, taylor_map):
    width_qk = HEADS * FEAT
    blocks = SEQLEN // TOK_DEV
    query_raw = projected[:, :width_qk].reshape(blocks, TOK_DEV, width_qk)
    key_raw = projected[:, width_qk:2 * width_qk].reshape(blocks, TOK_DEV, width_qk)
    value_all = projected[:, 2 * width_qk:].reshape(blocks, TOK_DEV, D)
    block_ids = pack_ids.reshape(blocks, TOK_DEV)

    def block_step(carried_state, inputs):
        state_sum, norm_sum, prev_id = carried_state
        query_blk, key_blk, value_blk, ids_blk = inputs
        block_out = block_forward(query_blk, key_blk, value_blk, ids_blk, prev_id, state_sum, norm_sum, taylor_map)
        state_loc, norm_loc = block_summary(key_blk, value_blk, ids_blk, taylor_map)
        boundary = ids_blk[-1] != prev_id
        state_next = jnp.where(boundary, state_loc, state_sum + state_loc)
        norm_next = jnp.where(boundary, norm_loc, norm_sum + norm_loc)
        return ((state_next, norm_next, ids_blk[-1]), block_out)
    init_state = (jnp.zeros((HEADS, TAYLOR, HEAD_DIM), projected.dtype), jnp.zeros((HEADS, TAYLOR), projected.dtype), jnp.zeros((), jnp.int32))
    final_state, outputs = lax.scan(block_step, init_state, (query_raw, key_raw, value_all, block_ids))
    return outputs.reshape(SEQLEN, D)

def reference(tokens, query_weight, key_weight, value_weight, cotangent, doc_ids):
    taylor_map = taylor_table(FEAT)
    weights = jnp.concatenate([query_weight, key_weight, value_weight], axis=1)

    def one_pack(pack_args):
        pack_tokens, pack_cotan, pack_ids = pack_args
        projected = jnp.dot(pack_tokens, weights, preferred_element_type=jnp.float32)

        def attend(proj_in):
            return pack_forward(proj_in, pack_ids, taylor_map)
        output, pullback = jax.vjp(attend, projected)
        grad_float, = pullback(pack_cotan.astype(jnp.float32))
        grad_projected = grad_float.astype(jnp.bfloat16)
        grad_input = jnp.dot(grad_projected, weights.T, preferred_element_type=jnp.float32).astype(jnp.bfloat16)
        grad_proj = jnp.dot(pack_tokens.T, grad_projected, preferred_element_type=jnp.float32)
        return (output.astype(jnp.bfloat16), grad_input, grad_proj)
    mixed, grad_tokens, grad_packs = lax.map(one_pack, (tokens, cotangent, doc_ids))
    return (mixed, grad_tokens, lax.optimization_barrier(jnp.sum(grad_packs, axis=0)))
```

```python
import jax
import jax.numpy as jnp
import numpy as np
from jax import lax
from jax.sharding import PartitionSpec as P

HEADS = 16
FEAT = 16
HEAD_DIM = 128


highest = lax.Precision.HIGHEST


def from_behind(value, axis, steps):
    count = lax.axis_size(axis)
    first, last = (max(0, -steps), min(count, count - steps))
    return lax.ppermute(value, axis, [(source, source + steps) for source in range(first, last)])


def entering(value, axis, join, neutral, backward):
    count, mine = (lax.axis_size(axis), lax.axis_index(axis))
    pieces = jax.tree.map(lambda part: lax.all_gather(part, axis), value)
    if backward:
        pieces = jax.tree.map(lambda part: part[::-1], pieces)
        mine = count - 1 - mine
    so_far = jax.tree.map(
        lambda part, zero: jnp.full_like(part, 0) + jnp.asarray(zero, part.dtype), value, neutral
    )

    def turn(position, so_far):
        longer = join(so_far, jax.tree.map(lambda part: part[position], pieces))
        return jax.tree.map(lambda new, old: jnp.where(position < mine, new, old), longer, so_far)

    return lax.fori_loop(0, count - 1, turn, so_far)


def taylor_table(feat_width):
    row_index, col_index = np.triu_indices(feat_width)
    taylor_map = np.zeros((feat_width * feat_width, len(row_index)), np.float32)
    taylor_map[row_index * feat_width + col_index, np.arange(len(row_index))] = np.where(
        row_index == col_index, 1.0 / np.sqrt(2.0), 1.0
    )
    return jnp.asarray(taylor_map)


def expand_features(vectors, taylor_map):
    lead_shape = vectors.shape[:-1]
    feat_width = vectors.shape[-1]
    outer_prod = (vectors[..., :, None] * vectors[..., None, :]).reshape(
        lead_shape + (feat_width * feat_width,)
    )
    square = jnp.einsum(
        "thp,pc->thc", outer_prod, taylor_map.astype(vectors.dtype), precision=highest
    )
    return jnp.concatenate([jnp.ones(lead_shape + (1,), vectors.dtype), vectors, square], axis=-1)


def block_forward(query_raw, key_raw, value_all, doc_local, prev_id, state_in, norm_in, taylor_map):
    length = query_raw.shape[0]
    queries = (0.5 * query_raw).reshape(length, HEADS, FEAT)
    key_feats = (0.5 * key_raw).reshape(length, HEADS, FEAT)
    values = value_all.reshape(length, HEADS, HEAD_DIM)
    scores = jnp.einsum("thf,shf->hts", queries, key_feats, precision=highest)
    kernel = 1.0 + scores + 0.5 * scores * scores
    positions = jnp.arange(length)
    allowed = (positions[:, None] >= positions[None, :]) & (
        doc_local[:, None] == doc_local[None, :]
    )
    kernel = jnp.where(allowed[None], kernel, 0.0)
    numerator = jnp.einsum("hts,shd->thd", kernel, values, precision=highest)
    denominator = jnp.sum(kernel, axis=2).T
    carried = (doc_local == prev_id).astype(kernel.dtype)[:, None]
    phi_query = expand_features(queries, taylor_map)
    numerator = numerator + carried[:, :, None] * jnp.einsum(
        "thf,hfd->thd", phi_query, state_in, precision=highest
    )
    denominator = denominator + carried * jnp.einsum(
        "thf,hf->th", phi_query, norm_in, precision=highest
    )
    return (numerator / denominator[:, :, None]).reshape(length, HEADS * HEAD_DIM)


def block_summary(key_raw, value_all, doc_local, taylor_map):
    length = key_raw.shape[0]
    key_feats = (0.5 * key_raw).reshape(length, HEADS, FEAT)
    values = value_all.reshape(length, HEADS, HEAD_DIM)
    phi_key = expand_features(key_feats, taylor_map)
    tail_mask = (doc_local == doc_local[-1]).astype(phi_key.dtype)[:, None, None]
    weighted = phi_key * tail_mask
    state_sum = jnp.einsum("thf,thd->hfd", weighted, values, precision=highest)
    norm_sum = jnp.sum(weighted, axis=0)
    return (state_sum, norm_sum)


def forward_combine(earlier, later):
    state_sum = jnp.where(later[2] > 0, later[0], earlier[0] + later[0])
    norm_sum = jnp.where(later[2] > 0, later[1], earlier[1] + later[1])
    return (state_sum, norm_sum, jnp.maximum(earlier[2], later[2]))


def adjoint_combine(earlier, later):
    state_sum = later[0] + jnp.where(later[2] > 0, 0.0, earlier[0])
    norm_sum = later[1] + jnp.where(later[2] > 0, 0.0, earlier[1])
    return (state_sum, norm_sum, jnp.maximum(earlier[2], later[2]))


def on_device(tokens, query_weight, key_weight, value_weight, cotangent, doc_ids):
    inputs = tokens[0]
    doc_local = doc_ids[0]
    cotan_local = cotangent[0]
    taylor_map = taylor_table(FEAT)
    width_qk = HEADS * FEAT
    weights = jnp.concatenate([query_weight, key_weight, value_weight], axis=1)
    projected = jnp.dot(inputs, weights, preferred_element_type=jnp.float32)
    shifted_id = from_behind(doc_local[-1:] + 1, "seq", 1)[0]
    prev_id = shifted_id - 1
    boundary = (doc_local[-1] != prev_id).astype(jnp.float32)

    def summary(proj_in):
        return block_summary(
            proj_in[:, width_qk : 2 * width_qk], proj_in[:, 2 * width_qk :], doc_local, taylor_map
        )

    (state_loc, norm_loc), summary_pull = jax.vjp(summary, projected)
    zero_state = jnp.zeros_like(state_loc)
    zero_norm = jnp.zeros_like(norm_loc)
    zero_flag = jnp.zeros((), jnp.float32)
    state_in, norm_in, flag_in = entering(
        (state_loc, norm_loc, boundary),
        "seq",
        forward_combine,
        (zero_state, zero_norm, zero_flag),
        False,
    )

    def attend(proj_in, state_sum, norm_sum):
        return block_forward(
            proj_in[:, :width_qk],
            proj_in[:, width_qk : 2 * width_qk],
            proj_in[:, 2 * width_qk :],
            doc_local,
            prev_id,
            state_sum,
            norm_sum,
            taylor_map,
        )

    output, attend_pull = jax.vjp(attend, projected, state_in, norm_in)
    grad_direct, grad_state_in, grad_norm_in = attend_pull(cotan_local.astype(jnp.float32))
    grad_state_loc, grad_norm_loc, flag_out = entering(
        (grad_state_in, grad_norm_in, boundary),
        "seq",
        adjoint_combine,
        (zero_state, zero_norm, zero_flag),
        True,
    )
    (grad_carried,) = summary_pull((grad_state_loc, grad_norm_loc))
    grad_projected = (grad_direct + grad_carried).astype(jnp.bfloat16)
    grad_input = jnp.dot(grad_projected, weights.T, preferred_element_type=jnp.float32).astype(
        jnp.bfloat16
    )
    seq_count = lax.axis_size("seq")
    width = weights.shape[1]
    tokens_pack = lax.all_gather(inputs.astype(jnp.float32), "seq", axis=0, tiled=True)
    grad_cols = lax.all_to_all(
        grad_projected.astype(jnp.float32), "seq", split_axis=1, concat_axis=0, tiled=True
    )
    pack_part = lax.dot_general(
        tokens_pack,
        grad_cols,
        (((0,), (0,)), ((), ())),
        precision=highest,
        preferred_element_type=jnp.float32,
    )
    row_part = lax.psum_scatter(pack_part, "dp", scatter_dimension=0, tiled=True)
    grad_proj = lax.all_to_all(row_part, "seq", split_axis=0, concat_axis=1, tiled=True)
    del seq_count, width
    return (output.astype(jnp.bfloat16)[None], grad_input[None], grad_proj)


def solution(mesh):
    return jax.shard_map(
        on_device,
        mesh=mesh,
        in_specs=(P("dp", "seq", None), P(), P(), P(), P("dp", "seq", None), P("dp", "seq")),
        out_specs=(P("dp", "seq", None), P("dp", "seq", None), P(("dp", "seq"), None)),
        check_vma=False,
    )
```

```python
import jax
import jax.numpy as jnp
import numpy as np
from jax import lax
from jax.sharding import PartitionSpec as P

HEADS = 16
FEAT = 16
HEAD_DIM = 128


highest = lax.Precision.HIGHEST


def pack_rows(parts):
    flat = jnp.concatenate([part.reshape(-1) for part in parts])
    size = flat.shape[0]
    padded = -(-size // 1024) * 1024
    flat = jnp.pad(flat, (0, padded - size))
    return flat.reshape(padded // 128, 128)


def unpack_rows(packed, shapes):
    flat = packed.reshape(-1)
    out, offset = [], 0
    for shape in shapes:
        count = int(np.prod(shape))
        out.append(flat[offset : offset + count].reshape(shape))
        offset += count
    return out


def carry_weights(last_ids, backward):
    count, mine = (last_ids.shape[0], lax.axis_index("seq"))
    before = jnp.concatenate([jnp.full((1,), -1.0, last_ids.dtype), last_ids[:-1]])
    flags = (last_ids != before).astype(jnp.int32)
    order = jnp.arange(count)
    upto = jnp.sum(jnp.where(order[None, :] <= order[:, None], flags[None, :], 0), axis=1)
    if backward:
        below = upto - flags
        at_mine = jnp.sum(jnp.where(order == mine, upto, 0))
        chosen = (order > mine) & (below == at_mine)
    else:
        at_prev = jnp.sum(jnp.where(order == mine - 1, upto, 0))
        chosen = (order < mine) & (upto == at_prev)
    return chosen.astype(jnp.float32)


def gathered_sum(packed, weights_of):
    pieces = lax.all_gather(packed, "seq")
    weights = weights_of(pieces)
    return jnp.sum(weights[:, None, None] * pieces, axis=0), pieces


def taylor_table(feat_width):
    row_index, col_index = np.triu_indices(feat_width)
    taylor_map = np.zeros((feat_width * feat_width, len(row_index)), np.float32)
    taylor_map[row_index * feat_width + col_index, np.arange(len(row_index))] = np.where(
        row_index == col_index, 1.0 / np.sqrt(2.0), 1.0
    )
    return jnp.asarray(taylor_map)


def expand_features(vectors, taylor_map):
    lead_shape = vectors.shape[:-1]
    feat_width = vectors.shape[-1]
    outer_prod = (vectors[..., :, None] * vectors[..., None, :]).reshape(
        lead_shape + (feat_width * feat_width,)
    )
    square = jnp.einsum(
        "thp,pc->thc", outer_prod, taylor_map.astype(vectors.dtype), precision=highest
    )
    return jnp.concatenate([jnp.ones(lead_shape + (1,), vectors.dtype), vectors, square], axis=-1)


def block_forward(query_raw, key_raw, value_all, doc_local, prev_id, state_in, norm_in, taylor_map):
    length = query_raw.shape[0]
    queries = (0.5 * query_raw).reshape(length, HEADS, FEAT)
    key_feats = (0.5 * key_raw).reshape(length, HEADS, FEAT)
    values = value_all.reshape(length, HEADS, HEAD_DIM)
    scores = jnp.einsum("thf,shf->hts", queries, key_feats, precision=highest)
    kernel = 1.0 + scores + 0.5 * scores * scores
    positions = jnp.arange(length)
    allowed = (positions[:, None] >= positions[None, :]) & (
        doc_local[:, None] == doc_local[None, :]
    )
    kernel = jnp.where(allowed[None], kernel, 0.0)
    numerator = jnp.einsum("hts,shd->thd", kernel, values, precision=highest)
    denominator = jnp.sum(kernel, axis=2).T
    carried = (doc_local == prev_id).astype(kernel.dtype)[:, None]
    phi_query = expand_features(queries, taylor_map)
    numerator = numerator + carried[:, :, None] * jnp.einsum(
        "thf,hfd->thd", phi_query, state_in, precision=highest
    )
    denominator = denominator + carried * jnp.einsum(
        "thf,hf->th", phi_query, norm_in, precision=highest
    )
    return (numerator / denominator[:, :, None]).reshape(length, HEADS * HEAD_DIM)


def block_summary(key_raw, value_all, doc_local, taylor_map):
    length = key_raw.shape[0]
    key_feats = (0.5 * key_raw).reshape(length, HEADS, FEAT)
    values = value_all.reshape(length, HEADS, HEAD_DIM)
    phi_key = expand_features(key_feats, taylor_map)
    tail_mask = (doc_local == doc_local[-1]).astype(phi_key.dtype)[:, None, None]
    weighted = phi_key * tail_mask
    state_sum = jnp.einsum("thf,thd->hfd", weighted, values, precision=highest)
    norm_sum = jnp.sum(weighted, axis=0)
    return (state_sum, norm_sum)


def on_device(tokens, query_weight, key_weight, value_weight, cotangent, doc_ids):
    inputs = tokens[0]
    doc_local = doc_ids[0]
    cotan_local = cotangent[0]
    taylor_map = taylor_table(FEAT)
    width_qk = HEADS * FEAT
    weights = jnp.concatenate([query_weight, key_weight, value_weight], axis=1)
    projected = jnp.dot(inputs, weights, preferred_element_type=jnp.float32)

    def summary(proj_in):
        return block_summary(
            proj_in[:, width_qk : 2 * width_qk], proj_in[:, 2 * width_qk :], doc_local, taylor_map
        )

    (state_loc, norm_loc), summary_pull = jax.vjp(summary, projected)
    last_id = doc_local[-1:].astype(jnp.float32)
    shapes = (state_loc.shape, norm_loc.shape, (1,))
    id_index = state_loc.size + norm_loc.size
    packed = pack_rows((state_loc, norm_loc, last_id))

    def ids_of(pieces):
        return pieces.reshape(pieces.shape[0], -1)[:, id_index]

    forward_sum, pieces = gathered_sum(packed, lambda got: carry_weights(ids_of(got), False))
    last_ids = ids_of(pieces)
    state_in, norm_in, _ = unpack_rows(forward_sum, shapes)
    mine = lax.axis_index("seq")
    prev_id = jnp.sum(jnp.where(jnp.arange(last_ids.shape[0]) == mine - 1, last_ids, 0.0))
    prev_id = jnp.where(mine > 0, prev_id, -1.0).astype(jnp.int32)

    def attend(proj_in, state_sum, norm_sum):
        return block_forward(
            proj_in[:, :width_qk],
            proj_in[:, width_qk : 2 * width_qk],
            proj_in[:, 2 * width_qk :],
            doc_local,
            prev_id,
            state_sum,
            norm_sum,
            taylor_map,
        )

    output, attend_pull = jax.vjp(attend, projected, state_in, norm_in)
    grad_direct, grad_state_in, grad_norm_in = attend_pull(cotan_local.astype(jnp.float32))
    back_weights = carry_weights(last_ids, True)
    backward_sum, _ = gathered_sum(
        pack_rows((grad_state_in, grad_norm_in)), lambda got: back_weights
    )
    grad_state_loc, grad_norm_loc = unpack_rows(backward_sum, shapes[:2])
    (grad_carried,) = summary_pull((grad_state_loc, grad_norm_loc))
    grad_projected = (grad_direct + grad_carried).astype(jnp.bfloat16)
    grad_input = jnp.dot(grad_projected, weights.T, preferred_element_type=jnp.float32).astype(
        jnp.bfloat16
    )
    tokens_pack = lax.all_gather(inputs.astype(jnp.float32), "seq", axis=0, tiled=True)
    grad_cols = lax.all_to_all(
        grad_projected.astype(jnp.float32), "seq", split_axis=1, concat_axis=0, tiled=True
    )
    pack_part = lax.dot_general(
        tokens_pack,
        grad_cols,
        (((0,), (0,)), ((), ())),
        precision=highest,
        preferred_element_type=jnp.float32,
    )
    row_part = lax.psum_scatter(pack_part, "dp", scatter_dimension=0, tiled=True)
    grad_proj = lax.all_to_all(row_part, "seq", split_axis=0, concat_axis=1, tiled=True)
    return (output.astype(jnp.bfloat16)[None], grad_input[None], grad_proj)


def solution(mesh):
    return jax.shard_map(
        on_device,
        mesh=mesh,
        in_specs=(P("dp", "seq", None), P(), P(), P(), P("dp", "seq", None), P("dp", "seq")),
        out_specs=(P("dp", "seq", None), P("dp", "seq", None), P(("dp", "seq"), None)),
        check_vma=False,
    )
```

```python
import jax
import jax.numpy as jnp
import numpy as np
from jax import lax
from jax.sharding import PartitionSpec as P

HEADS = 16
FEAT = 16
HEAD_DIM = 128


highest = lax.Precision.HIGHEST


def pack_heads(state, norm, extra):
    heads, feats, lanes = state.shape
    rows = -(-(feats + 3) // 8) * 8
    norm_rows = jnp.pad(norm, ((0, 0), (0, 2 * lanes - feats))).reshape(heads, 2, lanes)
    extra_rows = jnp.broadcast_to(extra, (heads, 1, lanes)).astype(state.dtype)
    filler = jnp.zeros((heads, rows - feats - 3, lanes), state.dtype)
    return jnp.concatenate([state, norm_rows, extra_rows, filler], axis=1)


def unpack_heads(packed, feats):
    heads, _, lanes = packed.shape
    state = packed[:, :feats, :]
    norm = packed[:, feats : feats + 2, :].reshape(heads, 2 * lanes)[:, :feats]
    return state, norm


def carry_weights(last_ids, backward):
    count, mine = (last_ids.shape[0], lax.axis_index("seq"))
    before = jnp.concatenate([jnp.full((1,), -1.0, last_ids.dtype), last_ids[:-1]])
    flags = (last_ids != before).astype(jnp.int32)
    order = jnp.arange(count)
    upto = jnp.sum(jnp.where(order[None, :] <= order[:, None], flags[None, :], 0), axis=1)
    if backward:
        below = upto - flags
        at_mine = jnp.sum(jnp.where(order == mine, upto, 0))
        chosen = (order > mine) & (below == at_mine)
    else:
        at_prev = jnp.sum(jnp.where(order == mine - 1, upto, 0))
        chosen = (order < mine) & (upto == at_prev)
    return chosen.astype(jnp.float32)


def gathered_sum(packed, weights_of):
    pieces = lax.all_gather(packed, "seq")
    weights = weights_of(pieces)
    scale = weights.reshape(weights.shape + (1,) * (pieces.ndim - 1))
    return jnp.sum(scale * pieces, axis=0), pieces


def taylor_table(feat_width):
    row_index, col_index = np.triu_indices(feat_width)
    taylor_map = np.zeros((feat_width * feat_width, len(row_index)), np.float32)
    taylor_map[row_index * feat_width + col_index, np.arange(len(row_index))] = np.where(
        row_index == col_index, 1.0 / np.sqrt(2.0), 1.0
    )
    return jnp.asarray(taylor_map)


def expand_features(vectors, taylor_map):
    lead_shape = vectors.shape[:-1]
    feat_width = vectors.shape[-1]
    outer_prod = (vectors[..., :, None] * vectors[..., None, :]).reshape(
        lead_shape + (feat_width * feat_width,)
    )
    square = jnp.einsum(
        "thp,pc->thc", outer_prod, taylor_map.astype(vectors.dtype), precision=highest
    )
    return jnp.concatenate([jnp.ones(lead_shape + (1,), vectors.dtype), vectors, square], axis=-1)


def block_forward(query_raw, key_raw, value_all, doc_local, prev_id, state_in, norm_in, taylor_map):
    length = query_raw.shape[0]
    queries = (0.5 * query_raw).reshape(length, HEADS, FEAT)
    key_feats = (0.5 * key_raw).reshape(length, HEADS, FEAT)
    values = value_all.reshape(length, HEADS, HEAD_DIM)
    scores = jnp.einsum("thf,shf->hts", queries, key_feats, precision=highest)
    kernel = 1.0 + scores + 0.5 * scores * scores
    positions = jnp.arange(length)
    allowed = (positions[:, None] >= positions[None, :]) & (
        doc_local[:, None] == doc_local[None, :]
    )
    kernel = jnp.where(allowed[None], kernel, 0.0)
    numerator = jnp.einsum("hts,shd->thd", kernel, values, precision=highest)
    denominator = jnp.sum(kernel, axis=2).T
    carried = (doc_local == prev_id).astype(kernel.dtype)[:, None]
    phi_query = expand_features(queries, taylor_map)
    numerator = numerator + carried[:, :, None] * jnp.einsum(
        "thf,hfd->thd", phi_query, state_in, precision=highest
    )
    denominator = denominator + carried * jnp.einsum(
        "thf,hf->th", phi_query, norm_in, precision=highest
    )
    return (numerator / denominator[:, :, None]).reshape(length, HEADS * HEAD_DIM)


def block_summary(key_raw, value_all, doc_local, taylor_map):
    length = key_raw.shape[0]
    key_feats = (0.5 * key_raw).reshape(length, HEADS, FEAT)
    values = value_all.reshape(length, HEADS, HEAD_DIM)
    phi_key = expand_features(key_feats, taylor_map)
    tail_mask = (doc_local == doc_local[-1]).astype(phi_key.dtype)[:, None, None]
    weighted = phi_key * tail_mask
    state_sum = jnp.einsum("thf,thd->hfd", weighted, values, precision=highest)
    norm_sum = jnp.sum(weighted, axis=0)
    return (state_sum, norm_sum)


def on_device(tokens, query_weight, key_weight, value_weight, cotangent, doc_ids):
    inputs = tokens[0]
    doc_local = doc_ids[0]
    cotan_local = cotangent[0]
    taylor_map = taylor_table(FEAT)
    width_qk = HEADS * FEAT
    weights = jnp.concatenate([query_weight, key_weight, value_weight], axis=1)
    projected = jnp.dot(inputs, weights, preferred_element_type=jnp.float32)

    def summary(proj_in):
        return block_summary(
            proj_in[:, width_qk : 2 * width_qk], proj_in[:, 2 * width_qk :], doc_local, taylor_map
        )

    (state_loc, norm_loc), summary_pull = jax.vjp(summary, projected)
    feats = state_loc.shape[1]
    last_id = doc_local[-1].astype(jnp.float32)
    packed = pack_heads(state_loc, norm_loc, last_id)

    def ids_of(pieces):
        return pieces[:, 0, feats + 2, 0]

    forward_sum, pieces = gathered_sum(packed, lambda got: carry_weights(ids_of(got), False))
    last_ids = ids_of(pieces)
    state_in, norm_in = unpack_heads(forward_sum, feats)
    tokens_wide, state_in, norm_in = lax.optimization_barrier(
        (inputs.astype(jnp.float32), state_in, norm_in)
    )
    tokens_pack = lax.all_gather(tokens_wide, "seq", axis=0, tiled=True)
    mine = lax.axis_index("seq")
    prev_id = jnp.sum(jnp.where(jnp.arange(last_ids.shape[0]) == mine - 1, last_ids, 0.0))
    prev_id = jnp.where(mine > 0, prev_id, -1.0).astype(jnp.int32)

    def attend(proj_in, state_sum, norm_sum):
        return block_forward(
            proj_in[:, :width_qk],
            proj_in[:, width_qk : 2 * width_qk],
            proj_in[:, 2 * width_qk :],
            doc_local,
            prev_id,
            state_sum,
            norm_sum,
            taylor_map,
        )

    output, attend_pull = jax.vjp(attend, projected, state_in, norm_in)
    grad_direct, grad_state_in, grad_norm_in = attend_pull(cotan_local.astype(jnp.float32))
    back_weights = carry_weights(last_ids, True)
    back_packed = pack_heads(grad_state_in, grad_norm_in, jnp.zeros((), jnp.float32))
    tokens_pack, back_packed = lax.optimization_barrier((tokens_pack, back_packed))
    backward_sum, _ = gathered_sum(back_packed, lambda got: back_weights)
    grad_state_loc, grad_norm_loc = unpack_heads(backward_sum, feats)
    (grad_carried,) = summary_pull((grad_state_loc, grad_norm_loc))
    grad_projected = (grad_direct + grad_carried).astype(jnp.bfloat16)
    grad_input = jnp.dot(grad_projected, weights.T, preferred_element_type=jnp.float32).astype(
        jnp.bfloat16
    )
    grad_cols = lax.all_to_all(
        grad_projected.astype(jnp.float32), "seq", split_axis=1, concat_axis=0, tiled=True
    )
    pack_part = lax.dot_general(
        tokens_pack,
        grad_cols,
        (((0,), (0,)), ((), ())),
        precision=highest,
        preferred_element_type=jnp.float32,
    )
    row_part = lax.psum_scatter(pack_part, "dp", scatter_dimension=0, tiled=True)
    grad_proj = lax.all_to_all(row_part, "seq", split_axis=0, concat_axis=1, tiled=True)
    return (output.astype(jnp.bfloat16)[None], grad_input[None], grad_proj)


def solution(mesh):
    return jax.shard_map(
        on_device,
        mesh=mesh,
        in_specs=(P("dp", "seq", None), P(), P(), P(), P("dp", "seq", None), P("dp", "seq")),
        out_specs=(P("dp", "seq", None), P("dp", "seq", None), P(("dp", "seq"), None)),
        check_vma=False,
    )
```

```python
import jax
import jax.numpy as jnp
import numpy as np
from jax import lax
from jax.sharding import PartitionSpec as P

HEADS = 16
FEAT = 16
HEAD_DIM = 128


highest = lax.Precision.HIGHEST


def pack_heads(state, norm, extra):
    heads, feats, lanes = state.shape
    rows = -(-(feats + 3) // 8) * 8
    norm_rows = jnp.pad(norm, ((0, 0), (0, 2 * lanes - feats))).reshape(heads, 2, lanes)
    extra_rows = jnp.broadcast_to(extra, (heads, 1, lanes)).astype(state.dtype)
    filler = jnp.zeros((heads, rows - feats - 3, lanes), state.dtype)
    return jnp.concatenate([state, norm_rows, extra_rows, filler], axis=1)


def unpack_heads(packed, feats):
    heads, _, lanes = packed.shape
    state = packed[:, :feats, :]
    norm = packed[:, feats : feats + 2, :].reshape(heads, 2 * lanes)[:, :feats]
    return state, norm


def shifted(value, steps):
    count = lax.axis_size("seq")
    if steps > 0:
        pairs = [(source, source + steps) for source in range(count - steps)]
    else:
        pairs = [(source, source + steps) for source in range(-steps, count)]
    return lax.ppermute(value, "seq", pairs)


def segmented_scan(packed, flag_row, direction, reach):
    carry = shifted(packed, direction)
    covered = 1
    while covered < reach:
        earlier = shifted(carry, direction * covered)
        carry = jnp.where(carry[0, flag_row, 0] > 0, carry, carry + earlier)
        covered *= 2
    return carry


def taylor_table(feat_width):
    row_index, col_index = np.triu_indices(feat_width)
    taylor_map = np.zeros((feat_width * feat_width, len(row_index)), np.float32)
    taylor_map[row_index * feat_width + col_index, np.arange(len(row_index))] = np.where(
        row_index == col_index, 1.0 / np.sqrt(2.0), 1.0
    )
    return jnp.asarray(taylor_map)


def expand_features(vectors, taylor_map):
    lead_shape = vectors.shape[:-1]
    feat_width = vectors.shape[-1]
    outer_prod = (vectors[..., :, None] * vectors[..., None, :]).reshape(
        lead_shape + (feat_width * feat_width,)
    )
    square = jnp.einsum(
        "thp,pc->thc", outer_prod, taylor_map.astype(vectors.dtype), precision=highest
    )
    return jnp.concatenate([jnp.ones(lead_shape + (1,), vectors.dtype), vectors, square], axis=-1)


def block_forward(query_raw, key_raw, value_all, doc_local, prev_id, state_in, norm_in, taylor_map):
    length = query_raw.shape[0]
    queries = (0.5 * query_raw).reshape(length, HEADS, FEAT)
    key_feats = (0.5 * key_raw).reshape(length, HEADS, FEAT)
    values = value_all.reshape(length, HEADS, HEAD_DIM)
    scores = jnp.einsum("thf,shf->hts", queries, key_feats, precision=highest)
    kernel = 1.0 + scores + 0.5 * scores * scores
    positions = jnp.arange(length)
    allowed = (positions[:, None] >= positions[None, :]) & (
        doc_local[:, None] == doc_local[None, :]
    )
    kernel = jnp.where(allowed[None], kernel, 0.0)
    numerator = jnp.einsum("hts,shd->thd", kernel, values, precision=highest)
    denominator = jnp.sum(kernel, axis=2).T
    carried = (doc_local == prev_id).astype(kernel.dtype)[:, None]
    phi_query = expand_features(queries, taylor_map)
    numerator = numerator + carried[:, :, None] * jnp.einsum(
        "thf,hfd->thd", phi_query, state_in, precision=highest
    )
    denominator = denominator + carried * jnp.einsum(
        "thf,hf->th", phi_query, norm_in, precision=highest
    )
    return (numerator / denominator[:, :, None]).reshape(length, HEADS * HEAD_DIM)


def block_summary(key_raw, value_all, doc_local, taylor_map):
    length = key_raw.shape[0]
    key_feats = (0.5 * key_raw).reshape(length, HEADS, FEAT)
    values = value_all.reshape(length, HEADS, HEAD_DIM)
    phi_key = expand_features(key_feats, taylor_map)
    tail_mask = (doc_local == doc_local[-1]).astype(phi_key.dtype)[:, None, None]
    weighted = phi_key * tail_mask
    state_sum = jnp.einsum("thf,thd->hfd", weighted, values, precision=highest)
    norm_sum = jnp.sum(weighted, axis=0)
    return (state_sum, norm_sum)


def on_device(tokens, query_weight, key_weight, value_weight, cotangent, doc_ids):
    inputs = tokens[0]
    doc_local = doc_ids[0]
    cotan_local = cotangent[0]
    taylor_map = taylor_table(FEAT)
    width_qk = HEADS * FEAT
    weights = jnp.concatenate([query_weight, key_weight, value_weight], axis=1)
    projected = jnp.dot(inputs, weights, preferred_element_type=jnp.float32)

    def summary(proj_in):
        return block_summary(
            proj_in[:, width_qk : 2 * width_qk], proj_in[:, 2 * width_qk :], doc_local, taylor_map
        )

    (state_loc, norm_loc), summary_pull = jax.vjp(summary, projected)
    feats = state_loc.shape[1]
    count, length = (lax.axis_size("seq"), doc_local.shape[0])
    longest = count * length // 2
    reach = min(count - 1, -(-(longest - 1) // length))
    prev_id = shifted(doc_local[-1:] + 1, 1)[0] - 1
    boundary = (doc_local[-1] != prev_id).astype(jnp.float32)
    forward_sum = segmented_scan(pack_heads(state_loc, norm_loc, boundary), feats + 2, 1, reach)
    state_in, norm_in = unpack_heads(forward_sum, feats)
    tokens_pack = lax.all_gather(inputs.astype(jnp.float32), "seq", axis=0, tiled=True)

    def attend(proj_in, state_sum, norm_sum):
        return block_forward(
            proj_in[:, :width_qk],
            proj_in[:, width_qk : 2 * width_qk],
            proj_in[:, 2 * width_qk :],
            doc_local,
            prev_id,
            state_sum,
            norm_sum,
            taylor_map,
        )

    output, attend_pull = jax.vjp(attend, projected, state_in, norm_in)
    grad_direct, grad_state_in, grad_norm_in = attend_pull(cotan_local.astype(jnp.float32))
    backward_sum = segmented_scan(
        pack_heads(grad_state_in, grad_norm_in, boundary), feats + 2, -1, reach
    )
    grad_state_loc, grad_norm_loc = unpack_heads(backward_sum, feats)
    (grad_carried,) = summary_pull((grad_state_loc, grad_norm_loc))
    grad_projected = (grad_direct + grad_carried).astype(jnp.bfloat16)
    grad_input = jnp.dot(grad_projected, weights.T, preferred_element_type=jnp.float32).astype(
        jnp.bfloat16
    )
    grad_cols = lax.all_to_all(
        grad_projected.astype(jnp.float32), "seq", split_axis=1, concat_axis=0, tiled=True
    )
    pack_part = lax.dot_general(
        tokens_pack,
        grad_cols,
        (((0,), (0,)), ((), ())),
        precision=highest,
        preferred_element_type=jnp.float32,
    )
    row_part = lax.psum_scatter(pack_part, "dp", scatter_dimension=0, tiled=True)
    grad_proj = lax.all_to_all(row_part, "seq", split_axis=0, concat_axis=1, tiled=True)
    return (output.astype(jnp.bfloat16)[None], grad_input[None], grad_proj)


def solution(mesh):
    return jax.shard_map(
        on_device,
        mesh=mesh,
        in_specs=(P("dp", "seq", None), P(), P(), P(), P("dp", "seq", None), P("dp", "seq")),
        out_specs=(P("dp", "seq", None), P("dp", "seq", None), P(("dp", "seq"), None)),
        check_vma=False,
    )
```

```python
import jax
import jax.numpy as jnp
import numpy as np
from jax import lax
from jax.sharding import PartitionSpec as P

HEADS = 16
FEAT = 16
HEAD_DIM = 128


highest = lax.Precision.HIGHEST


def pack_heads(state, norm, extra):
    heads, feats, lanes = state.shape
    rows = -(-(feats + 3) // 8) * 8
    norm_rows = jnp.pad(norm, ((0, 0), (0, 2 * lanes - feats))).reshape(heads, 2, lanes)
    extra_rows = jnp.broadcast_to(extra, (heads, 1, lanes)).astype(state.dtype)
    filler = jnp.zeros((heads, rows - feats - 3, lanes), state.dtype)
    return jnp.concatenate([state, norm_rows, extra_rows, filler], axis=1)


def unpack_heads(packed, feats):
    heads, _, lanes = packed.shape
    state = packed[:, :feats, :]
    norm = packed[:, feats : feats + 2, :].reshape(heads, 2 * lanes)[:, :feats]
    return state, norm


def shifted(value, steps):
    count = lax.axis_size("seq")
    if steps > 0:
        pairs = [(source, source + steps) for source in range(count - steps)]
    else:
        pairs = [(source, source + steps) for source in range(-steps, count)]
    return lax.ppermute(value, "seq", pairs)


def segmented_scan(packed, flag_row, direction, reach):
    carry = shifted(packed, direction)
    covered = 1
    while covered < reach:
        earlier = shifted(carry, direction * covered)
        carry = jnp.where(carry[0, flag_row, 0] > 0, carry, carry + earlier)
        covered *= 2
    return carry


def taylor_table(feat_width):
    row_index, col_index = np.triu_indices(feat_width)
    taylor_map = np.zeros((feat_width * feat_width, len(row_index)), np.float32)
    taylor_map[row_index * feat_width + col_index, np.arange(len(row_index))] = np.where(
        row_index == col_index, 1.0 / np.sqrt(2.0), 1.0
    )
    return jnp.asarray(taylor_map)


def expand_features(vectors, taylor_map):
    lead_shape = vectors.shape[:-1]
    feat_width = vectors.shape[-1]
    outer_prod = (vectors[..., :, None] * vectors[..., None, :]).reshape(
        lead_shape + (feat_width * feat_width,)
    )
    square = jnp.einsum(
        "thp,pc->thc", outer_prod, taylor_map.astype(vectors.dtype), precision=highest
    )
    return jnp.concatenate([jnp.ones(lead_shape + (1,), vectors.dtype), vectors, square], axis=-1)


def block_forward(query_raw, key_raw, value_all, doc_local, prev_id, state_in, norm_in, taylor_map):
    length = query_raw.shape[0]
    queries = (0.5 * query_raw).reshape(length, HEADS, FEAT)
    key_feats = (0.5 * key_raw).reshape(length, HEADS, FEAT)
    values = value_all.reshape(length, HEADS, HEAD_DIM)
    scores = jnp.einsum("thf,shf->hts", queries, key_feats, precision=highest)
    kernel = 1.0 + scores + 0.5 * scores * scores
    positions = jnp.arange(length)
    allowed = (positions[:, None] >= positions[None, :]) & (
        doc_local[:, None] == doc_local[None, :]
    )
    kernel = jnp.where(allowed[None], kernel, 0.0)
    numerator = jnp.einsum("hts,shd->thd", kernel, values, precision=highest)
    denominator = jnp.sum(kernel, axis=2).T
    carried = (doc_local == prev_id).astype(kernel.dtype)[:, None]
    phi_query = expand_features(queries, taylor_map)
    numerator = numerator + carried[:, :, None] * jnp.einsum(
        "thf,hfd->thd", phi_query, state_in, precision=highest
    )
    denominator = denominator + carried * jnp.einsum(
        "thf,hf->th", phi_query, norm_in, precision=highest
    )
    return (numerator / denominator[:, :, None]).reshape(length, HEADS * HEAD_DIM)


def block_summary(key_raw, value_all, doc_local, taylor_map):
    length = key_raw.shape[0]
    key_feats = (0.5 * key_raw).reshape(length, HEADS, FEAT)
    values = value_all.reshape(length, HEADS, HEAD_DIM)
    phi_key = expand_features(key_feats, taylor_map)
    tail_mask = (doc_local == doc_local[-1]).astype(phi_key.dtype)[:, None, None]
    weighted = phi_key * tail_mask
    state_sum = jnp.einsum("thf,thd->hfd", weighted, values, precision=highest)
    norm_sum = jnp.sum(weighted, axis=0)
    return (state_sum, norm_sum)


def on_device(tokens, query_weight, key_weight, value_weight, cotangent, doc_ids):
    inputs = tokens[0]
    doc_local = doc_ids[0]
    cotan_local = cotangent[0]
    taylor_map = taylor_table(FEAT)
    width_qk = HEADS * FEAT
    parts = (query_weight, key_weight, value_weight)
    projected = jnp.concatenate(
        [jnp.dot(inputs, part, preferred_element_type=jnp.float32) for part in parts], axis=1
    )

    def summary(proj_in):
        return block_summary(
            proj_in[:, width_qk : 2 * width_qk], proj_in[:, 2 * width_qk :], doc_local, taylor_map
        )

    (state_loc, norm_loc), summary_pull = jax.vjp(summary, projected)
    feats = state_loc.shape[1]
    count, length = (lax.axis_size("seq"), doc_local.shape[0])
    longest = count * length // 2
    reach = min(count - 1, -(-(longest - 1) // length))
    prev_id = shifted(doc_local[-1:] + 1, 1)[0] - 1
    boundary = (doc_local[-1] != prev_id).astype(jnp.float32)
    forward_sum = segmented_scan(pack_heads(state_loc, norm_loc, boundary), feats + 2, 1, reach)
    state_in, norm_in = unpack_heads(forward_sum, feats)
    tokens_pack = lax.all_gather(inputs.astype(jnp.float32), "seq", axis=0, tiled=True)

    def attend(proj_in, state_sum, norm_sum):
        return block_forward(
            proj_in[:, :width_qk],
            proj_in[:, width_qk : 2 * width_qk],
            proj_in[:, 2 * width_qk :],
            doc_local,
            prev_id,
            state_sum,
            norm_sum,
            taylor_map,
        )

    output, attend_pull = jax.vjp(attend, projected, state_in, norm_in)
    grad_direct, grad_state_in, grad_norm_in = attend_pull(cotan_local.astype(jnp.float32))
    backward_sum = segmented_scan(
        pack_heads(grad_state_in, grad_norm_in, boundary), feats + 2, -1, reach
    )
    grad_state_loc, grad_norm_loc = unpack_heads(backward_sum, feats)
    (grad_carried,) = summary_pull((grad_state_loc, grad_norm_loc))
    grad_projected = (grad_direct + grad_carried).astype(jnp.bfloat16)
    edges = np.cumsum([0] + [part.shape[1] for part in parts])
    grad_input = sum(
        lax.dot_general(
            grad_projected[:, start:stop],
            part,
            (((1,), (1,)), ((), ())),
            preferred_element_type=jnp.float32,
        )
        for part, start, stop in zip(parts, edges[:-1], edges[1:])
    ).astype(jnp.bfloat16)
    grad_cols = lax.all_to_all(
        grad_projected.astype(jnp.float32), "seq", split_axis=1, concat_axis=0, tiled=True
    )
    pack_part = lax.dot_general(
        tokens_pack,
        grad_cols,
        (((0,), (0,)), ((), ())),
        precision=lax.Precision.HIGH,
        preferred_element_type=jnp.float32,
    )
    row_part = lax.psum_scatter(pack_part, "dp", scatter_dimension=0, tiled=True)
    grad_proj = lax.all_to_all(row_part, "seq", split_axis=0, concat_axis=1, tiled=True)
    return (output.astype(jnp.bfloat16)[None], grad_input[None], grad_proj)


def solution(mesh):
    return jax.shard_map(
        on_device,
        mesh=mesh,
        in_specs=(P("dp", "seq", None), P(), P(), P(), P("dp", "seq", None), P("dp", "seq")),
        out_specs=(P("dp", "seq", None), P("dp", "seq", None), P(("dp", "seq"), None)),
        check_vma=False,
    )
```

```python
import jax
import jax.numpy as jnp
import numpy as np
from jax import lax
from jax.sharding import PartitionSpec as P

HEADS = 16
FEAT = 16
HEAD_DIM = 128


highest = lax.Precision.HIGHEST


def pack_heads(state, norm, extra):
    heads, feats, lanes = state.shape
    rows = -(-(feats + 3) // 8) * 8
    norm_rows = jnp.pad(norm, ((0, 0), (0, 2 * lanes - feats))).reshape(heads, 2, lanes)
    extra_rows = jnp.broadcast_to(extra, (heads, 1, lanes)).astype(state.dtype)
    filler = jnp.zeros((heads, rows - feats - 3, lanes), state.dtype)
    return jnp.concatenate([state, norm_rows, extra_rows, filler], axis=1)


def unpack_heads(packed, feats):
    heads, _, lanes = packed.shape
    state = packed[:, :feats, :]
    norm = packed[:, feats : feats + 2, :].reshape(heads, 2 * lanes)[:, :feats]
    return state, norm


def shifted(value, steps):
    count = lax.axis_size("seq")
    if steps > 0:
        pairs = [(source, source + steps) for source in range(count - steps)]
    else:
        pairs = [(source, source + steps) for source in range(-steps, count)]
    return lax.ppermute(value, "seq", pairs)


def segmented_scan(packed, flag_row, direction, reach):
    carry = shifted(packed, direction)
    covered = 1
    while covered < reach:
        earlier = shifted(carry, direction * covered)
        carry = jnp.where(carry[0, flag_row, 0] > 0, carry, carry + earlier)
        covered *= 2
    return carry


def taylor_table(feat_width):
    row_index, col_index = np.triu_indices(feat_width)
    taylor_map = np.zeros((feat_width * feat_width, len(row_index)), np.float32)
    taylor_map[row_index * feat_width + col_index, np.arange(len(row_index))] = np.where(
        row_index == col_index, 1.0 / np.sqrt(2.0), 1.0
    )
    return jnp.asarray(taylor_map)


def expand_features(vectors, taylor_map):
    lead_shape = vectors.shape[:-1]
    feat_width = vectors.shape[-1]
    outer_prod = (vectors[..., :, None] * vectors[..., None, :]).reshape(
        lead_shape + (feat_width * feat_width,)
    )
    square = jnp.einsum(
        "thp,pc->thc", outer_prod, taylor_map.astype(vectors.dtype), precision=highest
    )
    return jnp.concatenate([jnp.ones(lead_shape + (1,), vectors.dtype), vectors, square], axis=-1)


def block_forward(query_raw, key_raw, value_all, doc_local, prev_id, state_in, norm_in, taylor_map):
    length = query_raw.shape[0]
    queries = (0.5 * query_raw).reshape(length, HEADS, FEAT)
    key_feats = (0.5 * key_raw).reshape(length, HEADS, FEAT)
    values = value_all.reshape(length, HEADS, HEAD_DIM)
    scores = jnp.einsum("thf,shf->hts", queries, key_feats, precision=highest)
    kernel = 1.0 + scores + 0.5 * scores * scores
    positions = jnp.arange(length)
    allowed = (positions[:, None] >= positions[None, :]) & (
        doc_local[:, None] == doc_local[None, :]
    )
    kernel = jnp.where(allowed[None], kernel, 0.0)
    numerator = jnp.einsum("hts,shd->thd", kernel, values, precision=highest)
    denominator = jnp.sum(kernel, axis=2).T
    carried = (doc_local == prev_id).astype(kernel.dtype)[:, None]
    phi_query = expand_features(queries, taylor_map)
    numerator = numerator + carried[:, :, None] * jnp.einsum(
        "thf,hfd->thd", phi_query, state_in, precision=highest
    )
    denominator = denominator + carried * jnp.einsum(
        "thf,hf->th", phi_query, norm_in, precision=highest
    )
    return (numerator / denominator[:, :, None]).reshape(length, HEADS * HEAD_DIM)


def block_summary(key_raw, value_all, doc_local, taylor_map):
    length = key_raw.shape[0]
    key_feats = (0.5 * key_raw).reshape(length, HEADS, FEAT)
    values = value_all.reshape(length, HEADS, HEAD_DIM)
    phi_key = expand_features(key_feats, taylor_map)
    tail_mask = (doc_local == doc_local[-1]).astype(phi_key.dtype)[:, None, None]
    weighted = phi_key * tail_mask
    state_sum = jnp.einsum("thf,thd->hfd", weighted, values, precision=highest)
    norm_sum = jnp.sum(weighted, axis=0)
    return (state_sum, norm_sum)


def on_device(tokens, query_weight, key_weight, value_weight, cotangent, doc_ids):
    inputs = tokens[0]
    doc_local = doc_ids[0]
    cotan_local = cotangent[0]
    taylor_map = taylor_table(FEAT)
    width_qk = HEADS * FEAT
    parts = (query_weight, key_weight, value_weight)
    projected = lax.optimization_barrier(
        jnp.concatenate(
            [jnp.dot(inputs, part, preferred_element_type=jnp.float32) for part in parts], axis=1
        )
    )

    def summary(proj_in):
        return block_summary(
            proj_in[:, width_qk : 2 * width_qk], proj_in[:, 2 * width_qk :], doc_local, taylor_map
        )

    (state_loc, norm_loc), summary_pull = jax.vjp(summary, projected)
    feats = state_loc.shape[1]
    count, length = (lax.axis_size("seq"), doc_local.shape[0])
    longest = count * length // 2
    reach = min(count - 1, -(-(longest - 1) // length))
    prev_id = shifted(doc_local[-1:] + 1, 1)[0] - 1
    boundary = (doc_local[-1] != prev_id).astype(jnp.float32)
    forward_sum = segmented_scan(pack_heads(state_loc, norm_loc, boundary), feats + 2, 1, reach)
    state_in, norm_in = unpack_heads(forward_sum, feats)
    tokens_pack = lax.all_gather(inputs.astype(jnp.float32), "seq", axis=0, tiled=True)

    def attend(proj_in, state_sum, norm_sum):
        return block_forward(
            proj_in[:, :width_qk],
            proj_in[:, width_qk : 2 * width_qk],
            proj_in[:, 2 * width_qk :],
            doc_local,
            prev_id,
            state_sum,
            norm_sum,
            taylor_map,
        )

    output, attend_pull = jax.vjp(attend, projected, state_in, norm_in)
    grad_direct, grad_state_in, grad_norm_in = attend_pull(cotan_local.astype(jnp.float32))
    backward_sum = segmented_scan(
        pack_heads(grad_state_in, grad_norm_in, boundary), feats + 2, -1, reach
    )
    grad_state_loc, grad_norm_loc = unpack_heads(backward_sum, feats)
    (grad_carried,) = summary_pull((grad_state_loc, grad_norm_loc))
    grad_projected = (grad_direct + grad_carried).astype(jnp.bfloat16)
    edges = np.cumsum([0] + [part.shape[1] for part in parts])
    grad_input = sum(
        lax.dot_general(
            grad_projected[:, start:stop],
            part,
            (((1,), (1,)), ((), ())),
            preferred_element_type=jnp.float32,
        )
        for part, start, stop in zip(parts, edges[:-1], edges[1:])
    ).astype(jnp.bfloat16)
    grad_cols = lax.all_to_all(
        grad_projected.astype(jnp.float32), "seq", split_axis=1, concat_axis=0, tiled=True
    )
    pack_part = lax.dot_general(
        tokens_pack,
        grad_cols,
        (((0,), (0,)), ((), ())),
        precision=lax.Precision.HIGH,
        preferred_element_type=jnp.float32,
    )
    row_part = lax.psum_scatter(pack_part, "dp", scatter_dimension=0, tiled=True)
    grad_proj = lax.all_to_all(row_part, "seq", split_axis=0, concat_axis=1, tiled=True)
    return (output.astype(jnp.bfloat16)[None], grad_input[None], grad_proj)


def solution(mesh):
    return jax.shard_map(
        on_device,
        mesh=mesh,
        in_specs=(P("dp", "seq", None), P(), P(), P(), P("dp", "seq", None), P("dp", "seq")),
        out_specs=(P("dp", "seq", None), P("dp", "seq", None), P(("dp", "seq"), None)),
        check_vma=False,
    )
```

```python
import jax
import jax.numpy as jnp
import numpy as np
from jax import lax
from jax.sharding import PartitionSpec as P

HEADS = 16
FEAT = 16
HEAD_DIM = 128


highest = lax.Precision.HIGHEST


def pack_heads(state, norm, extra):
    heads, feats, lanes = state.shape
    rows = -(-(feats + 3) // 8) * 8
    norm_rows = jnp.pad(norm, ((0, 0), (0, 2 * lanes - feats))).reshape(heads, 2, lanes)
    extra_rows = jnp.broadcast_to(extra, (heads, 1, lanes)).astype(state.dtype)
    filler = jnp.zeros((heads, rows - feats - 3, lanes), state.dtype)
    return jnp.concatenate([state, norm_rows, extra_rows, filler], axis=1)


def unpack_heads(packed, feats):
    heads, _, lanes = packed.shape
    state = packed[:, :feats, :]
    norm = packed[:, feats : feats + 2, :].reshape(heads, 2 * lanes)[:, :feats]
    return state, norm


def shifted(value, steps):
    count = lax.axis_size("seq")
    if steps > 0:
        pairs = [(source, source + steps) for source in range(count - steps)]
    else:
        pairs = [(source, source + steps) for source in range(-steps, count)]
    return lax.ppermute(value, "seq", pairs)


def direct_scan(packed, flag_row, direction, reach):
    total, keep = None, None
    for distance in range(1, reach + 1):
        piece = shifted(packed, direction * distance)
        total = piece if total is None else total + keep * piece
        stays = 1.0 - piece[0, flag_row, 0]
        keep = stays if keep is None else keep * stays
    return total


def taylor_table(feat_width):
    row_index, col_index = np.triu_indices(feat_width)
    taylor_map = np.zeros((feat_width * feat_width, len(row_index)), np.float32)
    taylor_map[row_index * feat_width + col_index, np.arange(len(row_index))] = np.where(
        row_index == col_index, 1.0 / np.sqrt(2.0), 1.0
    )
    return jnp.asarray(taylor_map)


def expand_features(vectors, taylor_map):
    lead_shape = vectors.shape[:-1]
    feat_width = vectors.shape[-1]
    outer_prod = (vectors[..., :, None] * vectors[..., None, :]).reshape(
        lead_shape + (feat_width * feat_width,)
    )
    square = jnp.einsum(
        "thp,pc->thc", outer_prod, taylor_map.astype(vectors.dtype), precision=highest
    )
    return jnp.concatenate([jnp.ones(lead_shape + (1,), vectors.dtype), vectors, square], axis=-1)


def block_forward(query_raw, key_raw, value_all, doc_local, prev_id, state_in, norm_in, taylor_map):
    length = query_raw.shape[0]
    queries = (0.5 * query_raw).reshape(length, HEADS, FEAT)
    key_feats = (0.5 * key_raw).reshape(length, HEADS, FEAT)
    values = value_all.reshape(length, HEADS, HEAD_DIM)
    scores = jnp.einsum("thf,shf->hts", queries, key_feats, precision=highest)
    kernel = 1.0 + scores + 0.5 * scores * scores
    positions = jnp.arange(length)
    allowed = (positions[:, None] >= positions[None, :]) & (
        doc_local[:, None] == doc_local[None, :]
    )
    kernel = jnp.where(allowed[None], kernel, 0.0)
    numerator = jnp.einsum("hts,shd->thd", kernel, values, precision=highest)
    denominator = jnp.sum(kernel, axis=2).T
    carried = (doc_local == prev_id).astype(kernel.dtype)[:, None]
    phi_query = expand_features(queries, taylor_map)
    numerator = numerator + carried[:, :, None] * jnp.einsum(
        "thf,hfd->thd", phi_query, state_in, precision=highest
    )
    denominator = denominator + carried * jnp.einsum(
        "thf,hf->th", phi_query, norm_in, precision=highest
    )
    return (numerator / denominator[:, :, None]).reshape(length, HEADS * HEAD_DIM)


def block_summary(key_raw, value_all, doc_local, taylor_map):
    length = key_raw.shape[0]
    key_feats = (0.5 * key_raw).reshape(length, HEADS, FEAT)
    values = value_all.reshape(length, HEADS, HEAD_DIM)
    phi_key = expand_features(key_feats, taylor_map)
    tail_mask = (doc_local == doc_local[-1]).astype(phi_key.dtype)[:, None, None]
    weighted = phi_key * tail_mask
    state_sum = jnp.einsum("thf,thd->hfd", weighted, values, precision=highest)
    norm_sum = jnp.sum(weighted, axis=0)
    return (state_sum, norm_sum)


def on_device(tokens, query_weight, key_weight, value_weight, cotangent, doc_ids):
    inputs = tokens[0]
    doc_local = doc_ids[0]
    cotan_local = cotangent[0]
    taylor_map = taylor_table(FEAT)
    width_qk = HEADS * FEAT
    parts = (query_weight, key_weight, value_weight)
    projected = lax.optimization_barrier(
        jnp.concatenate(
            [jnp.dot(inputs, part, preferred_element_type=jnp.float32) for part in parts], axis=1
        )
    )

    def summary(proj_in):
        return block_summary(
            proj_in[:, width_qk : 2 * width_qk], proj_in[:, 2 * width_qk :], doc_local, taylor_map
        )

    (state_loc, norm_loc), summary_pull = jax.vjp(summary, projected)
    feats = state_loc.shape[1]
    count, length = (lax.axis_size("seq"), doc_local.shape[0])
    longest = count * length // 2
    reach = min(count - 1, -(-(longest - 1) // length))
    prev_id = shifted(doc_local[-1:] + 1, 1)[0] - 1
    boundary = (doc_local[-1] != prev_id).astype(jnp.float32)
    forward_sum = direct_scan(pack_heads(state_loc, norm_loc, boundary), feats + 2, 1, reach)
    state_in, norm_in = unpack_heads(forward_sum, feats)
    tokens_pack = lax.all_gather(inputs.astype(jnp.float32), "seq", axis=0, tiled=True)

    def attend(proj_in, state_sum, norm_sum):
        return block_forward(
            proj_in[:, :width_qk],
            proj_in[:, width_qk : 2 * width_qk],
            proj_in[:, 2 * width_qk :],
            doc_local,
            prev_id,
            state_sum,
            norm_sum,
            taylor_map,
        )

    output, attend_pull = jax.vjp(attend, projected, state_in, norm_in)
    grad_direct, grad_state_in, grad_norm_in = attend_pull(cotan_local.astype(jnp.float32))
    backward_sum = direct_scan(
        pack_heads(grad_state_in, grad_norm_in, boundary), feats + 2, -1, reach
    )
    grad_state_loc, grad_norm_loc = unpack_heads(backward_sum, feats)
    (grad_carried,) = summary_pull((grad_state_loc, grad_norm_loc))
    grad_projected = (grad_direct + grad_carried).astype(jnp.bfloat16)
    edges = np.cumsum([0] + [part.shape[1] for part in parts])
    grad_input = sum(
        lax.dot_general(
            grad_projected[:, start:stop],
            part,
            (((1,), (1,)), ((), ())),
            preferred_element_type=jnp.float32,
        )
        for part, start, stop in zip(parts, edges[:-1], edges[1:])
    ).astype(jnp.bfloat16)
    grad_cols = lax.all_to_all(
        grad_projected.astype(jnp.float32), "seq", split_axis=1, concat_axis=0, tiled=True
    )
    pack_part = lax.dot_general(
        tokens_pack,
        grad_cols,
        (((0,), (0,)), ((), ())),
        precision=lax.Precision.HIGH,
        preferred_element_type=jnp.float32,
    )
    row_part = lax.psum_scatter(pack_part, "dp", scatter_dimension=0, tiled=True)
    grad_proj = lax.all_to_all(row_part, "seq", split_axis=0, concat_axis=1, tiled=True)
    return (output.astype(jnp.bfloat16)[None], grad_input[None], grad_proj)


def solution(mesh):
    return jax.shard_map(
        on_device,
        mesh=mesh,
        in_specs=(P("dp", "seq", None), P(), P(), P(), P("dp", "seq", None), P("dp", "seq")),
        out_specs=(P("dp", "seq", None), P("dp", "seq", None), P(("dp", "seq"), None)),
        check_vma=False,
    )
```

```python
import jax
import jax.numpy as jnp
import numpy as np
from jax import lax
from jax.sharding import PartitionSpec as P

HEADS = 16
FEAT = 16
HEAD_DIM = 128


highest = lax.Precision.HIGHEST


def pack_heads(state, norm, extra):
    heads, feats, lanes = state.shape
    rows = -(-(feats + 3) // 8) * 8
    norm_rows = jnp.pad(norm, ((0, 0), (0, 2 * lanes - feats))).reshape(heads, 2, lanes)
    extra_rows = jnp.broadcast_to(extra, (heads, 1, lanes)).astype(state.dtype)
    filler = jnp.zeros((heads, rows - feats - 3, lanes), state.dtype)
    return jnp.concatenate([state, norm_rows, extra_rows, filler], axis=1)


def unpack_heads(packed, feats):
    heads, _, lanes = packed.shape
    state = packed[:, :feats, :]
    norm = packed[:, feats : feats + 2, :].reshape(heads, 2 * lanes)[:, :feats]
    return state, norm


def shifted(value, steps):
    count = lax.axis_size("seq")
    if steps > 0:
        pairs = [(source, source + steps) for source in range(count - steps)]
    else:
        pairs = [(source, source + steps) for source in range(-steps, count)]
    return lax.ppermute(value, "seq", pairs)


def segmented_scan(packed, flag_row, direction, reach):
    carry = shifted(packed, direction)
    covered = 1
    while covered < reach:
        earlier = shifted(carry, direction * covered)
        carry = jnp.where(carry[0, flag_row, 0] > 0, carry, carry + earlier)
        covered *= 2
    return carry


def chip_scan(packed, flag_row, direction, reach):
    count = lax.axis_size("seq")
    if count % 2:
        return segmented_scan(packed, flag_row, direction, reach)
    chips = count // 2
    lead, other = (1, 0) if direction > 0 else (0, 1)

    def fold(near, far):
        return jnp.where(near[0, flag_row, 0] > 0, near, near + far)

    def chip_shift(value, distance):
        step = direction * distance
        pairs = [
            (2 * chip + lead, 2 * (chip + step) + lead)
            for chip in range(chips)
            if 0 <= chip + step < chips
        ]
        return lax.ppermute(value, "seq", pairs)

    partner = lax.ppermute(
        packed, "seq", [(2 * chip + other, 2 * chip + lead) for chip in range(chips)]
    )
    carry = chip_shift(fold(packed, partner), 1)
    chip_reach = min(chips - 1, -(-reach // 2))
    covered = 1
    while covered < chip_reach:
        carry = fold(carry, chip_shift(carry, covered))
        covered *= 2
    handed = lax.ppermute(
        carry, "seq", [(2 * chip + lead, 2 * chip + other) for chip in range(chips)]
    )
    core = lax.axis_index("seq") % 2
    return jnp.where(core == lead, fold(partner, carry), handed)


def taylor_table(feat_width):
    row_index, col_index = np.triu_indices(feat_width)
    taylor_map = np.zeros((feat_width * feat_width, len(row_index)), np.float32)
    taylor_map[row_index * feat_width + col_index, np.arange(len(row_index))] = np.where(
        row_index == col_index, 1.0 / np.sqrt(2.0), 1.0
    )
    return jnp.asarray(taylor_map)


def expand_features(vectors, taylor_map):
    lead_shape = vectors.shape[:-1]
    feat_width = vectors.shape[-1]
    outer_prod = (vectors[..., :, None] * vectors[..., None, :]).reshape(
        lead_shape + (feat_width * feat_width,)
    )
    square = jnp.einsum(
        "thp,pc->thc", outer_prod, taylor_map.astype(vectors.dtype), precision=highest
    )
    return jnp.concatenate([jnp.ones(lead_shape + (1,), vectors.dtype), vectors, square], axis=-1)


def block_forward(query_raw, key_raw, value_all, doc_local, prev_id, state_in, norm_in, taylor_map):
    length = query_raw.shape[0]
    queries = (0.5 * query_raw).reshape(length, HEADS, FEAT)
    key_feats = (0.5 * key_raw).reshape(length, HEADS, FEAT)
    values = value_all.reshape(length, HEADS, HEAD_DIM)
    scores = jnp.einsum("thf,shf->hts", queries, key_feats, precision=highest)
    kernel = 1.0 + scores + 0.5 * scores * scores
    positions = jnp.arange(length)
    allowed = (positions[:, None] >= positions[None, :]) & (
        doc_local[:, None] == doc_local[None, :]
    )
    kernel = jnp.where(allowed[None], kernel, 0.0)
    numerator = jnp.einsum("hts,shd->thd", kernel, values, precision=highest)
    denominator = jnp.sum(kernel, axis=2).T
    carried = (doc_local == prev_id).astype(kernel.dtype)[:, None]
    phi_query = expand_features(queries, taylor_map)
    numerator = numerator + carried[:, :, None] * jnp.einsum(
        "thf,hfd->thd", phi_query, state_in, precision=highest
    )
    denominator = denominator + carried * jnp.einsum(
        "thf,hf->th", phi_query, norm_in, precision=highest
    )
    return (numerator / denominator[:, :, None]).reshape(length, HEADS * HEAD_DIM)


def block_summary(key_raw, value_all, doc_local, taylor_map):
    length = key_raw.shape[0]
    key_feats = (0.5 * key_raw).reshape(length, HEADS, FEAT)
    values = value_all.reshape(length, HEADS, HEAD_DIM)
    phi_key = expand_features(key_feats, taylor_map)
    tail_mask = (doc_local == doc_local[-1]).astype(phi_key.dtype)[:, None, None]
    weighted = phi_key * tail_mask
    state_sum = jnp.einsum("thf,thd->hfd", weighted, values, precision=highest)
    norm_sum = jnp.sum(weighted, axis=0)
    return (state_sum, norm_sum)


def on_device(tokens, query_weight, key_weight, value_weight, cotangent, doc_ids):
    inputs = tokens[0]
    doc_local = doc_ids[0]
    cotan_local = cotangent[0]
    taylor_map = taylor_table(FEAT)
    width_qk = HEADS * FEAT
    parts = (query_weight, key_weight, value_weight)
    projected = lax.optimization_barrier(
        jnp.concatenate(
            [jnp.dot(inputs, part, preferred_element_type=jnp.float32) for part in parts], axis=1
        )
    )

    def summary(proj_in):
        return block_summary(
            proj_in[:, width_qk : 2 * width_qk], proj_in[:, 2 * width_qk :], doc_local, taylor_map
        )

    (state_loc, norm_loc), summary_pull = jax.vjp(summary, projected)
    feats = state_loc.shape[1]
    count, length = (lax.axis_size("seq"), doc_local.shape[0])
    longest = count * length // 2
    reach = min(count - 1, -(-(longest - 1) // length))
    prev_id = shifted(doc_local[-1:] + 1, 1)[0] - 1
    boundary = (doc_local[-1] != prev_id).astype(jnp.float32)
    forward_sum = chip_scan(pack_heads(state_loc, norm_loc, boundary), feats + 2, 1, reach)
    state_in, norm_in = unpack_heads(forward_sum, feats)
    tokens_pack = lax.all_gather(inputs.astype(jnp.float32), "seq", axis=0, tiled=True)

    def attend(proj_in, state_sum, norm_sum):
        return block_forward(
            proj_in[:, :width_qk],
            proj_in[:, width_qk : 2 * width_qk],
            proj_in[:, 2 * width_qk :],
            doc_local,
            prev_id,
            state_sum,
            norm_sum,
            taylor_map,
        )

    output, attend_pull = jax.vjp(attend, projected, state_in, norm_in)
    grad_direct, grad_state_in, grad_norm_in = attend_pull(cotan_local.astype(jnp.float32))
    backward_sum = chip_scan(
        pack_heads(grad_state_in, grad_norm_in, boundary), feats + 2, -1, reach
    )
    grad_state_loc, grad_norm_loc = unpack_heads(backward_sum, feats)
    (grad_carried,) = summary_pull((grad_state_loc, grad_norm_loc))
    grad_projected = (grad_direct + grad_carried).astype(jnp.bfloat16)
    edges = np.cumsum([0] + [part.shape[1] for part in parts])
    grad_input = sum(
        lax.dot_general(
            grad_projected[:, start:stop],
            part,
            (((1,), (1,)), ((), ())),
            preferred_element_type=jnp.float32,
        )
        for part, start, stop in zip(parts, edges[:-1], edges[1:])
    ).astype(jnp.bfloat16)
    grad_cols = lax.all_to_all(
        grad_projected.astype(jnp.float32), "seq", split_axis=1, concat_axis=0, tiled=True
    )
    pack_part = lax.dot_general(
        tokens_pack,
        grad_cols,
        (((0,), (0,)), ((), ())),
        precision=lax.Precision.HIGH,
        preferred_element_type=jnp.float32,
    )
    row_part = lax.psum_scatter(pack_part, "dp", scatter_dimension=0, tiled=True)
    grad_proj = lax.all_to_all(row_part, "seq", split_axis=0, concat_axis=1, tiled=True)
    return (output.astype(jnp.bfloat16)[None], grad_input[None], grad_proj)


def solution(mesh):
    return jax.shard_map(
        on_device,
        mesh=mesh,
        in_specs=(P("dp", "seq", None), P(), P(), P(), P("dp", "seq", None), P("dp", "seq")),
        out_specs=(P("dp", "seq", None), P("dp", "seq", None), P(("dp", "seq"), None)),
        check_vma=False,
    )
```

```python
import jax
import jax.numpy as jnp
import numpy as np
from jax import lax
from jax.sharding import PartitionSpec as P

HEADS = 16
FEAT = 16
HEAD_DIM = 128


highest = lax.Precision.HIGHEST


def pack_heads(state, norm, extra):
    heads, feats, lanes = state.shape
    rows = -(-(feats + 3) // 8) * 8
    norm_rows = jnp.pad(norm, ((0, 0), (0, 2 * lanes - feats))).reshape(heads, 2, lanes)
    extra_rows = jnp.broadcast_to(extra, (heads, 1, lanes)).astype(state.dtype)
    filler = jnp.zeros((heads, rows - feats - 3, lanes), state.dtype)
    return jnp.concatenate([state, norm_rows, extra_rows, filler], axis=1)


def unpack_heads(packed, feats):
    heads, _, lanes = packed.shape
    state = packed[:, :feats, :]
    norm = packed[:, feats : feats + 2, :].reshape(heads, 2 * lanes)[:, :feats]
    return state, norm


def shifted(value, steps):
    count = lax.axis_size("seq")
    if steps > 0:
        pairs = [(source, source + steps) for source in range(count - steps)]
    else:
        pairs = [(source, source + steps) for source in range(-steps, count)]
    return lax.ppermute(value, "seq", pairs)


def segmented_scan(packed, flag_row, direction, reach):
    carry = shifted(packed, direction)
    covered = 1
    while covered < reach:
        earlier = shifted(carry, direction * covered)
        carry = jnp.where(carry[0, flag_row, 0] > 0, carry, carry + earlier)
        covered *= 2
    return carry


def chip_scan(packed, flag_row, direction, reach):
    count = lax.axis_size("seq")
    if count % 2:
        return segmented_scan(packed, flag_row, direction, reach)
    chips = count // 2
    lead, other = (1, 0) if direction > 0 else (0, 1)

    def fold(near, far):
        return jnp.where(near[0, flag_row, 0] > 0, near, near + far)

    def chip_shift(value, distance):
        step = direction * distance
        pairs = [
            (2 * chip + lead, 2 * (chip + step) + lead)
            for chip in range(chips)
            if 0 <= chip + step < chips
        ]
        return lax.ppermute(value, "seq", pairs)

    partner = lax.ppermute(
        packed, "seq", [(2 * chip + other, 2 * chip + lead) for chip in range(chips)]
    )
    carry = chip_shift(fold(packed, partner), 1)
    chip_reach = min(chips - 1, -(-reach // 2))
    covered = 1
    while covered < chip_reach:
        carry = fold(carry, chip_shift(carry, covered))
        covered *= 2
    handed = lax.ppermute(
        carry, "seq", [(2 * chip + lead, 2 * chip + other) for chip in range(chips)]
    )
    core = lax.axis_index("seq") % 2
    return jnp.where(core == lead, fold(partner, carry), handed)


def taylor_table(feat_width):
    row_index, col_index = np.triu_indices(feat_width)
    taylor_map = np.zeros((feat_width * feat_width, len(row_index)), np.float32)
    taylor_map[row_index * feat_width + col_index, np.arange(len(row_index))] = np.where(
        row_index == col_index, 1.0 / np.sqrt(2.0), 1.0
    )
    return jnp.asarray(taylor_map)


def expand_features(vectors, taylor_map):
    lead_shape = vectors.shape[:-1]
    feat_width = vectors.shape[-1]
    outer_prod = (vectors[..., :, None] * vectors[..., None, :]).reshape(
        lead_shape + (feat_width * feat_width,)
    )
    square = jnp.einsum(
        "thp,pc->thc", outer_prod, taylor_map.astype(vectors.dtype), precision=highest
    )
    return jnp.concatenate([jnp.ones(lead_shape + (1,), vectors.dtype), vectors, square], axis=-1)


def block_forward(query_raw, key_raw, value_all, doc_local, prev_id, state_in, norm_in, taylor_map):
    length = query_raw.shape[0]
    queries = (0.5 * query_raw).reshape(length, HEADS, FEAT)
    key_feats = (0.5 * key_raw).reshape(length, HEADS, FEAT)
    values = value_all.reshape(length, HEADS, HEAD_DIM)
    scores = jnp.einsum("thf,shf->hts", queries, key_feats, precision=highest)
    kernel = 1.0 + scores + 0.5 * scores * scores
    positions = jnp.arange(length)
    allowed = (positions[:, None] >= positions[None, :]) & (
        doc_local[:, None] == doc_local[None, :]
    )
    kernel = jnp.where(allowed[None], kernel, 0.0)
    numerator = jnp.einsum("hts,shd->thd", kernel, values, precision=highest)
    denominator = jnp.sum(kernel, axis=2).T
    carried = (doc_local == prev_id).astype(kernel.dtype)[:, None]
    phi_query = expand_features(queries, taylor_map)
    numerator = numerator + carried[:, :, None] * jnp.einsum(
        "thf,hfd->thd", phi_query, state_in, precision=highest
    )
    denominator = denominator + carried * jnp.einsum(
        "thf,hf->th", phi_query, norm_in, precision=highest
    )
    return (numerator / denominator[:, :, None]).reshape(length, HEADS * HEAD_DIM)


def block_summary(key_raw, value_all, doc_local, taylor_map):
    length = key_raw.shape[0]
    key_feats = (0.5 * key_raw).reshape(length, HEADS, FEAT)
    values = value_all.reshape(length, HEADS, HEAD_DIM)
    phi_key = expand_features(key_feats, taylor_map)
    tail_mask = (doc_local == doc_local[-1]).astype(phi_key.dtype)[:, None, None]
    weighted = phi_key * tail_mask
    state_sum = jnp.einsum("thf,thd->hfd", weighted, values, precision=highest)
    norm_sum = jnp.sum(weighted, axis=0)
    return (state_sum, norm_sum)


def on_device(tokens, query_weight, key_weight, value_weight, cotangent, doc_ids):
    inputs = tokens[0]
    doc_local = doc_ids[0]
    cotan_local = cotangent[0]
    taylor_map = taylor_table(FEAT)
    width_qk = HEADS * FEAT
    parts = (query_weight, key_weight, value_weight)
    projected = lax.optimization_barrier(
        jnp.concatenate(
            [jnp.dot(inputs, part, preferred_element_type=jnp.float32) for part in parts], axis=1
        )
    )

    def summary(proj_in):
        return block_summary(
            proj_in[:, width_qk : 2 * width_qk], proj_in[:, 2 * width_qk :], doc_local, taylor_map
        )

    (state_loc, norm_loc), summary_pull = jax.vjp(summary, projected)
    feats = state_loc.shape[1]
    count, length = (lax.axis_size("seq"), doc_local.shape[0])
    longest = count * length // 2
    reach = min(count - 1, -(-(longest - 1) // length))
    prev_id = shifted(doc_local[-1:] + 1, 1)[0] - 1
    boundary = (doc_local[-1] != prev_id).astype(jnp.float32)
    forward_sum = chip_scan(pack_heads(state_loc, norm_loc, boundary), feats + 2, 1, reach)
    state_in, norm_in = unpack_heads(forward_sum, feats)
    tokens_wide = inputs.astype(jnp.float32)
    half = tokens_wide.shape[1] // 2
    tokens_first = lax.all_gather(tokens_wide[:, :half], "seq", axis=0, tiled=True)
    tokens_rest, state_in, norm_in = lax.optimization_barrier(
        (tokens_wide[:, half:], state_in, norm_in)
    )
    tokens_second = lax.all_gather(tokens_rest, "seq", axis=0, tiled=True)

    def attend(proj_in, state_sum, norm_sum):
        return block_forward(
            proj_in[:, :width_qk],
            proj_in[:, width_qk : 2 * width_qk],
            proj_in[:, 2 * width_qk :],
            doc_local,
            prev_id,
            state_sum,
            norm_sum,
            taylor_map,
        )

    output, attend_pull = jax.vjp(attend, projected, state_in, norm_in)
    grad_direct, grad_state_in, grad_norm_in = attend_pull(cotan_local.astype(jnp.float32))
    backward_sum = chip_scan(
        pack_heads(grad_state_in, grad_norm_in, boundary), feats + 2, -1, reach
    )
    grad_state_loc, grad_norm_loc = unpack_heads(backward_sum, feats)
    (grad_carried,) = summary_pull((grad_state_loc, grad_norm_loc))
    grad_projected = (grad_direct + grad_carried).astype(jnp.bfloat16)
    edges = np.cumsum([0] + [part.shape[1] for part in parts])
    grad_input = sum(
        lax.dot_general(
            grad_projected[:, start:stop],
            part,
            (((1,), (1,)), ((), ())),
            preferred_element_type=jnp.float32,
        )
        for part, start, stop in zip(parts, edges[:-1], edges[1:])
    ).astype(jnp.bfloat16)
    grad_cols = lax.all_to_all(
        grad_projected.astype(jnp.float32), "seq", split_axis=1, concat_axis=0, tiled=True
    )
    pack_part = jnp.concatenate(
        [
            lax.dot_general(
                tokens_half,
                grad_cols,
                (((0,), (0,)), ((), ())),
                precision=lax.Precision.HIGH,
                preferred_element_type=jnp.float32,
            )
            for tokens_half in (tokens_first, tokens_second)
        ],
        axis=0,
    )
    row_part = lax.psum_scatter(pack_part, "dp", scatter_dimension=0, tiled=True)
    grad_proj = lax.all_to_all(row_part, "seq", split_axis=0, concat_axis=1, tiled=True)
    return (output.astype(jnp.bfloat16)[None], grad_input[None], grad_proj)


def solution(mesh):
    return jax.shard_map(
        on_device,
        mesh=mesh,
        in_specs=(P("dp", "seq", None), P(), P(), P(), P("dp", "seq", None), P("dp", "seq")),
        out_specs=(P("dp", "seq", None), P("dp", "seq", None), P(("dp", "seq"), None)),
        check_vma=False,
    )
```

```python
import jax
import jax.numpy as jnp
import numpy as np
from jax import lax
from jax.sharding import PartitionSpec as P

HEADS = 16
FEAT = 16
HEAD_DIM = 128


highest = lax.Precision.HIGHEST


def pack_heads(state, norm, extra):
    heads, feats, lanes = state.shape
    rows = -(-(feats + 3) // 8) * 8
    norm_rows = jnp.pad(norm, ((0, 0), (0, 2 * lanes - feats))).reshape(heads, 2, lanes)
    extra_rows = jnp.broadcast_to(extra, (heads, 1, lanes)).astype(state.dtype)
    filler = jnp.zeros((heads, rows - feats - 3, lanes), state.dtype)
    return jnp.concatenate([state, norm_rows, extra_rows, filler], axis=1)


def unpack_heads(packed, feats):
    heads, _, lanes = packed.shape
    state = packed[:, :feats, :]
    norm = packed[:, feats : feats + 2, :].reshape(heads, 2 * lanes)[:, :feats]
    return state, norm


def shifted(value, steps):
    count = lax.axis_size("seq")
    if steps > 0:
        pairs = [(source, source + steps) for source in range(count - steps)]
    else:
        pairs = [(source, source + steps) for source in range(-steps, count)]
    return lax.ppermute(value, "seq", pairs)


def segmented_scan(packed, flag_row, direction, reach):
    carry = shifted(packed, direction)
    covered = 1
    while covered < reach:
        earlier = shifted(carry, direction * covered)
        carry = jnp.where(carry[0, flag_row, 0] > 0, carry, carry + earlier)
        covered *= 2
    return carry


def chip_scan(packed, flag_row, direction, reach):
    count = lax.axis_size("seq")
    if count % 2:
        return segmented_scan(packed, flag_row, direction, reach)
    chips = count // 2
    lead, other = (1, 0) if direction > 0 else (0, 1)

    def fold(near, far):
        return jnp.where(near[0, flag_row, 0] > 0, near, near + far)

    def chip_shift(value, distance):
        step = direction * distance
        pairs = [
            (2 * chip + lead, 2 * (chip + step) + lead)
            for chip in range(chips)
            if 0 <= chip + step < chips
        ]
        return lax.ppermute(value, "seq", pairs)

    partner = lax.ppermute(
        packed, "seq", [(2 * chip + other, 2 * chip + lead) for chip in range(chips)]
    )
    carry = chip_shift(fold(packed, partner), 1)
    chip_reach = min(chips - 1, -(-reach // 2))
    covered = 1
    while covered < chip_reach:
        carry = fold(carry, chip_shift(carry, covered))
        covered *= 2
    handed = lax.ppermute(
        carry, "seq", [(2 * chip + lead, 2 * chip + other) for chip in range(chips)]
    )
    core = lax.axis_index("seq") % 2
    return jnp.where(core == lead, fold(partner, carry), handed)


def taylor_table(feat_width):
    row_index, col_index = np.triu_indices(feat_width)
    taylor_map = np.zeros((feat_width * feat_width, len(row_index)), np.float32)
    taylor_map[row_index * feat_width + col_index, np.arange(len(row_index))] = np.where(
        row_index == col_index, 1.0 / np.sqrt(2.0), 1.0
    )
    return jnp.asarray(taylor_map)


def expand_features(vectors, taylor_map):
    lead_shape = vectors.shape[:-1]
    feat_width = vectors.shape[-1]
    outer_prod = (vectors[..., :, None] * vectors[..., None, :]).reshape(
        lead_shape + (feat_width * feat_width,)
    )
    square = jnp.einsum(
        "thp,pc->thc", outer_prod, taylor_map.astype(vectors.dtype), precision=highest
    )
    return jnp.concatenate([jnp.ones(lead_shape + (1,), vectors.dtype), vectors, square], axis=-1)


def block_forward(query_raw, key_raw, value_all, doc_local, prev_id, state_in, norm_in, taylor_map):
    length = query_raw.shape[0]
    queries = (0.5 * query_raw).reshape(length, HEADS, FEAT)
    key_feats = (0.5 * key_raw).reshape(length, HEADS, FEAT)
    values = value_all.reshape(length, HEADS, HEAD_DIM)
    scores = jnp.einsum("thf,shf->hts", queries, key_feats, precision=highest)
    kernel = 1.0 + scores + 0.5 * scores * scores
    positions = jnp.arange(length)
    allowed = (positions[:, None] >= positions[None, :]) & (
        doc_local[:, None] == doc_local[None, :]
    )
    kernel = jnp.where(allowed[None], kernel, 0.0)
    numerator = jnp.einsum("hts,shd->thd", kernel, values, precision=highest)
    denominator = jnp.sum(kernel, axis=2).T
    carried = (doc_local == prev_id).astype(kernel.dtype)[:, None]
    phi_query = expand_features(queries, taylor_map)
    numerator = numerator + carried[:, :, None] * jnp.einsum(
        "thf,hfd->thd", phi_query, state_in, precision=highest
    )
    denominator = denominator + carried * jnp.einsum(
        "thf,hf->th", phi_query, norm_in, precision=highest
    )
    return (numerator / denominator[:, :, None]).reshape(length, HEADS * HEAD_DIM)


def block_summary(key_raw, value_all, doc_local, taylor_map):
    length = key_raw.shape[0]
    key_feats = (0.5 * key_raw).reshape(length, HEADS, FEAT)
    values = value_all.reshape(length, HEADS, HEAD_DIM)
    phi_key = expand_features(key_feats, taylor_map)
    tail_mask = (doc_local == doc_local[-1]).astype(phi_key.dtype)[:, None, None]
    weighted = phi_key * tail_mask
    state_sum = jnp.einsum("thf,thd->hfd", weighted, values, precision=highest)
    norm_sum = jnp.sum(weighted, axis=0)
    return (state_sum, norm_sum)


def on_device(tokens, query_weight, key_weight, value_weight, cotangent, doc_ids):
    inputs = tokens[0]
    doc_local = doc_ids[0]
    cotan_local = cotangent[0]
    taylor_map = taylor_table(FEAT)
    width_qk = HEADS * FEAT
    parts = (query_weight, key_weight, value_weight)
    projected = lax.optimization_barrier(
        jnp.concatenate(
            [jnp.dot(inputs, part, preferred_element_type=jnp.float32) for part in parts], axis=1
        )
    )

    def summary(proj_in):
        return block_summary(
            proj_in[:, width_qk : 2 * width_qk], proj_in[:, 2 * width_qk :], doc_local, taylor_map
        )

    (state_loc, norm_loc), summary_pull = jax.vjp(summary, projected)
    feats = state_loc.shape[1]
    count, length = (lax.axis_size("seq"), doc_local.shape[0])
    longest = count * length // 2
    reach = min(count - 1, -(-(longest - 1) // length))
    prev_id = shifted(doc_local[-1:] + 1, 1)[0] - 1
    boundary = (doc_local[-1] != prev_id).astype(jnp.float32)
    forward_sum = chip_scan(pack_heads(state_loc, norm_loc, boundary), feats + 2, 1, reach)
    state_in, norm_in = unpack_heads(forward_sum, feats)
    tokens_pack = lax.all_gather(inputs.astype(jnp.float32), "seq", axis=0, tiled=True)

    def attend(proj_in, state_sum, norm_sum):
        return block_forward(
            proj_in[:, :width_qk],
            proj_in[:, width_qk : 2 * width_qk],
            proj_in[:, 2 * width_qk :],
            doc_local,
            prev_id,
            state_sum,
            norm_sum,
            taylor_map,
        )

    output, attend_pull = jax.vjp(attend, projected, state_in, norm_in)
    grad_direct, grad_state_in, grad_norm_in = attend_pull(cotan_local.astype(jnp.float32))
    backward_sum = chip_scan(
        pack_heads(grad_state_in, grad_norm_in, boundary), feats + 2, -1, reach
    )
    grad_state_loc, grad_norm_loc = unpack_heads(backward_sum, feats)
    (grad_carried,) = summary_pull((grad_state_loc, grad_norm_loc))
    grad_projected = (grad_direct + grad_carried).astype(jnp.bfloat16)
    edges = np.cumsum([0] + [part.shape[1] for part in parts])
    grad_input = sum(
        lax.dot_general(
            grad_projected[:, start:stop],
            part,
            (((1,), (1,)), ((), ())),
            preferred_element_type=jnp.float32,
        )
        for part, start, stop in zip(parts, edges[:-1], edges[1:])
    ).astype(jnp.bfloat16)
    grad_cols = lax.all_to_all(
        grad_projected.astype(jnp.float32), "seq", split_axis=1, concat_axis=0, tiled=True
    )
    pack_part = lax.dot_general(
        tokens_pack,
        grad_cols,
        (((0,), (0,)), ((), ())),
        precision=lax.Precision.HIGH,
        preferred_element_type=jnp.float32,
    )
    planes = lax.axis_size("dp")
    row_part = jnp.sum(
        lax.all_to_all(
            pack_part.reshape((planes, pack_part.shape[0] // planes) + pack_part.shape[1:]),
            "dp",
            0,
            0,
        ),
        axis=0,
    )
    grad_proj = lax.all_to_all(row_part, "seq", split_axis=0, concat_axis=1, tiled=True)
    return (output.astype(jnp.bfloat16)[None], grad_input[None], grad_proj)


def solution(mesh):
    return jax.shard_map(
        on_device,
        mesh=mesh,
        in_specs=(P("dp", "seq", None), P(), P(), P(), P("dp", "seq", None), P("dp", "seq")),
        out_specs=(P("dp", "seq", None), P("dp", "seq", None), P(("dp", "seq"), None)),
        check_vma=False,
    )
```

```python
import jax
import jax.numpy as jnp
import numpy as np
from jax import lax
from jax.sharding import PartitionSpec as P

HEADS = 16
FEAT = 16
HEAD_DIM = 128


highest = lax.Precision.HIGHEST


def pack_heads(state, norm, extra):
    heads, feats, lanes = state.shape
    rows = -(-(feats + 3) // 8) * 8
    norm_rows = jnp.pad(norm, ((0, 0), (0, 2 * lanes - feats))).reshape(heads, 2, lanes)
    extra_rows = jnp.broadcast_to(extra, (heads, 1, lanes)).astype(state.dtype)
    filler = jnp.zeros((heads, rows - feats - 3, lanes), state.dtype)
    return jnp.concatenate([state, norm_rows, extra_rows, filler], axis=1)


def unpack_heads(packed, feats):
    heads, _, lanes = packed.shape
    state = packed[:, :feats, :]
    norm = packed[:, feats : feats + 2, :].reshape(heads, 2 * lanes)[:, :feats]
    return state, norm


def shifted(value, steps):
    count = lax.axis_size("seq")
    if steps > 0:
        pairs = [(source, source + steps) for source in range(count - steps)]
    else:
        pairs = [(source, source + steps) for source in range(-steps, count)]
    return lax.ppermute(value, "seq", pairs)


def segmented_scan(packed, flag_row, direction, reach):
    carry = shifted(packed, direction)
    covered = 1
    while covered < reach:
        earlier = shifted(carry, direction * covered)
        carry = jnp.where(carry[0, flag_row, 0] > 0, carry, carry + earlier)
        covered *= 2
    return carry


def chip_scan(packed, flag_row, direction, reach):
    count = lax.axis_size("seq")
    if count % 2 or packed.shape[0] % 2:
        return segmented_scan(packed, flag_row, direction, reach)
    chips, split = (count // 2, packed.shape[0] // 2)
    lead = 1 if direction > 0 else 0
    core = lax.axis_index("seq") % 2
    swap = [(2 * chip + side, 2 * chip + 1 - side) for chip in range(chips) for side in (0, 1)]

    def fold(near, far):
        return jnp.where(near[0, flag_row, 0] > 0, near, near + far)

    def chip_shift(value, distance):
        step = direction * distance
        pairs = [
            (2 * chip + side, 2 * (chip + step) + side)
            for chip in range(chips)
            if 0 <= chip + step < chips
            for side in (0, 1)
        ]
        return lax.ppermute(value, "seq", pairs)

    low, high = (packed[:split], packed[split:])
    mine = jnp.where(core == 0, low, high)
    got = lax.ppermute(jnp.where(core == 0, high, low), "seq", swap)
    summary = jnp.where(core == lead, fold(mine, got), fold(got, mine))
    carry = chip_shift(summary, 1)
    chip_reach = min(chips - 1, -(-reach // 2))
    covered = 1
    while covered < chip_reach:
        carry = fold(carry, chip_shift(carry, covered))
        covered *= 2
    back = lax.ppermute(jnp.where(core == lead, carry, fold(mine, carry)), "seq", swap)
    kept = jnp.where(core == lead, fold(got, carry), carry)
    return jnp.where(
        core == 0, jnp.concatenate([kept, back], axis=0), jnp.concatenate([back, kept], axis=0)
    )


def taylor_table(feat_width):
    row_index, col_index = np.triu_indices(feat_width)
    taylor_map = np.zeros((feat_width * feat_width, len(row_index)), np.float32)
    taylor_map[row_index * feat_width + col_index, np.arange(len(row_index))] = np.where(
        row_index == col_index, 1.0 / np.sqrt(2.0), 1.0
    )
    return jnp.asarray(taylor_map)


def expand_features(vectors, taylor_map):
    lead_shape = vectors.shape[:-1]
    feat_width = vectors.shape[-1]
    outer_prod = (vectors[..., :, None] * vectors[..., None, :]).reshape(
        lead_shape + (feat_width * feat_width,)
    )
    square = jnp.einsum(
        "thp,pc->thc", outer_prod, taylor_map.astype(vectors.dtype), precision=highest
    )
    return jnp.concatenate([jnp.ones(lead_shape + (1,), vectors.dtype), vectors, square], axis=-1)


def block_forward(query_raw, key_raw, value_all, doc_local, prev_id, state_in, norm_in, taylor_map):
    length = query_raw.shape[0]
    queries = (0.5 * query_raw).reshape(length, HEADS, FEAT)
    key_feats = (0.5 * key_raw).reshape(length, HEADS, FEAT)
    values = value_all.reshape(length, HEADS, HEAD_DIM)
    scores = jnp.einsum("thf,shf->hts", queries, key_feats, precision=highest)
    kernel = 1.0 + scores + 0.5 * scores * scores
    positions = jnp.arange(length)
    allowed = (positions[:, None] >= positions[None, :]) & (
        doc_local[:, None] == doc_local[None, :]
    )
    kernel = jnp.where(allowed[None], kernel, 0.0)
    numerator = jnp.einsum("hts,shd->thd", kernel, values, precision=highest)
    denominator = jnp.sum(kernel, axis=2).T
    carried = (doc_local == prev_id).astype(kernel.dtype)[:, None]
    phi_query = expand_features(queries, taylor_map)
    numerator = numerator + carried[:, :, None] * jnp.einsum(
        "thf,hfd->thd", phi_query, state_in, precision=highest
    )
    denominator = denominator + carried * jnp.einsum(
        "thf,hf->th", phi_query, norm_in, precision=highest
    )
    return (numerator / denominator[:, :, None]).reshape(length, HEADS * HEAD_DIM)


def block_summary(key_raw, value_all, doc_local, taylor_map):
    length = key_raw.shape[0]
    key_feats = (0.5 * key_raw).reshape(length, HEADS, FEAT)
    values = value_all.reshape(length, HEADS, HEAD_DIM)
    phi_key = expand_features(key_feats, taylor_map)
    tail_mask = (doc_local == doc_local[-1]).astype(phi_key.dtype)[:, None, None]
    weighted = phi_key * tail_mask
    state_sum = jnp.einsum("thf,thd->hfd", weighted, values, precision=highest)
    norm_sum = jnp.sum(weighted, axis=0)
    return (state_sum, norm_sum)


def on_device(tokens, query_weight, key_weight, value_weight, cotangent, doc_ids):
    inputs = tokens[0]
    doc_local = doc_ids[0]
    cotan_local = cotangent[0]
    taylor_map = taylor_table(FEAT)
    width_qk = HEADS * FEAT
    parts = (query_weight, key_weight, value_weight)
    projected = lax.optimization_barrier(
        jnp.concatenate(
            [jnp.dot(inputs, part, preferred_element_type=jnp.float32) for part in parts], axis=1
        )
    )

    def summary(proj_in):
        return block_summary(
            proj_in[:, width_qk : 2 * width_qk], proj_in[:, 2 * width_qk :], doc_local, taylor_map
        )

    (state_loc, norm_loc), summary_pull = jax.vjp(summary, projected)
    feats = state_loc.shape[1]
    count, length = (lax.axis_size("seq"), doc_local.shape[0])
    longest = count * length // 2
    reach = min(count - 1, -(-(longest - 1) // length))
    prev_id = shifted(doc_local[-1:] + 1, 1)[0] - 1
    boundary = (doc_local[-1] != prev_id).astype(jnp.float32)
    forward_sum = chip_scan(pack_heads(state_loc, norm_loc, boundary), feats + 2, 1, reach)
    state_in, norm_in = unpack_heads(forward_sum, feats)
    tokens_pack = lax.all_gather(inputs.astype(jnp.float32), "seq", axis=0, tiled=True)

    def attend(proj_in, state_sum, norm_sum):
        return block_forward(
            proj_in[:, :width_qk],
            proj_in[:, width_qk : 2 * width_qk],
            proj_in[:, 2 * width_qk :],
            doc_local,
            prev_id,
            state_sum,
            norm_sum,
            taylor_map,
        )

    output, attend_pull = jax.vjp(attend, projected, state_in, norm_in)
    grad_direct, grad_state_in, grad_norm_in = attend_pull(cotan_local.astype(jnp.float32))
    backward_sum = chip_scan(
        pack_heads(grad_state_in, grad_norm_in, boundary), feats + 2, -1, reach
    )
    grad_state_loc, grad_norm_loc = unpack_heads(backward_sum, feats)
    (grad_carried,) = summary_pull((grad_state_loc, grad_norm_loc))
    grad_projected = (grad_direct + grad_carried).astype(jnp.bfloat16)
    edges = np.cumsum([0] + [part.shape[1] for part in parts])
    grad_input = sum(
        lax.dot_general(
            grad_projected[:, start:stop],
            part,
            (((1,), (1,)), ((), ())),
            preferred_element_type=jnp.float32,
        )
        for part, start, stop in zip(parts, edges[:-1], edges[1:])
    ).astype(jnp.bfloat16)
    grad_cols = lax.all_to_all(
        grad_projected.astype(jnp.float32), "seq", split_axis=1, concat_axis=0, tiled=True
    )
    pack_part = lax.dot_general(
        tokens_pack,
        grad_cols,
        (((0,), (0,)), ((), ())),
        precision=lax.Precision.HIGH,
        preferred_element_type=jnp.float32,
    )
    row_part = lax.psum_scatter(pack_part, "dp", scatter_dimension=0, tiled=True)
    grad_proj = lax.all_to_all(row_part, "seq", split_axis=0, concat_axis=1, tiled=True)
    return (output.astype(jnp.bfloat16)[None], grad_input[None], grad_proj)


def solution(mesh):
    return jax.shard_map(
        on_device,
        mesh=mesh,
        in_specs=(P("dp", "seq", None), P(), P(), P(), P("dp", "seq", None), P("dp", "seq")),
        out_specs=(P("dp", "seq", None), P("dp", "seq", None), P(("dp", "seq"), None)),
        check_vma=False,
    )
```

```python
import jax
import jax.numpy as jnp
import numpy as np
from jax import lax
from jax.sharding import PartitionSpec as P

HEADS = 16
FEAT = 16
HEAD_DIM = 128


highest = lax.Precision.HIGHEST


def pack_heads(state, norm, extra):
    heads, feats, lanes = state.shape
    rows = -(-(feats + 3) // 8) * 8
    norm_rows = jnp.pad(norm, ((0, 0), (0, 2 * lanes - feats))).reshape(heads, 2, lanes)
    extra_rows = jnp.broadcast_to(extra, (heads, 1, lanes)).astype(state.dtype)
    filler = jnp.zeros((heads, rows - feats - 3, lanes), state.dtype)
    return jnp.concatenate([state, norm_rows, extra_rows, filler], axis=1)


def unpack_heads(packed, feats):
    heads, _, lanes = packed.shape
    state = packed[:, :feats, :]
    norm = packed[:, feats : feats + 2, :].reshape(heads, 2 * lanes)[:, :feats]
    return state, norm


def shifted(value, steps):
    count = lax.axis_size("seq")
    if steps > 0:
        pairs = [(source, source + steps) for source in range(count - steps)]
    else:
        pairs = [(source, source + steps) for source in range(-steps, count)]
    return lax.ppermute(value, "seq", pairs)


def segmented_scan(packed, flag_row, direction, reach):
    carry = shifted(packed, direction)
    covered = 1
    while covered < reach:
        earlier = shifted(carry, direction * covered)
        carry = jnp.where(carry[0, flag_row, 0] > 0, carry, carry + earlier)
        covered *= 2
    return carry


def chip_scan(packed, flag_row, direction, reach):
    count = lax.axis_size("seq")
    if count % 2 or packed.shape[0] % 2:
        return segmented_scan(packed, flag_row, direction, reach)
    chips, split = (count // 2, packed.shape[0] // 2)
    lead = 1 if direction > 0 else 0
    core = lax.axis_index("seq") % 2
    swap = [(2 * chip + side, 2 * chip + 1 - side) for chip in range(chips) for side in (0, 1)]

    def fold(near, far):
        return jnp.where(near[0, flag_row, 0] > 0, near, near + far)

    def chip_shift(value, distance):
        step = direction * distance
        pairs = [
            (2 * chip + side, 2 * (chip + step) + side)
            for chip in range(chips)
            if 0 <= chip + step < chips
            for side in (0, 1)
        ]
        return lax.ppermute(value, "seq", pairs)

    low, high = (packed[:split], packed[split:])
    mine = jnp.where(core == 0, low, high)
    got = lax.ppermute(jnp.where(core == 0, high, low), "seq", swap)
    summary = jnp.where(core == lead, fold(mine, got), fold(got, mine))
    carry = chip_shift(summary, 1)
    chip_reach = min(chips - 1, -(-reach // 2))
    covered = 1
    while covered < chip_reach:
        carry = fold(carry, chip_shift(carry, covered))
        covered *= 2
    back = lax.ppermute(jnp.where(core == lead, carry, fold(mine, carry)), "seq", swap)
    kept = jnp.where(core == lead, fold(got, carry), carry)
    return jnp.where(
        core == 0, jnp.concatenate([kept, back], axis=0), jnp.concatenate([back, kept], axis=0)
    )


def taylor_table(feat_width):
    row_index, col_index = np.triu_indices(feat_width)
    taylor_map = np.zeros((feat_width * feat_width, len(row_index)), np.float32)
    taylor_map[row_index * feat_width + col_index, np.arange(len(row_index))] = np.where(
        row_index == col_index, 1.0 / np.sqrt(2.0), 1.0
    )
    return jnp.asarray(taylor_map)


def expand_features(vectors, taylor_map):
    lead_shape = vectors.shape[:-1]
    feat_width = vectors.shape[-1]
    outer_prod = (vectors[..., :, None] * vectors[..., None, :]).reshape(
        lead_shape + (feat_width * feat_width,)
    )
    square = jnp.einsum(
        "thp,pc->thc", outer_prod, taylor_map.astype(vectors.dtype), precision=highest
    )
    return jnp.concatenate([jnp.ones(lead_shape + (1,), vectors.dtype), vectors, square], axis=-1)


def block_forward(query_raw, key_raw, value_all, doc_local, prev_id, state_in, norm_in, taylor_map):
    length = query_raw.shape[0]
    queries = (0.5 * query_raw).reshape(length, HEADS, FEAT)
    key_feats = (0.5 * key_raw).reshape(length, HEADS, FEAT)
    values = value_all.reshape(length, HEADS, HEAD_DIM)
    scores = jnp.einsum("thf,shf->hts", queries, key_feats, precision=highest)
    kernel = 1.0 + scores + 0.5 * scores * scores
    positions = jnp.arange(length)
    allowed = (positions[:, None] >= positions[None, :]) & (
        doc_local[:, None] == doc_local[None, :]
    )
    kernel = jnp.where(allowed[None], kernel, 0.0)
    numerator = jnp.einsum("hts,shd->thd", kernel, values, precision=highest)
    denominator = jnp.sum(kernel, axis=2).T
    carried = (doc_local == prev_id).astype(kernel.dtype)[:, None]
    phi_query = expand_features(queries, taylor_map)
    numerator = numerator + carried[:, :, None] * jnp.einsum(
        "thf,hfd->thd", phi_query, state_in, precision=highest
    )
    denominator = denominator + carried * jnp.sum(phi_query * norm_in[None], axis=-1)
    return (numerator / denominator[:, :, None]).reshape(length, HEADS * HEAD_DIM)


def block_summary(key_raw, value_all, doc_local, taylor_map):
    length = key_raw.shape[0]
    key_feats = (0.5 * key_raw).reshape(length, HEADS, FEAT)
    values = value_all.reshape(length, HEADS, HEAD_DIM)
    phi_key = expand_features(key_feats, taylor_map)
    tail_mask = (doc_local == doc_local[-1]).astype(phi_key.dtype)[:, None, None]
    weighted = phi_key * tail_mask
    state_sum = jnp.einsum("thf,thd->hfd", weighted, values, precision=highest)
    norm_sum = jnp.sum(weighted, axis=0)
    return (state_sum, norm_sum)


def on_device(tokens, query_weight, key_weight, value_weight, cotangent, doc_ids):
    inputs = tokens[0]
    doc_local = doc_ids[0]
    cotan_local = cotangent[0]
    taylor_map = taylor_table(FEAT)
    width_qk = HEADS * FEAT
    parts = (query_weight, key_weight, value_weight)
    projected = lax.optimization_barrier(
        jnp.concatenate(
            [jnp.dot(inputs, part, preferred_element_type=jnp.float32) for part in parts], axis=1
        )
    )

    def summary(proj_in):
        return block_summary(
            proj_in[:, width_qk : 2 * width_qk], proj_in[:, 2 * width_qk :], doc_local, taylor_map
        )

    (state_loc, norm_loc), summary_pull = jax.vjp(summary, projected)
    feats = state_loc.shape[1]
    count, length = (lax.axis_size("seq"), doc_local.shape[0])
    longest = count * length // 2
    reach = min(count - 1, -(-(longest - 1) // length))
    prev_id = shifted(doc_local[-1:] + 1, 1)[0] - 1
    boundary = (doc_local[-1] != prev_id).astype(jnp.float32)
    forward_sum = chip_scan(pack_heads(state_loc, norm_loc, boundary), feats + 2, 1, reach)
    state_in, norm_in = unpack_heads(forward_sum, feats)
    tokens_pack = lax.all_gather(inputs.astype(jnp.float32), "seq", axis=0, tiled=True)

    def attend(proj_in, state_sum, norm_sum):
        return block_forward(
            proj_in[:, :width_qk],
            proj_in[:, width_qk : 2 * width_qk],
            proj_in[:, 2 * width_qk :],
            doc_local,
            prev_id,
            state_sum,
            norm_sum,
            taylor_map,
        )

    output, attend_pull = jax.vjp(attend, projected, state_in, norm_in)
    grad_direct, grad_state_in, grad_norm_in = attend_pull(cotan_local.astype(jnp.float32))
    backward_sum = chip_scan(
        pack_heads(grad_state_in, grad_norm_in, boundary), feats + 2, -1, reach
    )
    grad_state_loc, grad_norm_loc = unpack_heads(backward_sum, feats)
    (grad_carried,) = summary_pull((grad_state_loc, grad_norm_loc))
    grad_projected = (grad_direct + grad_carried).astype(jnp.bfloat16)
    edges = np.cumsum([0] + [part.shape[1] for part in parts])
    grad_input = sum(
        lax.dot_general(
            grad_projected[:, start:stop],
            part,
            (((1,), (1,)), ((), ())),
            preferred_element_type=jnp.float32,
        )
        for part, start, stop in zip(parts, edges[:-1], edges[1:])
    ).astype(jnp.bfloat16)
    grad_cols = lax.all_to_all(
        grad_projected.astype(jnp.float32), "seq", split_axis=1, concat_axis=0, tiled=True
    )
    pack_part = lax.dot_general(
        tokens_pack,
        grad_cols,
        (((0,), (0,)), ((), ())),
        precision=lax.Precision.HIGH,
        preferred_element_type=jnp.float32,
    )
    row_part = lax.psum_scatter(pack_part, "dp", scatter_dimension=0, tiled=True)
    grad_proj = lax.all_to_all(row_part, "seq", split_axis=0, concat_axis=1, tiled=True)
    return (output.astype(jnp.bfloat16)[None], grad_input[None], grad_proj)


def solution(mesh):
    return jax.shard_map(
        on_device,
        mesh=mesh,
        in_specs=(P("dp", "seq", None), P(), P(), P(), P("dp", "seq", None), P("dp", "seq")),
        out_specs=(P("dp", "seq", None), P("dp", "seq", None), P(("dp", "seq"), None)),
        check_vma=False,
    )
```

```python
import jax
import jax.numpy as jnp
import numpy as np
from jax import lax
from jax.sharding import PartitionSpec as P

HEADS = 16
FEAT = 16
HEAD_DIM = 128


highest = lax.Precision.HIGHEST


def pack_heads(state, norm, extra):
    heads, feats, lanes = state.shape
    rows = -(-(feats + 3) // 8) * 8
    norm_rows = jnp.pad(norm, ((0, 0), (0, 2 * lanes - feats))).reshape(heads, 2, lanes)
    extra_rows = jnp.broadcast_to(extra, (heads, 1, lanes)).astype(state.dtype)
    filler = jnp.zeros((heads, rows - feats - 3, lanes), state.dtype)
    return jnp.concatenate([state, norm_rows, extra_rows, filler], axis=1)


def unpack_heads(packed, feats):
    heads, _, lanes = packed.shape
    state = packed[:, :feats, :]
    norm = packed[:, feats : feats + 2, :].reshape(heads, 2 * lanes)[:, :feats]
    return state, norm


def shifted(value, steps):
    count = lax.axis_size("seq")
    if steps > 0:
        pairs = [(source, source + steps) for source in range(count - steps)]
    else:
        pairs = [(source, source + steps) for source in range(-steps, count)]
    return lax.ppermute(value, "seq", pairs)


def segmented_scan(packed, flag_row, direction, reach):
    carry = shifted(packed, direction)
    covered = 1
    while covered < reach:
        earlier = shifted(carry, direction * covered)
        carry = jnp.where(carry[0, flag_row, 0] > 0, carry, carry + earlier)
        covered *= 2
    return carry


def chip_scan(packed, flag_row, direction, reach):
    count = lax.axis_size("seq")
    if count % 2 or packed.shape[0] % 2:
        return segmented_scan(packed, flag_row, direction, reach)
    chips, split = (count // 2, packed.shape[0] // 2)
    lead = 1 if direction > 0 else 0
    core = lax.axis_index("seq") % 2
    swap = [(2 * chip + side, 2 * chip + 1 - side) for chip in range(chips) for side in (0, 1)]

    def fold(near, far):
        return jnp.where(near[0, flag_row, 0] > 0, near, near + far)

    def chip_shift(value, distance):
        step = direction * distance
        pairs = [
            (2 * chip + side, 2 * (chip + step) + side)
            for chip in range(chips)
            if 0 <= chip + step < chips
            for side in (0, 1)
        ]
        return lax.ppermute(value, "seq", pairs)

    low, high = (packed[:split], packed[split:])
    mine = jnp.where(core == 0, low, high)
    got = lax.ppermute(jnp.where(core == 0, high, low), "seq", swap)
    summary = jnp.where(core == lead, fold(mine, got), fold(got, mine))
    carry = chip_shift(summary, 1)
    chip_reach = min(chips - 1, -(-reach // 2))
    covered = 1
    while covered < chip_reach:
        carry = fold(carry, chip_shift(carry, covered))
        covered *= 2
    back = lax.ppermute(jnp.where(core == lead, carry, fold(mine, carry)), "seq", swap)
    kept = jnp.where(core == lead, fold(got, carry), carry)
    return jnp.where(
        core == 0, jnp.concatenate([kept, back], axis=0), jnp.concatenate([back, kept], axis=0)
    )


def taylor_table(feat_width):
    row_index, col_index = np.triu_indices(feat_width)
    taylor_map = np.zeros((feat_width * feat_width, len(row_index)), np.float32)
    taylor_map[row_index * feat_width + col_index, np.arange(len(row_index))] = np.where(
        row_index == col_index, 1.0 / np.sqrt(2.0), 1.0
    )
    return jnp.asarray(taylor_map)


def expand_features(vectors, taylor_map):
    lead_shape = vectors.shape[:-1]
    feat_width = vectors.shape[-1]
    outer_prod = (vectors[..., :, None] * vectors[..., None, :]).reshape(
        lead_shape + (feat_width * feat_width,)
    )
    square = jnp.einsum(
        "thp,pc->thc", outer_prod, taylor_map.astype(vectors.dtype), precision=highest
    )
    return jnp.concatenate([jnp.ones(lead_shape + (1,), vectors.dtype), vectors, square], axis=-1)


def block_forward(query_raw, key_raw, value_all, doc_local, prev_id, state_in, norm_in, taylor_map):
    length = query_raw.shape[0]
    queries = (0.5 * query_raw).reshape(length, HEADS, FEAT)
    key_feats = (0.5 * key_raw).reshape(length, HEADS, FEAT)
    values = value_all.reshape(length, HEADS, HEAD_DIM)
    scores = jnp.einsum("thf,shf->hts", queries, key_feats, precision=highest)
    kernel = 1.0 + scores + 0.5 * scores * scores
    positions = jnp.arange(length)
    allowed = (positions[:, None] >= positions[None, :]) & (
        doc_local[:, None] == doc_local[None, :]
    )
    kernel = jnp.where(allowed[None], kernel, 0.0)
    numerator = jnp.einsum("hts,shd->thd", kernel, values, precision=highest)
    denominator = jnp.sum(kernel, axis=2).T
    carried = (doc_local == prev_id).astype(kernel.dtype)[:, None]
    phi_query = expand_features(queries, taylor_map)
    numerator = numerator + carried[:, :, None] * jnp.einsum(
        "thf,hfd->thd", phi_query, state_in, precision=highest
    )
    denominator = denominator + carried * jnp.sum(phi_query * norm_in[None], axis=-1)
    return (numerator / denominator[:, :, None]).reshape(length, HEADS * HEAD_DIM)


def block_summary(key_raw, value_all, doc_local, taylor_map):
    length = key_raw.shape[0]
    key_feats = (0.5 * key_raw).reshape(length, HEADS, FEAT)
    values = value_all.reshape(length, HEADS, HEAD_DIM)
    phi_key = expand_features(key_feats, taylor_map)
    tail_mask = (doc_local == doc_local[-1]).astype(phi_key.dtype)[:, None, None]
    weighted = phi_key * tail_mask
    state_sum = jnp.einsum("thf,thd->hfd", weighted, values, precision=highest)
    norm_sum = jnp.sum(weighted, axis=0)
    return (state_sum, norm_sum)


def on_device(tokens, query_weight, key_weight, value_weight, cotangent, doc_ids):
    inputs = tokens[0]
    doc_local = doc_ids[0]
    cotan_local = cotangent[0]
    taylor_map = taylor_table(FEAT)
    width_qk = HEADS * FEAT
    parts = (query_weight, key_weight, value_weight)
    projected = lax.optimization_barrier(
        jnp.concatenate(
            [jnp.dot(inputs, part, preferred_element_type=jnp.float32) for part in parts], axis=1
        )
    )

    def summary(proj_in):
        return block_summary(
            proj_in[:, width_qk : 2 * width_qk], proj_in[:, 2 * width_qk :], doc_local, taylor_map
        )

    (state_loc, norm_loc), summary_pull = jax.vjp(summary, projected)
    feats = state_loc.shape[1]
    count, length = (lax.axis_size("seq"), doc_local.shape[0])
    longest = count * length // 2
    reach = min(count - 1, -(-(longest - 1) // length))
    prev_id = shifted(doc_local[-1:] + 1, 1)[0] - 1
    boundary = (doc_local[-1] != prev_id).astype(jnp.float32)
    forward_sum = chip_scan(pack_heads(state_loc, norm_loc, boundary), feats + 2, 1, reach)
    state_in, norm_in = unpack_heads(forward_sum, feats)
    tokens_pack = lax.all_gather(inputs.astype(jnp.float32), "seq", axis=0, tiled=True)

    def attend(proj_in, state_sum, norm_sum):
        return block_forward(
            proj_in[:, :width_qk],
            proj_in[:, width_qk : 2 * width_qk],
            proj_in[:, 2 * width_qk :],
            doc_local,
            prev_id,
            state_sum,
            norm_sum,
            taylor_map,
        )

    output, attend_pull = jax.vjp(attend, projected, state_in, norm_in)
    grad_direct, grad_state_in, grad_norm_in = attend_pull(cotan_local.astype(jnp.float32))
    backward_sum = chip_scan(
        pack_heads(grad_state_in, grad_norm_in, boundary), feats + 2, -1, reach
    )
    grad_state_loc, grad_norm_loc = unpack_heads(backward_sum, feats)
    (grad_carried,) = summary_pull((grad_state_loc, grad_norm_loc))
    grad_projected = (grad_direct + grad_carried).astype(jnp.bfloat16)
    edges = np.cumsum([0] + [part.shape[1] for part in parts])
    grad_input = sum(
        lax.dot_general(
            grad_projected[:, start:stop],
            part,
            (((1,), (1,)), ((), ())),
            preferred_element_type=jnp.float32,
        )
        for part, start, stop in zip(parts, edges[:-1], edges[1:])
    ).astype(jnp.bfloat16)
    grad_cols = lax.all_to_all(
        grad_projected.astype(jnp.float32), "seq", split_axis=1, concat_axis=0, tiled=True
    )
    pack_part = lax.dot_general(
        tokens_pack,
        grad_cols,
        (((0,), (0,)), ((), ())),
        precision=lax.Precision.HIGH,
        preferred_element_type=jnp.float32,
    )
    row_part = lax.psum_scatter(pack_part, "dp", scatter_dimension=0, tiled=True)
    row_part, grad_input = lax.optimization_barrier((row_part, grad_input))
    grad_proj = lax.all_to_all(row_part, "seq", split_axis=0, concat_axis=1, tiled=True)
    return (output.astype(jnp.bfloat16)[None], grad_input[None], grad_proj)


def solution(mesh):
    return jax.shard_map(
        on_device,
        mesh=mesh,
        in_specs=(P("dp", "seq", None), P(), P(), P(), P("dp", "seq", None), P("dp", "seq")),
        out_specs=(P("dp", "seq", None), P("dp", "seq", None), P(("dp", "seq"), None)),
        check_vma=False,
    )
```

```python
import jax
import jax.numpy as jnp
import numpy as np
from jax import lax
from jax.experimental import pallas as pl
from jax.sharding import PartitionSpec as P

HEADS = 16
FEAT = 16
HEAD_DIM = 128


highest = lax.Precision.HIGHEST


def pack_heads(state, norm, extra):
    heads, feats, lanes = state.shape
    rows = -(-(feats + 3) // 8) * 8
    norm_rows = jnp.pad(norm, ((0, 0), (0, 2 * lanes - feats))).reshape(heads, 2, lanes)
    extra_rows = jnp.broadcast_to(extra, (heads, 1, lanes)).astype(state.dtype)
    filler = jnp.zeros((heads, rows - feats - 3, lanes), state.dtype)
    return jnp.concatenate([state, norm_rows, extra_rows, filler], axis=1)


def unpack_heads(packed, feats):
    heads, _, lanes = packed.shape
    state = packed[:, :feats, :]
    norm = packed[:, feats : feats + 2, :].reshape(heads, 2 * lanes)[:, :feats]
    return state, norm


def shifted(value, steps):
    count = lax.axis_size("seq")
    if steps > 0:
        pairs = [(source, source + steps) for source in range(count - steps)]
    else:
        pairs = [(source, source + steps) for source in range(-steps, count)]
    return lax.ppermute(value, "seq", pairs)


def segmented_scan(packed, flag_row, direction, reach):
    carry = shifted(packed, direction)
    covered = 1
    while covered < reach:
        earlier = shifted(carry, direction * covered)
        carry = jnp.where(carry[0, flag_row, 0] > 0, carry, carry + earlier)
        covered *= 2
    return carry


def chip_scan(packed, flag_row, direction, reach):
    count = lax.axis_size("seq")
    if count % 2 or packed.shape[0] % 2:
        return segmented_scan(packed, flag_row, direction, reach)
    chips, split = (count // 2, packed.shape[0] // 2)
    lead = 1 if direction > 0 else 0
    core = lax.axis_index("seq") % 2
    swap = [(2 * chip + side, 2 * chip + 1 - side) for chip in range(chips) for side in (0, 1)]

    def fold(near, far):
        return jnp.where(near[0, flag_row, 0] > 0, near, near + far)

    def chip_shift(value, distance):
        step = direction * distance
        pairs = [
            (2 * chip + side, 2 * (chip + step) + side)
            for chip in range(chips)
            if 0 <= chip + step < chips
            for side in (0, 1)
        ]
        return lax.ppermute(value, "seq", pairs)

    low, high = (packed[:split], packed[split:])
    mine = jnp.where(core == 0, low, high)
    got = lax.ppermute(jnp.where(core == 0, high, low), "seq", swap)
    summary = jnp.where(core == lead, fold(mine, got), fold(got, mine))
    carry = chip_shift(summary, 1)
    chip_reach = min(chips - 1, -(-reach // 2))
    covered = 1
    while covered < chip_reach:
        carry = fold(carry, chip_shift(carry, covered))
        covered *= 2
    back = lax.ppermute(jnp.where(core == lead, carry, fold(mine, carry)), "seq", swap)
    kept = jnp.where(core == lead, fold(got, carry), carry)
    return jnp.where(
        core == 0, jnp.concatenate([kept, back], axis=0), jnp.concatenate([back, kept], axis=0)
    )


def narrow_block(wide_ref, narrow_ref):
    narrow_ref[...] = wide_ref[...].astype(narrow_ref.dtype)


def narrowed(wide):
    rows, cols = wide.shape
    block = 256 if rows % 256 == 0 else rows
    return pl.pallas_call(
        narrow_block,
        out_shape=jax.ShapeDtypeStruct(wide.shape, jnp.bfloat16),
        grid=(rows // block,),
        in_specs=[pl.BlockSpec((block, cols), lambda step: (step, 0))],
        out_specs=pl.BlockSpec((block, cols), lambda step: (step, 0)),
    )(wide)


def taylor_table(feat_width):
    row_index, col_index = np.triu_indices(feat_width)
    taylor_map = np.zeros((feat_width * feat_width, len(row_index)), np.float32)
    taylor_map[row_index * feat_width + col_index, np.arange(len(row_index))] = np.where(
        row_index == col_index, 1.0 / np.sqrt(2.0), 1.0
    )
    return jnp.asarray(taylor_map)


def expand_features(vectors, taylor_map):
    lead_shape = vectors.shape[:-1]
    feat_width = vectors.shape[-1]
    outer_prod = (vectors[..., :, None] * vectors[..., None, :]).reshape(
        lead_shape + (feat_width * feat_width,)
    )
    square = jnp.einsum(
        "thp,pc->thc", outer_prod, taylor_map.astype(vectors.dtype), precision=highest
    )
    return jnp.concatenate([jnp.ones(lead_shape + (1,), vectors.dtype), vectors, square], axis=-1)


def block_forward(query_raw, key_raw, value_all, doc_local, prev_id, state_in, norm_in, taylor_map):
    length = query_raw.shape[0]
    queries = (0.5 * query_raw).reshape(length, HEADS, FEAT)
    key_feats = (0.5 * key_raw).reshape(length, HEADS, FEAT)
    values = value_all.reshape(length, HEADS, HEAD_DIM)
    scores = jnp.einsum("thf,shf->hts", queries, key_feats, precision=highest)
    kernel = 1.0 + scores + 0.5 * scores * scores
    positions = jnp.arange(length)
    allowed = (positions[:, None] >= positions[None, :]) & (
        doc_local[:, None] == doc_local[None, :]
    )
    kernel = jnp.where(allowed[None], kernel, 0.0)
    numerator = jnp.einsum("hts,shd->thd", kernel, values, precision=highest)
    denominator = jnp.sum(kernel, axis=2).T
    carried = (doc_local == prev_id).astype(kernel.dtype)[:, None]
    phi_query = expand_features(queries, taylor_map)
    numerator = numerator + carried[:, :, None] * jnp.einsum(
        "thf,hfd->thd", phi_query, state_in, precision=highest
    )
    denominator = denominator + carried * jnp.sum(phi_query * norm_in[None], axis=-1)
    return (numerator / denominator[:, :, None]).reshape(length, HEADS * HEAD_DIM)


def block_summary(key_raw, value_all, doc_local, taylor_map):
    length = key_raw.shape[0]
    key_feats = (0.5 * key_raw).reshape(length, HEADS, FEAT)
    values = value_all.reshape(length, HEADS, HEAD_DIM)
    phi_key = expand_features(key_feats, taylor_map)
    tail_mask = (doc_local == doc_local[-1]).astype(phi_key.dtype)[:, None, None]
    weighted = phi_key * tail_mask
    state_sum = jnp.einsum("thf,thd->hfd", weighted, values, precision=highest)
    norm_sum = jnp.sum(weighted, axis=0)
    return (state_sum, norm_sum)


def on_device(tokens, query_weight, key_weight, value_weight, cotangent, doc_ids):
    inputs = tokens[0]
    doc_local = doc_ids[0]
    cotan_local = cotangent[0]
    taylor_map = taylor_table(FEAT)
    width_qk = HEADS * FEAT
    parts = (query_weight, key_weight, value_weight)
    projected = lax.optimization_barrier(
        jnp.concatenate(
            [jnp.dot(inputs, part, preferred_element_type=jnp.float32) for part in parts], axis=1
        )
    )

    def summary(proj_in):
        return block_summary(
            proj_in[:, width_qk : 2 * width_qk], proj_in[:, 2 * width_qk :], doc_local, taylor_map
        )

    (state_loc, norm_loc), summary_pull = jax.vjp(summary, projected)
    feats = state_loc.shape[1]
    count, length = (lax.axis_size("seq"), doc_local.shape[0])
    longest = count * length // 2
    reach = min(count - 1, -(-(longest - 1) // length))
    prev_id = shifted(doc_local[-1:] + 1, 1)[0] - 1
    boundary = (doc_local[-1] != prev_id).astype(jnp.float32)
    forward_sum = chip_scan(pack_heads(state_loc, norm_loc, boundary), feats + 2, 1, reach)
    state_in, norm_in = unpack_heads(forward_sum, feats)
    tokens_pack = lax.all_gather(inputs.astype(jnp.float32), "seq", axis=0, tiled=True)

    def attend(proj_in, state_sum, norm_sum):
        return block_forward(
            proj_in[:, :width_qk],
            proj_in[:, width_qk : 2 * width_qk],
            proj_in[:, 2 * width_qk :],
            doc_local,
            prev_id,
            state_sum,
            norm_sum,
            taylor_map,
        )

    output, attend_pull = jax.vjp(attend, projected, state_in, norm_in)
    grad_direct, grad_state_in, grad_norm_in = attend_pull(cotan_local.astype(jnp.float32))
    backward_sum = chip_scan(
        pack_heads(grad_state_in, grad_norm_in, boundary), feats + 2, -1, reach
    )
    grad_state_loc, grad_norm_loc = unpack_heads(backward_sum, feats)
    (grad_carried,) = summary_pull((grad_state_loc, grad_norm_loc))
    grad_projected = (grad_direct + grad_carried).astype(jnp.bfloat16)
    edges = np.cumsum([0] + [part.shape[1] for part in parts])
    grad_input = sum(
        lax.dot_general(
            grad_projected[:, start:stop],
            part,
            (((1,), (1,)), ((), ())),
            preferred_element_type=jnp.float32,
        )
        for part, start, stop in zip(parts, edges[:-1], edges[1:])
    ).astype(jnp.bfloat16)
    grad_cols = lax.all_to_all(
        grad_projected.astype(jnp.float32), "seq", split_axis=1, concat_axis=0, tiled=True
    )
    pack_part = lax.dot_general(
        narrowed(tokens_pack),
        narrowed(grad_cols),
        (((0,), (0,)), ((), ())),
        preferred_element_type=jnp.float32,
    )
    row_part = lax.psum_scatter(pack_part, "dp", scatter_dimension=0, tiled=True)
    row_part, grad_input = lax.optimization_barrier((row_part, grad_input))
    grad_proj = lax.all_to_all(row_part, "seq", split_axis=0, concat_axis=1, tiled=True)
    return (output.astype(jnp.bfloat16)[None], grad_input[None], grad_proj)


def solution(mesh):
    return jax.shard_map(
        on_device,
        mesh=mesh,
        in_specs=(P("dp", "seq", None), P(), P(), P(), P("dp", "seq", None), P("dp", "seq")),
        out_specs=(P("dp", "seq", None), P("dp", "seq", None), P(("dp", "seq"), None)),
        check_vma=False,
    )
```

```python
import jax
import jax.numpy as jnp
import numpy as np
from jax import lax
from jax.sharding import PartitionSpec as P

HEADS = 16
FEAT = 16
HEAD_DIM = 128


highest = lax.Precision.HIGHEST


def pack_heads(state, norm, extra):
    heads, feats, lanes = state.shape
    rows = -(-(feats + 3) // 8) * 8
    norm_rows = jnp.pad(norm, ((0, 0), (0, 2 * lanes - feats))).reshape(heads, 2, lanes)
    extra_rows = jnp.broadcast_to(extra, (heads, 1, lanes)).astype(state.dtype)
    filler = jnp.zeros((heads, rows - feats - 3, lanes), state.dtype)
    return jnp.concatenate([state, norm_rows, extra_rows, filler], axis=1)


def unpack_heads(packed, feats):
    heads, _, lanes = packed.shape
    state = packed[:, :feats, :]
    norm = packed[:, feats : feats + 2, :].reshape(heads, 2 * lanes)[:, :feats]
    return state, norm


def shifted(value, steps):
    count = lax.axis_size("seq")
    if steps > 0:
        pairs = [(source, source + steps) for source in range(count - steps)]
    else:
        pairs = [(source, source + steps) for source in range(-steps, count)]
    return lax.ppermute(value, "seq", pairs)


def segmented_scan(packed, flag_row, direction, reach):
    carry = shifted(packed, direction)
    covered = 1
    while covered < reach:
        earlier = shifted(carry, direction * covered)
        carry = jnp.where(carry[0, flag_row, 0] > 0, carry, carry + earlier)
        covered *= 2
    return carry


def chip_scan(packed, flag_row, direction, reach):
    count = lax.axis_size("seq")
    if count % 2 or packed.shape[0] % 2:
        return segmented_scan(packed, flag_row, direction, reach)
    chips, split = (count // 2, packed.shape[0] // 2)
    lead = 1 if direction > 0 else 0
    core = lax.axis_index("seq") % 2
    swap = [(2 * chip + side, 2 * chip + 1 - side) for chip in range(chips) for side in (0, 1)]

    def fold(near, far):
        return jnp.where(near[0, flag_row, 0] > 0, near, near + far)

    def chip_shift(value, distance):
        step = direction * distance
        pairs = [
            (2 * chip + side, 2 * (chip + step) + side)
            for chip in range(chips)
            if 0 <= chip + step < chips
            for side in (0, 1)
        ]
        return lax.ppermute(value, "seq", pairs)

    low, high = (packed[:split], packed[split:])
    mine = jnp.where(core == 0, low, high)
    got = lax.ppermute(jnp.where(core == 0, high, low), "seq", swap)
    summary = jnp.where(core == lead, fold(mine, got), fold(got, mine))
    carry = chip_shift(summary, 1)
    chip_reach = min(chips - 1, -(-reach // 2))
    covered = 1
    if chip_reach > 1:
        carry = fold(carry, chip_shift(summary, 2))
        covered = 2
    while covered < chip_reach:
        carry = fold(carry, chip_shift(carry, covered))
        covered *= 2
    back = lax.ppermute(jnp.where(core == lead, carry, fold(mine, carry)), "seq", swap)
    kept = jnp.where(core == lead, fold(got, carry), carry)
    return jnp.where(
        core == 0, jnp.concatenate([kept, back], axis=0), jnp.concatenate([back, kept], axis=0)
    )


def taylor_table(feat_width):
    row_index, col_index = np.triu_indices(feat_width)
    taylor_map = np.zeros((feat_width * feat_width, len(row_index)), np.float32)
    taylor_map[row_index * feat_width + col_index, np.arange(len(row_index))] = np.where(
        row_index == col_index, 1.0 / np.sqrt(2.0), 1.0
    )
    return jnp.asarray(taylor_map)


def expand_features(vectors, taylor_map):
    lead_shape = vectors.shape[:-1]
    feat_width = vectors.shape[-1]
    outer_prod = (vectors[..., :, None] * vectors[..., None, :]).reshape(
        lead_shape + (feat_width * feat_width,)
    )
    square = jnp.einsum(
        "thp,pc->thc", outer_prod, taylor_map.astype(vectors.dtype), precision=highest
    )
    return jnp.concatenate([jnp.ones(lead_shape + (1,), vectors.dtype), vectors, square], axis=-1)


def block_forward(query_raw, key_raw, value_all, doc_local, prev_id, state_in, norm_in, taylor_map):
    length = query_raw.shape[0]
    queries = (0.5 * query_raw).reshape(length, HEADS, FEAT)
    key_feats = (0.5 * key_raw).reshape(length, HEADS, FEAT)
    values = value_all.reshape(length, HEADS, HEAD_DIM)
    scores = jnp.einsum("thf,shf->hts", queries, key_feats, precision=highest)
    kernel = 1.0 + scores + 0.5 * scores * scores
    positions = jnp.arange(length)
    allowed = (positions[:, None] >= positions[None, :]) & (
        doc_local[:, None] == doc_local[None, :]
    )
    kernel = jnp.where(allowed[None], kernel, 0.0)
    numerator = jnp.einsum("hts,shd->thd", kernel, values, precision=highest)
    denominator = jnp.sum(kernel, axis=2).T
    carried = (doc_local == prev_id).astype(kernel.dtype)[:, None]
    phi_query = expand_features(queries, taylor_map)
    numerator = numerator + carried[:, :, None] * jnp.einsum(
        "thf,hfd->thd", phi_query, state_in, precision=highest
    )
    denominator = denominator + carried * jnp.sum(phi_query * norm_in[None], axis=-1)
    return (numerator / denominator[:, :, None]).reshape(length, HEADS * HEAD_DIM)


def block_summary(key_raw, value_all, doc_local, taylor_map):
    length = key_raw.shape[0]
    key_feats = (0.5 * key_raw).reshape(length, HEADS, FEAT)
    values = value_all.reshape(length, HEADS, HEAD_DIM)
    phi_key = expand_features(key_feats, taylor_map)
    tail_mask = (doc_local == doc_local[-1]).astype(phi_key.dtype)[:, None, None]
    weighted = phi_key * tail_mask
    state_sum = jnp.einsum("thf,thd->hfd", weighted, values, precision=highest)
    norm_sum = jnp.sum(weighted, axis=0)
    return (state_sum, norm_sum)


def on_device(tokens, query_weight, key_weight, value_weight, cotangent, doc_ids):
    inputs = tokens[0]
    doc_local = doc_ids[0]
    cotan_local = cotangent[0]
    taylor_map = taylor_table(FEAT)
    width_qk = HEADS * FEAT
    parts = (query_weight, key_weight, value_weight)
    projected = lax.optimization_barrier(
        jnp.concatenate(
            [jnp.dot(inputs, part, preferred_element_type=jnp.float32) for part in parts], axis=1
        )
    )

    def summary(proj_in):
        return block_summary(
            proj_in[:, width_qk : 2 * width_qk], proj_in[:, 2 * width_qk :], doc_local, taylor_map
        )

    (state_loc, norm_loc), summary_pull = jax.vjp(summary, projected)
    feats = state_loc.shape[1]
    count, length = (lax.axis_size("seq"), doc_local.shape[0])
    longest = count * length // 2
    reach = min(count - 1, -(-(longest - 1) // length))
    prev_id = shifted(doc_local[-1:] + 1, 1)[0] - 1
    boundary = (doc_local[-1] != prev_id).astype(jnp.float32)
    forward_sum = chip_scan(pack_heads(state_loc, norm_loc, boundary), feats + 2, 1, reach)
    state_in, norm_in = unpack_heads(forward_sum, feats)
    tokens_pack = lax.all_gather(inputs.astype(jnp.float32), "seq", axis=0, tiled=True)

    def attend(proj_in, state_sum, norm_sum):
        return block_forward(
            proj_in[:, :width_qk],
            proj_in[:, width_qk : 2 * width_qk],
            proj_in[:, 2 * width_qk :],
            doc_local,
            prev_id,
            state_sum,
            norm_sum,
            taylor_map,
        )

    output, attend_pull = jax.vjp(attend, projected, state_in, norm_in)
    grad_direct, grad_state_in, grad_norm_in = attend_pull(cotan_local.astype(jnp.float32))
    backward_sum = chip_scan(
        pack_heads(grad_state_in, grad_norm_in, boundary), feats + 2, -1, reach
    )
    grad_state_loc, grad_norm_loc = unpack_heads(backward_sum, feats)
    (grad_carried,) = summary_pull((grad_state_loc, grad_norm_loc))
    grad_projected = (grad_direct + grad_carried).astype(jnp.bfloat16)
    edges = np.cumsum([0] + [part.shape[1] for part in parts])
    grad_input = sum(
        lax.dot_general(
            grad_projected[:, start:stop],
            part,
            (((1,), (1,)), ((), ())),
            preferred_element_type=jnp.float32,
        )
        for part, start, stop in zip(parts, edges[:-1], edges[1:])
    ).astype(jnp.bfloat16)
    grad_cols = lax.all_to_all(
        grad_projected.astype(jnp.float32), "seq", split_axis=1, concat_axis=0, tiled=True
    )
    pack_part = lax.dot_general(
        tokens_pack,
        grad_cols,
        (((0,), (0,)), ((), ())),
        precision=lax.Precision.HIGH,
        preferred_element_type=jnp.float32,
    )
    row_part = lax.psum_scatter(pack_part, "dp", scatter_dimension=0, tiled=True)
    row_part, grad_input = lax.optimization_barrier((row_part, grad_input))
    grad_proj = lax.all_to_all(row_part, "seq", split_axis=0, concat_axis=1, tiled=True)
    return (output.astype(jnp.bfloat16)[None], grad_input[None], grad_proj)


def solution(mesh):
    return jax.shard_map(
        on_device,
        mesh=mesh,
        in_specs=(P("dp", "seq", None), P(), P(), P(), P("dp", "seq", None), P("dp", "seq")),
        out_specs=(P("dp", "seq", None), P("dp", "seq", None), P(("dp", "seq"), None)),
        check_vma=False,
    )
```

```python
import jax
import jax.numpy as jnp
import numpy as np
from jax import lax
from jax.sharding import PartitionSpec as P

HEADS = 16
FEAT = 16
HEAD_DIM = 128


highest = lax.Precision.HIGHEST


def pack_heads(state, norm, extra):
    heads, feats, lanes = state.shape
    rows = -(-(feats + 3) // 8) * 8
    norm_rows = jnp.pad(norm, ((0, 0), (0, 2 * lanes - feats))).reshape(heads, 2, lanes)
    extra_rows = jnp.broadcast_to(extra, (heads, 1, lanes)).astype(state.dtype)
    filler = jnp.zeros((heads, rows - feats - 3, lanes), state.dtype)
    return jnp.concatenate([state, norm_rows, extra_rows, filler], axis=1)


def unpack_heads(packed, feats):
    heads, _, lanes = packed.shape
    state = packed[:, :feats, :]
    norm = packed[:, feats : feats + 2, :].reshape(heads, 2 * lanes)[:, :feats]
    return state, norm


def shifted(value, steps):
    count = lax.axis_size("seq")
    if steps > 0:
        pairs = [(source, source + steps) for source in range(count - steps)]
    else:
        pairs = [(source, source + steps) for source in range(-steps, count)]
    return lax.ppermute(value, "seq", pairs)


def segmented_scan(packed, flag_row, direction, reach):
    carry = shifted(packed, direction)
    covered = 1
    while covered < reach:
        earlier = shifted(carry, direction * covered)
        carry = jnp.where(carry[0, flag_row, 0] > 0, carry, carry + earlier)
        covered *= 2
    return carry


def chip_scan(packed, flag_row, direction, reach):
    count = lax.axis_size("seq")
    if count % 2 or packed.shape[0] % 2:
        return segmented_scan(packed, flag_row, direction, reach)
    chips, split = (count // 2, packed.shape[0] // 2)
    lead = 1 if direction > 0 else 0
    core = lax.axis_index("seq") % 2
    swap = [(2 * chip + side, 2 * chip + 1 - side) for chip in range(chips) for side in (0, 1)]

    def fold(near, far):
        return jnp.where(near[0, flag_row, 0] > 0, near, near + far)

    def chip_shift(value, distance):
        step = direction * distance
        pairs = [
            (2 * chip + side, 2 * (chip + step) + side)
            for chip in range(chips)
            if 0 <= chip + step < chips
            for side in (0, 1)
        ]
        return lax.ppermute(value, "seq", pairs)

    low, high = (packed[:split], packed[split:])
    mine = jnp.where(core == 0, low, high)
    got = lax.ppermute(jnp.where(core == 0, high, low), "seq", swap)
    summary = jnp.where(core == lead, fold(mine, got), fold(got, mine))
    carry = chip_shift(summary, 1)
    chip_reach = min(chips - 1, -(-reach // 2))
    covered = 1
    if chip_reach > 1:
        carry = fold(carry, chip_shift(summary, 2))
        covered = 2
    while covered < chip_reach:
        carry = fold(carry, chip_shift(carry, covered))
        covered *= 2
    back = lax.ppermute(jnp.where(core == lead, carry, fold(mine, carry)), "seq", swap)
    kept = jnp.where(core == lead, fold(got, carry), carry)
    return jnp.where(
        core == 0, jnp.concatenate([kept, back], axis=0), jnp.concatenate([back, kept], axis=0)
    )


def taylor_table(feat_width):
    row_index, col_index = np.triu_indices(feat_width)
    taylor_map = np.zeros((feat_width * feat_width, len(row_index)), np.float32)
    taylor_map[row_index * feat_width + col_index, np.arange(len(row_index))] = np.where(
        row_index == col_index, 1.0 / np.sqrt(2.0), 1.0
    )
    return jnp.asarray(taylor_map)


def expand_features(vectors, taylor_map):
    lead_shape = vectors.shape[:-1]
    feat_width = vectors.shape[-1]
    outer_prod = (vectors[..., :, None] * vectors[..., None, :]).reshape(
        lead_shape + (feat_width * feat_width,)
    )
    square = jnp.einsum(
        "thp,pc->thc", outer_prod, taylor_map.astype(vectors.dtype), precision=highest
    )
    return jnp.concatenate([jnp.ones(lead_shape + (1,), vectors.dtype), vectors, square], axis=-1)


def block_forward(query_raw, key_raw, value_all, doc_local, prev_id, state_in, norm_in, taylor_map):
    length = query_raw.shape[0]
    queries = (0.5 * query_raw).reshape(length, HEADS, FEAT)
    key_feats = (0.5 * key_raw).reshape(length, HEADS, FEAT)
    values = value_all.reshape(length, HEADS, HEAD_DIM)
    scores = jnp.einsum("thf,shf->hts", queries, key_feats, precision=highest)
    kernel = 1.0 + scores + 0.5 * scores * scores
    positions = jnp.arange(length)
    allowed = (positions[:, None] >= positions[None, :]) & (
        doc_local[:, None] == doc_local[None, :]
    )
    kernel = jnp.where(allowed[None], kernel, 0.0)
    numerator = jnp.einsum("hts,shd->thd", kernel, values, precision=highest)
    denominator = jnp.sum(kernel, axis=2).T
    carried = (doc_local == prev_id).astype(kernel.dtype)[:, None]
    phi_query = expand_features(queries, taylor_map)
    numerator = numerator + carried[:, :, None] * jnp.einsum(
        "thf,hfd->thd", phi_query, state_in, precision=highest
    )
    denominator = denominator + carried * jnp.sum(phi_query * norm_in[None], axis=-1)
    return (numerator / denominator[:, :, None]).reshape(length, HEADS * HEAD_DIM)


def block_summary(key_raw, value_all, doc_local, taylor_map):
    length = key_raw.shape[0]
    key_feats = (0.5 * key_raw).reshape(length, HEADS, FEAT)
    values = value_all.reshape(length, HEADS, HEAD_DIM)
    phi_key = expand_features(key_feats, taylor_map)
    tail_mask = (doc_local == doc_local[-1]).astype(phi_key.dtype)[:, None, None]
    weighted = phi_key * tail_mask
    state_sum = jnp.einsum("thf,thd->hfd", weighted, values, precision=highest)
    norm_sum = jnp.sum(weighted, axis=0)
    return (state_sum, norm_sum)


def on_device(tokens, query_weight, key_weight, value_weight, cotangent, doc_ids):
    inputs = tokens[0]
    doc_local = doc_ids[0]
    cotan_local = cotangent[0]
    taylor_map = taylor_table(FEAT)
    width_qk = HEADS * FEAT
    parts = (query_weight, key_weight, value_weight)
    projected = lax.optimization_barrier(
        jnp.concatenate(
            [jnp.dot(inputs, part, preferred_element_type=jnp.float32) for part in parts], axis=1
        )
    )

    def summary(proj_in):
        return block_summary(
            proj_in[:, width_qk : 2 * width_qk], proj_in[:, 2 * width_qk :], doc_local, taylor_map
        )

    (state_loc, norm_loc), summary_pull = jax.vjp(summary, projected)
    feats = state_loc.shape[1]
    count, length = (lax.axis_size("seq"), doc_local.shape[0])
    longest = count * length // 2
    reach = min(count - 1, -(-(longest - 1) // length))
    prev_id = shifted(doc_local[-1:] + 1, 1)[0] - 1
    boundary = (doc_local[-1] != prev_id).astype(jnp.float32)
    forward_sum = chip_scan(pack_heads(state_loc, norm_loc, boundary), feats + 2, 1, reach)
    state_in, norm_in = unpack_heads(forward_sum, feats)
    tokens_wide, state_in, norm_in = lax.optimization_barrier(
        (inputs.astype(jnp.float32), state_in, norm_in)
    )
    tokens_pack = lax.all_gather(tokens_wide, "seq", axis=0, tiled=True)

    def attend(proj_in, state_sum, norm_sum):
        return block_forward(
            proj_in[:, :width_qk],
            proj_in[:, width_qk : 2 * width_qk],
            proj_in[:, 2 * width_qk :],
            doc_local,
            prev_id,
            state_sum,
            norm_sum,
            taylor_map,
        )

    output, attend_pull = jax.vjp(attend, projected, state_in, norm_in)
    grad_direct, grad_state_in, grad_norm_in = attend_pull(cotan_local.astype(jnp.float32))
    backward_sum = chip_scan(
        pack_heads(grad_state_in, grad_norm_in, boundary), feats + 2, -1, reach
    )
    grad_state_loc, grad_norm_loc = unpack_heads(backward_sum, feats)
    (grad_carried,) = summary_pull((grad_state_loc, grad_norm_loc))
    grad_projected = (grad_direct + grad_carried).astype(jnp.bfloat16)
    edges = np.cumsum([0] + [part.shape[1] for part in parts])
    grad_input = sum(
        lax.dot_general(
            grad_projected[:, start:stop],
            part,
            (((1,), (1,)), ((), ())),
            preferred_element_type=jnp.float32,
        )
        for part, start, stop in zip(parts, edges[:-1], edges[1:])
    ).astype(jnp.bfloat16)
    grad_cols = lax.all_to_all(
        grad_projected.astype(jnp.float32), "seq", split_axis=1, concat_axis=0, tiled=True
    )
    pack_part = lax.dot_general(
        tokens_pack,
        grad_cols,
        (((0,), (0,)), ((), ())),
        precision=lax.Precision.HIGH,
        preferred_element_type=jnp.float32,
    )
    row_part = lax.psum_scatter(pack_part, "dp", scatter_dimension=0, tiled=True)
    row_part, grad_input = lax.optimization_barrier((row_part, grad_input))
    grad_proj = lax.all_to_all(row_part, "seq", split_axis=0, concat_axis=1, tiled=True)
    return (output.astype(jnp.bfloat16)[None], grad_input[None], grad_proj)


def solution(mesh):
    return jax.shard_map(
        on_device,
        mesh=mesh,
        in_specs=(P("dp", "seq", None), P(), P(), P(), P("dp", "seq", None), P("dp", "seq")),
        out_specs=(P("dp", "seq", None), P("dp", "seq", None), P(("dp", "seq"), None)),
        check_vma=False,
    )
```

```python
import jax
import jax.numpy as jnp
import numpy as np
from jax import lax
from jax.sharding import PartitionSpec as P

HEADS = 16
FEAT = 16
HEAD_DIM = 128


highest = lax.Precision.HIGHEST


def pack_heads(state, norm, extra):
    heads, feats, lanes = state.shape
    rows = -(-(feats + 3) // 8) * 8
    norm_rows = jnp.pad(norm, ((0, 0), (0, 2 * lanes - feats))).reshape(heads, 2, lanes)
    extra_rows = jnp.broadcast_to(extra, (heads, 1, lanes)).astype(state.dtype)
    filler = jnp.zeros((heads, rows - feats - 3, lanes), state.dtype)
    return jnp.concatenate([state, norm_rows, extra_rows, filler], axis=1)


def unpack_heads(packed, feats):
    heads, _, lanes = packed.shape
    state = packed[:, :feats, :]
    norm = packed[:, feats : feats + 2, :].reshape(heads, 2 * lanes)[:, :feats]
    return state, norm


def shifted(value, steps):
    count = lax.axis_size("seq")
    if steps > 0:
        pairs = [(source, source + steps) for source in range(count - steps)]
    else:
        pairs = [(source, source + steps) for source in range(-steps, count)]
    return lax.ppermute(value, "seq", pairs)


def segmented_scan(packed, flag_row, direction, reach):
    carry = shifted(packed, direction)
    covered = 1
    while covered < reach:
        earlier = shifted(carry, direction * covered)
        carry = jnp.where(carry[0, flag_row, 0] > 0, carry, carry + earlier)
        covered *= 2
    return carry


def chip_scan(packed, flag_row, direction, reach):
    count = lax.axis_size("seq")
    if count % 2 or packed.shape[0] % 2:
        return segmented_scan(packed, flag_row, direction, reach)
    chips, split = (count // 2, packed.shape[0] // 2)
    lead = 1 if direction > 0 else 0
    core = lax.axis_index("seq") % 2
    swap = [(2 * chip + side, 2 * chip + 1 - side) for chip in range(chips) for side in (0, 1)]

    def fold(near, far):
        return jnp.where(near[0, flag_row, 0] > 0, near, near + far)

    def chip_shift(value, distance):
        step = direction * distance
        pairs = [
            (2 * chip + side, 2 * (chip + step) + side)
            for chip in range(chips)
            if 0 <= chip + step < chips
            for side in (0, 1)
        ]
        return lax.ppermute(value, "seq", pairs)

    low, high = (packed[:split], packed[split:])
    mine = jnp.where(core == 0, low, high)
    got = lax.ppermute(jnp.where(core == 0, high, low), "seq", swap)
    summary = jnp.where(core == lead, fold(mine, got), fold(got, mine))
    carry = chip_shift(summary, 1)
    chip_reach = min(chips - 1, -(-reach // 2))
    covered = 1
    if chip_reach > 1:
        carry = fold(carry, chip_shift(summary, 2))
        covered = 2
    while covered < chip_reach:
        carry = fold(carry, chip_shift(carry, covered))
        covered *= 2
    back = lax.ppermute(jnp.where(core == lead, carry, fold(mine, carry)), "seq", swap)
    kept = jnp.where(core == lead, fold(got, carry), carry)
    return jnp.where(
        core == 0, jnp.concatenate([kept, back], axis=0), jnp.concatenate([back, kept], axis=0)
    )


def taylor_table(feat_width):
    row_index, col_index = np.triu_indices(feat_width)
    taylor_map = np.zeros((feat_width * feat_width, len(row_index)), np.float32)
    taylor_map[row_index * feat_width + col_index, np.arange(len(row_index))] = np.where(
        row_index == col_index, 1.0 / np.sqrt(2.0), 1.0
    )
    return jnp.asarray(taylor_map)


def expand_features(vectors, taylor_map):
    lead_shape = vectors.shape[:-1]
    feat_width = vectors.shape[-1]
    outer_prod = (vectors[..., :, None] * vectors[..., None, :]).reshape(
        lead_shape + (feat_width * feat_width,)
    )
    square = jnp.einsum(
        "thp,pc->thc", outer_prod, taylor_map.astype(vectors.dtype), precision=highest
    )
    return jnp.concatenate([jnp.ones(lead_shape + (1,), vectors.dtype), vectors, square], axis=-1)


def block_forward(query_raw, key_raw, value_all, doc_local, prev_id, state_in, norm_in, taylor_map):
    length = query_raw.shape[0]
    queries = (0.5 * query_raw).reshape(length, HEADS, FEAT)
    key_feats = (0.5 * key_raw).reshape(length, HEADS, FEAT)
    values = value_all.reshape(length, HEADS, HEAD_DIM)
    scores = jnp.einsum("thf,shf->hts", queries, key_feats, precision=highest)
    kernel = 1.0 + scores + 0.5 * scores * scores
    positions = jnp.arange(length)
    allowed = (positions[:, None] >= positions[None, :]) & (
        doc_local[:, None] == doc_local[None, :]
    )
    kernel = jnp.where(allowed[None], kernel, 0.0)
    numerator = jnp.einsum("hts,shd->thd", kernel, values, precision=highest)
    denominator = jnp.sum(kernel, axis=2).T
    carried = (doc_local == prev_id).astype(kernel.dtype)[:, None]
    phi_query = expand_features(queries, taylor_map)
    numerator = numerator + carried[:, :, None] * jnp.einsum(
        "thf,hfd->thd", phi_query, state_in, precision=highest
    )
    denominator = denominator + carried * jnp.sum(phi_query * norm_in[None], axis=-1)
    return (numerator / denominator[:, :, None]).reshape(length, HEADS * HEAD_DIM)


def block_summary(key_raw, value_all, doc_local, taylor_map):
    length = key_raw.shape[0]
    key_feats = (0.5 * key_raw).reshape(length, HEADS, FEAT)
    values = value_all.reshape(length, HEADS, HEAD_DIM)
    phi_key = expand_features(key_feats, taylor_map)
    tail_mask = (doc_local == doc_local[-1]).astype(phi_key.dtype)[:, None, None]
    weighted = phi_key * tail_mask
    state_sum = jnp.einsum("thf,thd->hfd", weighted, values, precision=highest)
    norm_sum = jnp.sum(weighted, axis=0)
    return (state_sum, norm_sum)


def on_device(tokens, query_weight, key_weight, value_weight, cotangent, doc_ids):
    inputs = tokens[0]
    doc_local = doc_ids[0]
    cotan_local = cotangent[0]
    taylor_map = taylor_table(FEAT)
    width_qk = HEADS * FEAT
    parts = (query_weight, key_weight, value_weight)
    projected = lax.optimization_barrier(
        jnp.concatenate(
            [jnp.dot(inputs, part, preferred_element_type=jnp.float32) for part in parts], axis=1
        )
    )

    def summary(proj_in):
        return block_summary(
            proj_in[:, width_qk : 2 * width_qk], proj_in[:, 2 * width_qk :], doc_local, taylor_map
        )

    (state_loc, norm_loc), summary_pull = jax.vjp(summary, projected)
    feats = state_loc.shape[1]
    count, length = (lax.axis_size("seq"), doc_local.shape[0])
    longest = count * length // 2
    reach = min(count - 1, -(-(longest - 1) // length))
    prev_id = shifted(doc_local[-1:] + 1, 1)[0] - 1
    boundary = (doc_local[-1] != prev_id).astype(jnp.float32)
    forward_sum = chip_scan(pack_heads(state_loc, norm_loc, boundary), feats + 2, 1, reach)
    state_in, norm_in = unpack_heads(forward_sum, feats)
    tokens_pack = lax.all_gather(inputs.astype(jnp.float32), "seq", axis=0, tiled=True)

    def attend(proj_in, state_sum, norm_sum):
        return block_forward(
            proj_in[:, :width_qk],
            proj_in[:, width_qk : 2 * width_qk],
            proj_in[:, 2 * width_qk :],
            doc_local,
            prev_id,
            state_sum,
            norm_sum,
            taylor_map,
        )

    output, attend_pull = jax.vjp(attend, projected, state_in, norm_in)
    grad_direct, grad_state_in, grad_norm_in = attend_pull(cotan_local.astype(jnp.float32))
    backward_sum = chip_scan(
        pack_heads(grad_state_in, grad_norm_in, boundary), feats + 2, -1, reach
    )
    grad_state_loc, grad_norm_loc = unpack_heads(backward_sum, feats)
    (grad_carried,) = summary_pull((grad_state_loc, grad_norm_loc))
    grad_projected = (grad_direct + grad_carried).astype(jnp.bfloat16)
    edges = np.cumsum([0] + [part.shape[1] for part in parts])
    grad_input = sum(
        lax.dot_general(
            grad_projected[:, start:stop],
            part,
            (((1,), (1,)), ((), ())),
            preferred_element_type=jnp.float32,
        )
        for part, start, stop in zip(parts, edges[:-1], edges[1:])
    ).astype(jnp.bfloat16)
    grad_wide = grad_projected.astype(jnp.float32)
    rows, count = (grad_wide.shape[0], lax.axis_size("seq"))
    block = grad_wide.shape[1] // count
    halves = []
    for lo, hi in ((0, block // 2), (block // 2, block)):
        part = grad_wide.reshape(rows, count, block)[:, :, lo:hi].reshape(rows, count * (hi - lo))
        grad_cols = lax.all_to_all(part, "seq", split_axis=1, concat_axis=0, tiled=True)
        pack_part = lax.dot_general(
            tokens_pack,
            grad_cols,
            (((0,), (0,)), ((), ())),
            precision=lax.Precision.HIGH,
            preferred_element_type=jnp.float32,
        )
        halves.append(lax.psum_scatter(pack_part, "dp", scatter_dimension=0, tiled=True))
    row_part = jnp.concatenate(halves, axis=1)
    row_part, grad_input = lax.optimization_barrier((row_part, grad_input))
    grad_proj = lax.all_to_all(row_part, "seq", split_axis=0, concat_axis=1, tiled=True)
    return (output.astype(jnp.bfloat16)[None], grad_input[None], grad_proj)


def solution(mesh):
    return jax.shard_map(
        on_device,
        mesh=mesh,
        in_specs=(P("dp", "seq", None), P(), P(), P(), P("dp", "seq", None), P("dp", "seq")),
        out_specs=(P("dp", "seq", None), P("dp", "seq", None), P(("dp", "seq"), None)),
        check_vma=False,
    )
```

```python
import jax
import jax.numpy as jnp
import numpy as np
from jax import lax
from jax.sharding import PartitionSpec as P

HEADS = 16
FEAT = 16
HEAD_DIM = 128


highest = lax.Precision.HIGHEST


def pack_heads(state, norm, extra):
    heads, feats, lanes = state.shape
    rows = -(-(feats + 3) // 8) * 8
    norm_rows = jnp.pad(norm, ((0, 0), (0, 2 * lanes - feats))).reshape(heads, 2, lanes)
    extra_rows = jnp.broadcast_to(extra, (heads, 1, lanes)).astype(state.dtype)
    filler = jnp.zeros((heads, rows - feats - 3, lanes), state.dtype)
    return jnp.concatenate([state, norm_rows, extra_rows, filler], axis=1)


def unpack_heads(packed, feats):
    heads, _, lanes = packed.shape
    state = packed[:, :feats, :]
    norm = packed[:, feats : feats + 2, :].reshape(heads, 2 * lanes)[:, :feats]
    return state, norm


def shifted(value, steps):
    count = lax.axis_size("seq")
    if steps > 0:
        pairs = [(source, source + steps) for source in range(count - steps)]
    else:
        pairs = [(source, source + steps) for source in range(-steps, count)]
    return lax.ppermute(value, "seq", pairs)


def segmented_scan(packed, flag_row, direction, reach):
    carry = shifted(packed, direction)
    covered = 1
    while covered < reach:
        earlier = shifted(carry, direction * covered)
        carry = jnp.where(carry[0, flag_row, 0] > 0, carry, carry + earlier)
        covered *= 2
    return carry


def chip_scan(packed, flag_row, direction, reach):
    count = lax.axis_size("seq")
    if count % 2 or packed.shape[0] % 2:
        return segmented_scan(packed, flag_row, direction, reach)
    chips, split = (count // 2, packed.shape[0] // 2)
    lead = 1 if direction > 0 else 0
    core = lax.axis_index("seq") % 2
    swap = [(2 * chip + side, 2 * chip + 1 - side) for chip in range(chips) for side in (0, 1)]

    def fold(near, far):
        return jnp.where(near[0, flag_row, 0] > 0, near, near + far)

    def chip_shift(value, distance):
        step = direction * distance
        pairs = [
            (2 * chip + side, 2 * (chip + step) + side)
            for chip in range(chips)
            if 0 <= chip + step < chips
            for side in (0, 1)
        ]
        return lax.ppermute(value, "seq", pairs)

    low, high = (packed[:split], packed[split:])
    mine = jnp.where(core == 0, low, high)
    got = lax.ppermute(jnp.where(core == 0, high, low), "seq", swap)
    summary = jnp.where(core == lead, fold(mine, got), fold(got, mine))
    carry = chip_shift(summary, 1)
    chip_reach = min(chips - 1, -(-reach // 2))
    covered = 1
    if chip_reach > 1:
        carry = fold(carry, chip_shift(summary, 2))
        covered = 2
    while covered < chip_reach:
        carry = fold(carry, chip_shift(carry, covered))
        covered *= 2
    back = lax.ppermute(jnp.where(core == lead, carry, fold(mine, carry)), "seq", swap)
    kept = jnp.where(core == lead, fold(got, carry), carry)
    return jnp.where(
        core == 0, jnp.concatenate([kept, back], axis=0), jnp.concatenate([back, kept], axis=0)
    )


def taylor_table(feat_width):
    row_index, col_index = np.triu_indices(feat_width)
    taylor_map = np.zeros((feat_width * feat_width, len(row_index)), np.float32)
    taylor_map[row_index * feat_width + col_index, np.arange(len(row_index))] = np.where(
        row_index == col_index, 1.0 / np.sqrt(2.0), 1.0
    )
    return jnp.asarray(taylor_map)


def expand_features(vectors, taylor_map):
    lead_shape = vectors.shape[:-1]
    feat_width = vectors.shape[-1]
    outer_prod = (vectors[..., :, None] * vectors[..., None, :]).reshape(
        lead_shape + (feat_width * feat_width,)
    )
    square = jnp.einsum(
        "thp,pc->thc", outer_prod, taylor_map.astype(vectors.dtype), precision=highest
    )
    return jnp.concatenate([jnp.ones(lead_shape + (1,), vectors.dtype), vectors, square], axis=-1)


def block_forward(query_raw, key_raw, value_all, doc_local, prev_id, state_in, norm_in, taylor_map):
    length = query_raw.shape[0]
    queries = (0.5 * query_raw).reshape(length, HEADS, FEAT)
    key_feats = (0.5 * key_raw).reshape(length, HEADS, FEAT)
    values = value_all.reshape(length, HEADS, HEAD_DIM)
    scores = jnp.einsum("thf,shf->hts", queries, key_feats, precision=highest)
    kernel = 1.0 + scores + 0.5 * scores * scores
    positions = jnp.arange(length)
    allowed = (positions[:, None] >= positions[None, :]) & (
        doc_local[:, None] == doc_local[None, :]
    )
    kernel = jnp.where(allowed[None], kernel, 0.0)
    numerator = jnp.einsum("hts,shd->thd", kernel, values, precision=highest)
    denominator = jnp.sum(kernel, axis=2).T
    carried = (doc_local == prev_id).astype(kernel.dtype)[:, None]
    phi_query = expand_features(queries, taylor_map)
    numerator = numerator + carried[:, :, None] * jnp.einsum(
        "thf,hfd->thd", phi_query, state_in, precision=highest
    )
    denominator = denominator + carried * jnp.sum(phi_query * norm_in[None], axis=-1)
    return (numerator / denominator[:, :, None]).reshape(length, HEADS * HEAD_DIM)


def block_summary(key_raw, value_all, doc_local, taylor_map):
    length = key_raw.shape[0]
    key_feats = (0.5 * key_raw).reshape(length, HEADS, FEAT)
    values = value_all.reshape(length, HEADS, HEAD_DIM)
    phi_key = expand_features(key_feats, taylor_map)
    tail_mask = (doc_local == doc_local[-1]).astype(phi_key.dtype)[:, None, None]
    weighted = phi_key * tail_mask
    state_sum = jnp.einsum("thf,thd->hfd", weighted, values, precision=highest)
    norm_sum = jnp.sum(weighted, axis=0)
    return (state_sum, norm_sum)


def on_device(tokens, query_weight, key_weight, value_weight, cotangent, doc_ids):
    inputs = tokens[0]
    doc_local = doc_ids[0]
    cotan_local = cotangent[0]
    taylor_map = taylor_table(FEAT)
    width_qk = HEADS * FEAT
    parts = (query_weight, key_weight, value_weight)
    projected = lax.optimization_barrier(
        jnp.concatenate(
            [jnp.dot(inputs, part, preferred_element_type=jnp.float32) for part in parts], axis=1
        )
    )

    def summary(proj_in):
        return block_summary(
            proj_in[:, width_qk : 2 * width_qk], proj_in[:, 2 * width_qk :], doc_local, taylor_map
        )

    (state_loc, norm_loc), summary_pull = jax.vjp(summary, projected)
    feats = state_loc.shape[1]
    tokens_wide, state_loc, norm_loc = lax.optimization_barrier(
        (inputs.astype(jnp.float32), state_loc, norm_loc)
    )
    tokens_pack = lax.all_gather(tokens_wide, "seq", axis=0, tiled=True)
    count, length = (lax.axis_size("seq"), doc_local.shape[0])
    longest = count * length // 2
    reach = min(count - 1, -(-(longest - 1) // length))
    prev_id = shifted(doc_local[-1:] + 1, 1)[0] - 1
    boundary = (doc_local[-1] != prev_id).astype(jnp.float32)
    forward_sum = chip_scan(pack_heads(state_loc, norm_loc, boundary), feats + 2, 1, reach)
    state_in, norm_in = unpack_heads(forward_sum, feats)

    def attend(proj_in, state_sum, norm_sum):
        return block_forward(
            proj_in[:, :width_qk],
            proj_in[:, width_qk : 2 * width_qk],
            proj_in[:, 2 * width_qk :],
            doc_local,
            prev_id,
            state_sum,
            norm_sum,
            taylor_map,
        )

    output, attend_pull = jax.vjp(attend, projected, state_in, norm_in)
    grad_direct, grad_state_in, grad_norm_in = attend_pull(cotan_local.astype(jnp.float32))
    backward_sum = chip_scan(
        pack_heads(grad_state_in, grad_norm_in, boundary), feats + 2, -1, reach
    )
    grad_state_loc, grad_norm_loc = unpack_heads(backward_sum, feats)
    (grad_carried,) = summary_pull((grad_state_loc, grad_norm_loc))
    grad_projected = (grad_direct + grad_carried).astype(jnp.bfloat16)
    edges = np.cumsum([0] + [part.shape[1] for part in parts])
    grad_input = sum(
        lax.dot_general(
            grad_projected[:, start:stop],
            part,
            (((1,), (1,)), ((), ())),
            preferred_element_type=jnp.float32,
        )
        for part, start, stop in zip(parts, edges[:-1], edges[1:])
    ).astype(jnp.bfloat16)
    grad_cols = lax.all_to_all(
        grad_projected.astype(jnp.float32), "seq", split_axis=1, concat_axis=0, tiled=True
    )
    pack_part = lax.dot_general(
        tokens_pack,
        grad_cols,
        (((0,), (0,)), ((), ())),
        precision=lax.Precision.HIGH,
        preferred_element_type=jnp.float32,
    )
    row_part = lax.psum_scatter(pack_part, "dp", scatter_dimension=0, tiled=True)
    row_part, grad_input = lax.optimization_barrier((row_part, grad_input))
    grad_proj = lax.all_to_all(row_part, "seq", split_axis=0, concat_axis=1, tiled=True)
    return (output.astype(jnp.bfloat16)[None], grad_input[None], grad_proj)


def solution(mesh):
    return jax.shard_map(
        on_device,
        mesh=mesh,
        in_specs=(P("dp", "seq", None), P(), P(), P(), P("dp", "seq", None), P("dp", "seq")),
        out_specs=(P("dp", "seq", None), P("dp", "seq", None), P(("dp", "seq"), None)),
        check_vma=False,
    )
```

```python
import jax
import jax.numpy as jnp
import numpy as np
from jax import lax
from jax.sharding import PartitionSpec as P

HEADS = 16
FEAT = 16
HEAD_DIM = 128


highest = lax.Precision.HIGHEST


def pack_heads(state, norm, extra):
    heads, feats, lanes = state.shape
    rows = -(-(feats + 3) // 8) * 8
    norm_rows = jnp.pad(norm, ((0, 0), (0, 2 * lanes - feats))).reshape(heads, 2, lanes)
    extra_rows = jnp.broadcast_to(extra, (heads, 1, lanes)).astype(state.dtype)
    filler = jnp.zeros((heads, rows - feats - 3, lanes), state.dtype)
    return jnp.concatenate([state, norm_rows, extra_rows, filler], axis=1)


def unpack_heads(packed, feats):
    heads, _, lanes = packed.shape
    state = packed[:, :feats, :]
    norm = packed[:, feats : feats + 2, :].reshape(heads, 2 * lanes)[:, :feats]
    return state, norm


def shifted(value, steps):
    count = lax.axis_size("seq")
    if steps > 0:
        pairs = [(source, source + steps) for source in range(count - steps)]
    else:
        pairs = [(source, source + steps) for source in range(-steps, count)]
    return lax.ppermute(value, "seq", pairs)


def segmented_scan(packed, flag_row, direction, reach):
    carry = shifted(packed, direction)
    covered = 1
    while covered < reach:
        earlier = shifted(carry, direction * covered)
        carry = jnp.where(carry[0, flag_row, 0] > 0, carry, carry + earlier)
        covered *= 2
    return carry


def chip_scan(packed, flag_row, direction, reach, rider=None):
    count = lax.axis_size("seq")
    if count % 2 or packed.shape[0] % 2:
        return segmented_scan(packed, flag_row, direction, reach), rider
    chips, split = (count // 2, packed.shape[0] // 2)
    lead = 1 if direction > 0 else 0
    core = lax.axis_index("seq") % 2
    swap = [(2 * chip + side, 2 * chip + 1 - side) for chip in range(chips) for side in (0, 1)]

    def fold(near, far):
        return jnp.where(near[0, flag_row, 0] > 0, near, near + far)

    def chip_shift(value, distance):
        step = direction * distance
        pairs = [
            (2 * chip + side, 2 * (chip + step) + side)
            for chip in range(chips)
            if 0 <= chip + step < chips
            for side in (0, 1)
        ]
        return lax.ppermute(value, "seq", pairs)

    low, high = (packed[:split], packed[split:])
    mine = jnp.where(core == 0, low, high)
    got = lax.ppermute(jnp.where(core == 0, high, low), "seq", swap)
    if rider is not None:
        rider, got = lax.optimization_barrier((rider, got))
    summary = jnp.where(core == lead, fold(mine, got), fold(got, mine))
    carry = chip_shift(summary, 1)
    chip_reach = min(chips - 1, -(-reach // 2))
    covered = 1
    if chip_reach > 1:
        carry = fold(carry, chip_shift(summary, 2))
        covered = 2
    while covered < chip_reach:
        carry = fold(carry, chip_shift(carry, covered))
        covered *= 2
    back = lax.ppermute(jnp.where(core == lead, carry, fold(mine, carry)), "seq", swap)
    kept = jnp.where(core == lead, fold(got, carry), carry)
    return (
        jnp.where(
            core == 0,
            jnp.concatenate([kept, back], axis=0),
            jnp.concatenate([back, kept], axis=0),
        ),
        rider,
    )


def taylor_table(feat_width):
    row_index, col_index = np.triu_indices(feat_width)
    taylor_map = np.zeros((feat_width * feat_width, len(row_index)), np.float32)
    taylor_map[row_index * feat_width + col_index, np.arange(len(row_index))] = np.where(
        row_index == col_index, 1.0 / np.sqrt(2.0), 1.0
    )
    return jnp.asarray(taylor_map)


def expand_features(vectors, taylor_map):
    lead_shape = vectors.shape[:-1]
    feat_width = vectors.shape[-1]
    outer_prod = (vectors[..., :, None] * vectors[..., None, :]).reshape(
        lead_shape + (feat_width * feat_width,)
    )
    square = jnp.einsum(
        "thp,pc->thc", outer_prod, taylor_map.astype(vectors.dtype), precision=highest
    )
    return jnp.concatenate([jnp.ones(lead_shape + (1,), vectors.dtype), vectors, square], axis=-1)


def block_forward(query_raw, key_raw, value_all, doc_local, prev_id, state_in, norm_in, taylor_map):
    length = query_raw.shape[0]
    queries = (0.5 * query_raw).reshape(length, HEADS, FEAT)
    key_feats = (0.5 * key_raw).reshape(length, HEADS, FEAT)
    values = value_all.reshape(length, HEADS, HEAD_DIM)
    scores = jnp.einsum("thf,shf->hts", queries, key_feats, precision=highest)
    kernel = 1.0 + scores + 0.5 * scores * scores
    positions = jnp.arange(length)
    allowed = (positions[:, None] >= positions[None, :]) & (
        doc_local[:, None] == doc_local[None, :]
    )
    kernel = jnp.where(allowed[None], kernel, 0.0)
    numerator = jnp.einsum("hts,shd->thd", kernel, values, precision=highest)
    denominator = jnp.sum(kernel, axis=2).T
    carried = (doc_local == prev_id).astype(kernel.dtype)[:, None]
    phi_query = expand_features(queries, taylor_map)
    numerator = numerator + carried[:, :, None] * jnp.einsum(
        "thf,hfd->thd", phi_query, state_in, precision=highest
    )
    denominator = denominator + carried * jnp.sum(phi_query * norm_in[None], axis=-1)
    return (numerator / denominator[:, :, None]).reshape(length, HEADS * HEAD_DIM)


def block_summary(key_raw, value_all, doc_local, taylor_map):
    length = key_raw.shape[0]
    key_feats = (0.5 * key_raw).reshape(length, HEADS, FEAT)
    values = value_all.reshape(length, HEADS, HEAD_DIM)
    phi_key = expand_features(key_feats, taylor_map)
    tail_mask = (doc_local == doc_local[-1]).astype(phi_key.dtype)[:, None, None]
    weighted = phi_key * tail_mask
    state_sum = jnp.einsum("thf,thd->hfd", weighted, values, precision=highest)
    norm_sum = jnp.sum(weighted, axis=0)
    return (state_sum, norm_sum)


def on_device(tokens, query_weight, key_weight, value_weight, cotangent, doc_ids):
    inputs = tokens[0]
    doc_local = doc_ids[0]
    cotan_local = cotangent[0]
    taylor_map = taylor_table(FEAT)
    width_qk = HEADS * FEAT
    parts = (query_weight, key_weight, value_weight)
    projected = lax.optimization_barrier(
        jnp.concatenate(
            [jnp.dot(inputs, part, preferred_element_type=jnp.float32) for part in parts], axis=1
        )
    )

    def summary(proj_in):
        return block_summary(
            proj_in[:, width_qk : 2 * width_qk], proj_in[:, 2 * width_qk :], doc_local, taylor_map
        )

    (state_loc, norm_loc), summary_pull = jax.vjp(summary, projected)
    feats = state_loc.shape[1]
    count, length = (lax.axis_size("seq"), doc_local.shape[0])
    longest = count * length // 2
    reach = min(count - 1, -(-(longest - 1) // length))
    prev_id = shifted(doc_local[-1:] + 1, 1)[0] - 1
    boundary = (doc_local[-1] != prev_id).astype(jnp.float32)
    forward_sum, tokens_wide = chip_scan(
        pack_heads(state_loc, norm_loc, boundary), feats + 2, 1, reach, inputs.astype(jnp.float32)
    )
    tokens_pack = lax.all_gather(tokens_wide, "seq", axis=0, tiled=True)
    state_in, norm_in = unpack_heads(forward_sum, feats)

    def attend(proj_in, state_sum, norm_sum):
        return block_forward(
            proj_in[:, :width_qk],
            proj_in[:, width_qk : 2 * width_qk],
            proj_in[:, 2 * width_qk :],
            doc_local,
            prev_id,
            state_sum,
            norm_sum,
            taylor_map,
        )

    output, attend_pull = jax.vjp(attend, projected, state_in, norm_in)
    grad_direct, grad_state_in, grad_norm_in = attend_pull(cotan_local.astype(jnp.float32))
    backward_sum, _ = chip_scan(
        pack_heads(grad_state_in, grad_norm_in, boundary), feats + 2, -1, reach
    )
    grad_state_loc, grad_norm_loc = unpack_heads(backward_sum, feats)
    (grad_carried,) = summary_pull((grad_state_loc, grad_norm_loc))
    grad_projected = (grad_direct + grad_carried).astype(jnp.bfloat16)
    edges = np.cumsum([0] + [part.shape[1] for part in parts])
    grad_input = sum(
        lax.dot_general(
            grad_projected[:, start:stop],
            part,
            (((1,), (1,)), ((), ())),
            preferred_element_type=jnp.float32,
        )
        for part, start, stop in zip(parts, edges[:-1], edges[1:])
    ).astype(jnp.bfloat16)
    grad_cols = lax.all_to_all(
        grad_projected.astype(jnp.float32), "seq", split_axis=1, concat_axis=0, tiled=True
    )
    pack_part = lax.dot_general(
        tokens_pack,
        grad_cols,
        (((0,), (0,)), ((), ())),
        precision=lax.Precision.HIGH,
        preferred_element_type=jnp.float32,
    )
    row_part = lax.psum_scatter(pack_part, "dp", scatter_dimension=0, tiled=True)
    row_part, grad_input = lax.optimization_barrier((row_part, grad_input))
    grad_proj = lax.all_to_all(row_part, "seq", split_axis=0, concat_axis=1, tiled=True)
    return (output.astype(jnp.bfloat16)[None], grad_input[None], grad_proj)


def solution(mesh):
    return jax.shard_map(
        on_device,
        mesh=mesh,
        in_specs=(P("dp", "seq", None), P(), P(), P(), P("dp", "seq", None), P("dp", "seq")),
        out_specs=(P("dp", "seq", None), P("dp", "seq", None), P(("dp", "seq"), None)),
        check_vma=False,
    )
```

```python
import jax
import jax.numpy as jnp
import numpy as np
from jax import lax
from jax.sharding import PartitionSpec as P

HEADS = 16
FEAT = 16
HEAD_DIM = 128


highest = lax.Precision.HIGHEST


def pack_heads(state, norm, extra):
    heads, feats, lanes = state.shape
    rows = -(-(feats + 3) // 8) * 8
    norm_rows = jnp.pad(norm, ((0, 0), (0, 2 * lanes - feats))).reshape(heads, 2, lanes)
    extra_rows = jnp.broadcast_to(extra, (heads, 1, lanes)).astype(state.dtype)
    filler = jnp.zeros((heads, rows - feats - 3, lanes), state.dtype)
    return jnp.concatenate([state, norm_rows, extra_rows, filler], axis=1)


def unpack_heads(packed, feats):
    heads, _, lanes = packed.shape
    state = packed[:, :feats, :]
    norm = packed[:, feats : feats + 2, :].reshape(heads, 2 * lanes)[:, :feats]
    return state, norm


def shifted(value, steps):
    count = lax.axis_size("seq")
    if steps > 0:
        pairs = [(source, source + steps) for source in range(count - steps)]
    else:
        pairs = [(source, source + steps) for source in range(-steps, count)]
    return lax.ppermute(value, "seq", pairs)


def segmented_scan(packed, flag_row, direction, reach):
    carry = shifted(packed, direction)
    covered = 1
    while covered < reach:
        earlier = shifted(carry, direction * covered)
        carry = jnp.where(carry[0, flag_row, 0] > 0, carry, carry + earlier)
        covered *= 2
    return carry


def chip_scan(packed, flag_row, direction, reach):
    count = lax.axis_size("seq")
    if count % 2 or packed.shape[0] % 2:
        return segmented_scan(packed, flag_row, direction, reach)
    chips, split = (count // 2, packed.shape[0] // 2)
    lead = 1 if direction > 0 else 0
    core = lax.axis_index("seq") % 2
    swap = [(2 * chip + side, 2 * chip + 1 - side) for chip in range(chips) for side in (0, 1)]

    def fold(near, far):
        return jnp.where(near[0, flag_row, 0] > 0, near, near + far)

    def chip_shift(value, distance):
        step = direction * distance
        pairs = [
            (2 * chip + side, 2 * (chip + step) + side)
            for chip in range(chips)
            if 0 <= chip + step < chips
            for side in (0, 1)
        ]
        return lax.ppermute(value, "seq", pairs)

    low, high = (packed[:split], packed[split:])
    mine = jnp.where(core == 0, low, high)
    got = lax.ppermute(jnp.where(core == 0, high, low), "seq", swap)
    summary = jnp.where(core == lead, fold(mine, got), fold(got, mine))
    carry = chip_shift(summary, 1)
    chip_reach = min(chips - 1, -(-reach // 2))
    covered = 1
    if chip_reach > 1:
        carry = fold(carry, chip_shift(summary, 2))
        covered = 2
    while covered < chip_reach:
        carry = fold(carry, chip_shift(carry, covered))
        covered *= 2
    back = lax.ppermute(jnp.where(core == lead, carry, fold(mine, carry)), "seq", swap)
    kept = jnp.where(core == lead, fold(got, carry), carry)
    return jnp.where(
        core == 0, jnp.concatenate([kept, back], axis=0), jnp.concatenate([back, kept], axis=0)
    )


def taylor_table(feat_width):
    row_index, col_index = np.triu_indices(feat_width)
    taylor_map = np.zeros((feat_width * feat_width, len(row_index)), np.float32)
    taylor_map[row_index * feat_width + col_index, np.arange(len(row_index))] = np.where(
        row_index == col_index, 1.0 / np.sqrt(2.0), 1.0
    )
    return jnp.asarray(taylor_map)


def expand_features(vectors, taylor_map):
    lead_shape = vectors.shape[:-1]
    feat_width = vectors.shape[-1]
    outer_prod = (vectors[..., :, None] * vectors[..., None, :]).reshape(
        lead_shape + (feat_width * feat_width,)
    )
    square = jnp.einsum(
        "thp,pc->thc", outer_prod, taylor_map.astype(vectors.dtype), precision=highest
    )
    return jnp.concatenate([jnp.ones(lead_shape + (1,), vectors.dtype), vectors, square], axis=-1)


def block_forward(query_raw, key_raw, value_all, doc_local, prev_id, state_in, norm_in, taylor_map):
    length = query_raw.shape[0]
    queries = (0.5 * query_raw).reshape(length, HEADS, FEAT)
    key_feats = (0.5 * key_raw).reshape(length, HEADS, FEAT)
    values = value_all.reshape(length, HEADS, HEAD_DIM)
    scores = jnp.einsum("thf,shf->hts", queries, key_feats, precision=highest)
    kernel = 1.0 + scores + 0.5 * scores * scores
    positions = jnp.arange(length)
    allowed = (positions[:, None] >= positions[None, :]) & (
        doc_local[:, None] == doc_local[None, :]
    )
    kernel = jnp.where(allowed[None], kernel, 0.0)
    numerator = jnp.einsum("hts,shd->thd", kernel, values, precision=highest)
    denominator = jnp.sum(kernel, axis=2).T
    carried = (doc_local == prev_id).astype(kernel.dtype)[:, None]
    phi_query = expand_features(queries, taylor_map)
    numerator = numerator + carried[:, :, None] * jnp.einsum(
        "thf,hfd->thd", phi_query, state_in, precision=highest
    )
    denominator = denominator + carried * jnp.sum(phi_query * norm_in[None], axis=-1)
    return (numerator / denominator[:, :, None]).reshape(length, HEADS * HEAD_DIM)


def block_summary(key_raw, value_all, doc_local, taylor_map):
    length = key_raw.shape[0]
    key_feats = (0.5 * key_raw).reshape(length, HEADS, FEAT)
    values = value_all.reshape(length, HEADS, HEAD_DIM)
    phi_key = expand_features(key_feats, taylor_map)
    tail_mask = (doc_local == doc_local[-1]).astype(phi_key.dtype)[:, None, None]
    weighted = phi_key * tail_mask
    state_sum = jnp.einsum("thf,thd->hfd", weighted, values, precision=highest)
    norm_sum = jnp.sum(weighted, axis=0)
    return (state_sum, norm_sum)


def on_device(tokens, query_weight, key_weight, value_weight, cotangent, doc_ids):
    inputs = tokens[0]
    doc_local = doc_ids[0]
    cotan_local = cotangent[0]
    taylor_map = taylor_table(FEAT)
    width_qk = HEADS * FEAT
    parts = (query_weight, key_weight, value_weight)
    projected = lax.optimization_barrier(
        jnp.concatenate(
            [jnp.dot(inputs, part, preferred_element_type=jnp.float32) for part in parts], axis=1
        )
    )

    def summary(proj_in):
        return block_summary(
            proj_in[:, width_qk : 2 * width_qk], proj_in[:, 2 * width_qk :], doc_local, taylor_map
        )

    (state_loc, norm_loc), summary_pull = jax.vjp(summary, projected)
    feats = state_loc.shape[1]
    tokens_wide, state_loc, norm_loc = lax.optimization_barrier(
        (inputs.astype(jnp.float32), state_loc, norm_loc)
    )
    tokens_pack = lax.all_gather(tokens_wide, "seq", axis=0, tiled=True)
    count, length = (lax.axis_size("seq"), doc_local.shape[0])
    longest = count * length // 2
    reach = min(count - 1, -(-(longest - 1) // length))
    last_id, state_loc = lax.optimization_barrier((doc_local[-1:] + 1, state_loc))
    prev_id = shifted(last_id, 1)[0] - 1
    boundary = (doc_local[-1] != prev_id).astype(jnp.float32)
    forward_sum = chip_scan(pack_heads(state_loc, norm_loc, boundary), feats + 2, 1, reach)
    state_in, norm_in = unpack_heads(forward_sum, feats)

    def attend(proj_in, state_sum, norm_sum):
        return block_forward(
            proj_in[:, :width_qk],
            proj_in[:, width_qk : 2 * width_qk],
            proj_in[:, 2 * width_qk :],
            doc_local,
            prev_id,
            state_sum,
            norm_sum,
            taylor_map,
        )

    output, attend_pull = jax.vjp(attend, projected, state_in, norm_in)
    grad_direct, grad_state_in, grad_norm_in = attend_pull(cotan_local.astype(jnp.float32))
    backward_sum = chip_scan(
        pack_heads(grad_state_in, grad_norm_in, boundary), feats + 2, -1, reach
    )
    grad_state_loc, grad_norm_loc = unpack_heads(backward_sum, feats)
    (grad_carried,) = summary_pull((grad_state_loc, grad_norm_loc))
    grad_projected = (grad_direct + grad_carried).astype(jnp.bfloat16)
    edges = np.cumsum([0] + [part.shape[1] for part in parts])
    grad_input = sum(
        lax.dot_general(
            grad_projected[:, start:stop],
            part,
            (((1,), (1,)), ((), ())),
            preferred_element_type=jnp.float32,
        )
        for part, start, stop in zip(parts, edges[:-1], edges[1:])
    ).astype(jnp.bfloat16)
    grad_cols = lax.all_to_all(
        grad_projected.astype(jnp.float32), "seq", split_axis=1, concat_axis=0, tiled=True
    )
    pack_part = lax.dot_general(
        tokens_pack,
        grad_cols,
        (((0,), (0,)), ((), ())),
        precision=lax.Precision.HIGH,
        preferred_element_type=jnp.float32,
    )
    row_part = lax.psum_scatter(pack_part, "dp", scatter_dimension=0, tiled=True)
    row_part, grad_input = lax.optimization_barrier((row_part, grad_input))
    grad_proj = lax.all_to_all(row_part, "seq", split_axis=0, concat_axis=1, tiled=True)
    return (output.astype(jnp.bfloat16)[None], grad_input[None], grad_proj)


def solution(mesh):
    return jax.shard_map(
        on_device,
        mesh=mesh,
        in_specs=(P("dp", "seq", None), P(), P(), P(), P("dp", "seq", None), P("dp", "seq")),
        out_specs=(P("dp", "seq", None), P("dp", "seq", None), P(("dp", "seq"), None)),
        check_vma=False,
    )
```

```python
import jax
import jax.numpy as jnp
import numpy as np
from jax import lax
from jax.sharding import PartitionSpec as P

HEADS = 16
FEAT = 16
HEAD_DIM = 128


highest = lax.Precision.HIGHEST


def pack_heads(state, norm, extra):
    heads, feats, lanes = state.shape
    rows = -(-(feats + 3) // 8) * 8
    norm_rows = jnp.pad(norm, ((0, 0), (0, 2 * lanes - feats))).reshape(heads, 2, lanes)
    extra_rows = jnp.broadcast_to(extra, (heads, 1, lanes)).astype(state.dtype)
    filler = jnp.zeros((heads, rows - feats - 3, lanes), state.dtype)
    return jnp.concatenate([state, norm_rows, extra_rows, filler], axis=1)


def unpack_heads(packed, feats):
    heads, _, lanes = packed.shape
    state = packed[:, :feats, :]
    norm = packed[:, feats : feats + 2, :].reshape(heads, 2 * lanes)[:, :feats]
    return state, norm


def shifted(value, steps):
    count = lax.axis_size("seq")
    if steps > 0:
        pairs = [(source, source + steps) for source in range(count - steps)]
    else:
        pairs = [(source, source + steps) for source in range(-steps, count)]
    return lax.ppermute(value, "seq", pairs)


def segmented_scan(packed, flag_row, direction, reach):
    carry = shifted(packed, direction)
    covered = 1
    while covered < reach:
        earlier = shifted(carry, direction * covered)
        carry = jnp.where(carry[0, flag_row, 0] > 0, carry, carry + earlier)
        covered *= 2
    return carry


def chip_scan(packed, flag_row, direction, reach):
    count = lax.axis_size("seq")
    if count % 2 or packed.shape[0] % 2:
        return segmented_scan(packed, flag_row, direction, reach)
    chips, split = (count // 2, packed.shape[0] // 2)
    lead = 1 if direction > 0 else 0
    core = lax.axis_index("seq") % 2
    swap = [(2 * chip + side, 2 * chip + 1 - side) for chip in range(chips) for side in (0, 1)]

    def fold(near, far):
        return jnp.where(near[0, flag_row, 0] > 0, near, near + far)

    def chip_shift(value, distance):
        step = direction * distance
        pairs = [
            (2 * chip + side, 2 * (chip + step) + side)
            for chip in range(chips)
            if 0 <= chip + step < chips
            for side in (0, 1)
        ]
        return lax.ppermute(value, "seq", pairs)

    low, high = (packed[:split], packed[split:])
    mine = jnp.where(core == 0, low, high)
    got = lax.ppermute(jnp.where(core == 0, high, low), "seq", swap)
    summary = jnp.where(core == lead, fold(mine, got), fold(got, mine))
    carry = chip_shift(summary, 1)
    chip_reach = min(chips - 1, -(-reach // 2))
    covered = 1
    if chip_reach > 1:
        carry = fold(carry, chip_shift(summary, 2))
        covered = 2
    while covered < chip_reach:
        carry = fold(carry, chip_shift(carry, covered))
        covered *= 2
    back = lax.ppermute(jnp.where(core == lead, carry, fold(mine, carry)), "seq", swap)
    kept = jnp.where(core == lead, fold(got, carry), carry)
    return jnp.where(
        core == 0, jnp.concatenate([kept, back], axis=0), jnp.concatenate([back, kept], axis=0)
    )


def taylor_table(feat_width):
    row_index, col_index = np.triu_indices(feat_width)
    taylor_map = np.zeros((feat_width * feat_width, len(row_index)), np.float32)
    taylor_map[row_index * feat_width + col_index, np.arange(len(row_index))] = np.where(
        row_index == col_index, 1.0 / np.sqrt(2.0), 1.0
    )
    return jnp.asarray(taylor_map)


def expand_features(vectors, taylor_map):
    lead_shape = vectors.shape[:-1]
    feat_width = vectors.shape[-1]
    outer_prod = (vectors[..., :, None] * vectors[..., None, :]).reshape(
        lead_shape + (feat_width * feat_width,)
    )
    square = jnp.einsum(
        "thp,pc->thc", outer_prod, taylor_map.astype(vectors.dtype), precision=highest
    )
    return jnp.concatenate([jnp.ones(lead_shape + (1,), vectors.dtype), vectors, square], axis=-1)


def block_forward(query_raw, key_raw, value_all, doc_local, prev_id, state_in, norm_in, taylor_map):
    length = query_raw.shape[0]
    queries = (0.5 * query_raw).reshape(length, HEADS, FEAT)
    key_feats = (0.5 * key_raw).reshape(length, HEADS, FEAT)
    values = value_all.reshape(length, HEADS, HEAD_DIM)
    scores = jnp.einsum("thf,shf->hts", queries, key_feats, precision=highest)
    kernel = 1.0 + scores + 0.5 * scores * scores
    positions = jnp.arange(length)
    allowed = (positions[:, None] >= positions[None, :]) & (
        doc_local[:, None] == doc_local[None, :]
    )
    kernel = jnp.where(allowed[None], kernel, 0.0)
    numerator = jnp.einsum("hts,shd->thd", kernel, values, precision=highest)
    denominator = jnp.sum(kernel, axis=2).T
    carried = (doc_local == prev_id).astype(kernel.dtype)[:, None]
    phi_query = expand_features(queries, taylor_map)
    numerator = numerator + carried[:, :, None] * jnp.einsum(
        "thf,hfd->thd", phi_query, state_in, precision=highest
    )
    denominator = denominator + carried * jnp.sum(phi_query * norm_in[None], axis=-1)
    return (numerator / denominator[:, :, None]).reshape(length, HEADS * HEAD_DIM)


def block_summary(key_raw, value_all, doc_local, taylor_map):
    length = key_raw.shape[0]
    key_feats = (0.5 * key_raw).reshape(length, HEADS, FEAT)
    values = value_all.reshape(length, HEADS, HEAD_DIM)
    phi_key = expand_features(key_feats, taylor_map)
    tail_mask = (doc_local == doc_local[-1]).astype(phi_key.dtype)[:, None, None]
    weighted = phi_key * tail_mask
    state_sum = jnp.einsum("thf,thd->hfd", weighted, values, precision=highest)
    norm_sum = jnp.sum(weighted, axis=0)
    return (state_sum, norm_sum)


def on_device(tokens, query_weight, key_weight, value_weight, cotangent, doc_ids):
    inputs = tokens[0]
    doc_local = doc_ids[0]
    cotan_local = cotangent[0]
    taylor_map = taylor_table(FEAT)
    width_qk = HEADS * FEAT
    parts = (query_weight, key_weight, value_weight)
    projected = lax.optimization_barrier(
        jnp.concatenate(
            [jnp.dot(inputs, part, preferred_element_type=jnp.float32) for part in parts], axis=1
        )
    )

    def summary(proj_in):
        return block_summary(
            proj_in[:, width_qk : 2 * width_qk], proj_in[:, 2 * width_qk :], doc_local, taylor_map
        )

    (state_loc, norm_loc), summary_pull = jax.vjp(summary, projected)
    feats = state_loc.shape[1]
    tokens_wide, state_loc, norm_loc = lax.optimization_barrier(
        (inputs.astype(jnp.float32), state_loc, norm_loc)
    )
    tokens_pack = lax.all_gather(tokens_wide, "seq", axis=0, tiled=True)
    count, length = (lax.axis_size("seq"), doc_local.shape[0])
    longest = count * length // 2
    reach = min(count - 1, -(-(longest - 1) // length))
    prev_id = shifted(doc_local[-1:] + 1, 1)[0] - 1
    boundary = (doc_local[-1] != prev_id).astype(jnp.float32)
    forward_sum = chip_scan(pack_heads(state_loc, norm_loc, boundary), feats + 2, 1, reach)
    state_in, norm_in = unpack_heads(forward_sum, feats)

    def attend(proj_in, state_sum, norm_sum):
        return block_forward(
            proj_in[:, :width_qk],
            proj_in[:, width_qk : 2 * width_qk],
            proj_in[:, 2 * width_qk :],
            doc_local,
            prev_id,
            state_sum,
            norm_sum,
            taylor_map,
        )

    output, attend_pull = jax.vjp(attend, projected, state_in, norm_in)
    grad_direct, grad_state_in, grad_norm_in = attend_pull(cotan_local.astype(jnp.float32))
    backward_sum = chip_scan(
        pack_heads(grad_state_in, grad_norm_in, boundary), feats + 2, -1, reach
    )
    grad_state_loc, grad_norm_loc = unpack_heads(backward_sum, feats)
    (grad_carried,) = summary_pull((grad_state_loc, grad_norm_loc))
    grad_projected = (grad_direct + grad_carried).astype(jnp.bfloat16)
    edges = np.cumsum([0] + [part.shape[1] for part in parts])
    grad_input = sum(
        lax.dot_general(
            grad_projected[:, start:stop],
            part,
            (((1,), (1,)), ((), ())),
            preferred_element_type=jnp.float32,
        )
        for part, start, stop in zip(parts, edges[:-1], edges[1:])
    ).astype(jnp.bfloat16)
    grad_cols = lax.all_to_all(
        grad_projected.astype(jnp.float32), "seq", split_axis=1, concat_axis=0, tiled=True
    )
    pack_part = lax.dot_general(
        grad_cols,
        tokens_pack,
        (((0,), (0,)), ((), ())),
        precision=lax.Precision.HIGH,
        preferred_element_type=jnp.float32,
    )
    row_part = lax.psum_scatter(pack_part, "dp", scatter_dimension=1, tiled=True)
    row_part, grad_input = lax.optimization_barrier((row_part, grad_input))
    grad_proj = lax.all_to_all(row_part, "seq", split_axis=1, concat_axis=0, tiled=True).T
    return (output.astype(jnp.bfloat16)[None], grad_input[None], grad_proj)


def solution(mesh):
    return jax.shard_map(
        on_device,
        mesh=mesh,
        in_specs=(P("dp", "seq", None), P(), P(), P(), P("dp", "seq", None), P("dp", "seq")),
        out_specs=(P("dp", "seq", None), P("dp", "seq", None), P(("dp", "seq"), None)),
        check_vma=False,
    )
```
